32 devices in a mesh: slab: 8 (over y, x, core), view: 4 (over z).
Axes of the slice: x: 2, y: 2, z: 4, core: 2. Of those that a mesh axis runs over, the one named last changes fastest.
Arguments:
- estimate: float32 [4, 1024, 1024], P(None, 'slab'), may hold values from 0.5 to 2
- views: float32 [4, 4, 1024, 1024], P('view', None, 'slab'), may hold values from 0.25 to 4
- psf: float32 [4, 1024, 1024], P('view', 'slab'), as said below
- pattern_mult: int32 [4, 8], P('view'), may hold values from 0 to 63
- pattern_shift: int32 [4, 8], P('view'), may hold values from 0 to 127
- interp: float32 [4, 8, 128], P('view'), may hold values from 0.05 to 0.45
Outputs:
- updated: float32 [4, 1024, 1024], P(None, 'slab')
The draws below stay inside these ranges and needn't reach their ends.
Inputs may be any that keep to these rules, and one draw needn't show every extreme that they name: `psf`: every entry is positive.
All inputs are finite; a program needn't handle non-finite values.
Results may differ from the reference program's by a relative error of at most 0.0001.
Values sent between devices are 32-bit elements; how exact they have to be, the bound alone decides.
No kernel may reach another device: no remote copies, remote signals or barrier semaphores. Data moves between devices by JAX's collectives and lax.ppermute only.
A program may use at most 128 MiB of HBM per device.

```python
import math
import jax
import jax.numpy as jnp
from jax import lax

NX = 1024
NZ = 1024
NY = 4
VIEWS = 4
NBLK = 8


def draw_psf(key, part):
    across = lax.iota(jnp.int32, NX)
    depths = lax.iota(jnp.int32, NZ)
    dist_x = jnp.minimum(across, NX - across).astype(jnp.float32)
    dist_z = jnp.minimum(depths, NZ - depths).astype(jnp.float32)
    core_x = (dist_x / (NX / 341.0))[:, None]
    core_z = (dist_z / (NZ / 128.0))[None, :]
    core = jnp.exp(-0.5 * core_x * core_x - 0.5 * core_z * core_z)
    broad_x = (dist_x / (NX / 8.0))[:, None]
    broad_z = (dist_z / (NZ / 512.0))[None, :]
    broad = 0.2 * jnp.exp(-0.5 * broad_x * broad_x - 0.5 * broad_z * broad_z)
    tail_x = (dist_x / (NX / 32.0))[:, None]
    tail_z = (dist_z / (NZ / 10.0))[None, :]
    tail = 0.002 / (1.0 + tail_x * tail_x + tail_z * tail_z)
    rough = jnp.exp(jax.random.uniform(key, (VIEWS, NX, NZ), jnp.float32, -0.7, 0.7))
    return rough * (core + broad + tail)[None]


def place_ends(entries, rng, smallest, largest):
    shape = entries.shape
    index_at = [jax.random.randint(jax.random.fold_in(rng, axis), (), 0, shape[axis]) for axis in range(len(shape))]
    entries = entries.at[tuple(index_at)].set(smallest)
    longest = shape.index(max(shape))
    index_at[longest] = (index_at[longest] + 1) % shape[longest]
    return entries.at[tuple(index_at)].set(largest)


def block_levels(own_key, shape, cuts, smallest, top_value):
    def one(dim, blocks):
        steps = jax.random.uniform(jax.random.fold_in(jax.random.fold_in(own_key, 6), dim), (blocks,), jnp.float32, smallest / len(cuts), top_value / len(cuts))
        return jnp.repeat(jnp.exp(steps), shape[dim] // blocks).reshape((-1,) + (1,) * (len(shape) - dim - 1))

    gain = one(*cuts[0])
    for cut in cuts[1:]:
        gain = gain * one(*cut)
    return gain


def setup_inputs(seed: int = 0) -> dict:
    key_of = jax.random.split(jax.random.key(seed), 7)
    estimate = jnp.clip(0.5 + 1.5 * jax.random.uniform(key_of[0], (NY, NX, NZ), jnp.float32) ** block_levels(key_of[0], (NY, NX, NZ), ((1, 8),), -0.2, 0.2), 0.5, 2.0)
    views = jnp.clip(jnp.exp(math.log(4.0) - 2.7725887 * jax.random.uniform(key_of[1], (VIEWS, NY, NX, NZ), jnp.float32) ** block_levels(key_of[1], (VIEWS, NY, NX, NZ), ((0, 4), (2, 8)), -0.2, 0.2)), 0.25, 4.0)
    psf = draw_psf(jax.random.fold_in(key_of[6], 71), 0)
    pattern_mult = place_ends(jax.random.randint(key_of[3], (VIEWS, NBLK), 0, 64), jax.random.fold_in(key_of[3], 1), 0, 63).astype(jnp.int32)
    pattern_shift = place_ends(jax.random.randint(key_of[4], (VIEWS, NBLK), 0, 128), jax.random.fold_in(key_of[4], 1), 0, 127).astype(jnp.int32)
    interp = jnp.clip(0.05 + 0.39999999 * jax.random.uniform(key_of[5], (VIEWS, NBLK, 128), jnp.float32) ** block_levels(key_of[5], (VIEWS, NBLK, 128), ((0, 4),), -0.2, 0.2), 0.05, 0.45)
    return dict(estimate=estimate, views=views, psf=psf, pattern_mult=pattern_mult, pattern_shift=pattern_shift, interp=interp)


highest = lax.Precision.HIGHEST


def block_matrix(multiplier, shifting, weights):
    positions = jnp.arange(128, dtype=jnp.int32)
    first_col = ((2 * multiplier[:, None] + 1) * positions[None, :] + shifting[:, None]) % 128
    second_col = (first_col + 1) % 128
    columns = positions[None, None, :]
    lower = (columns == first_col[:, :, None]).astype(jnp.float32)
    upper = (columns == second_col[:, :, None]).astype(jnp.float32)
    return (1.0 - weights)[:, :, None] * lower + weights[:, :, None] * upper


def reference(estimate, views, psf, pattern_mult, pattern_shift, interp):
    log_summed = jnp.zeros(estimate.shape, jnp.float32)
    for view_index in range(VIEWS):
        blocks = block_matrix(pattern_mult[view_index], pattern_shift[view_index], interp[view_index])
        shaped = estimate.reshape(NY, NX, NBLK, 128)
        sampled = jnp.einsum("bij,yxbj->yxbi", blocks, shaped, precision=highest).reshape(NY, NX, NZ)
        transfer = jnp.fft.fft2(psf[view_index])
        blurred = jnp.real(jnp.fft.ifft2(jnp.fft.fft2(sampled, axes=(1, 2)) * transfer[None], axes=(1, 2)))
        quotient = views[view_index] / blurred
        smeared = jnp.real(jnp.fft.ifft2(jnp.fft.fft2(quotient, axes=(1, 2)) * jnp.conj(transfer)[None], axes=(1, 2)))
        correction = jnp.einsum("bij,yxbi->yxbj", blocks, smeared.reshape(NY, NX, NBLK, 128), precision=highest).reshape(NY, NX, NZ)
        log_summed = log_summed + jnp.log(correction)
    return estimate * jnp.exp(log_summed / VIEWS)
```

```python
import math

import jax
import jax.numpy as jnp
from jax import lax
from jax.sharding import PartitionSpec as P

highest = lax.Precision.HIGHEST


def block_matrix(multiplier, shifting, weights):
    positions = jnp.arange(128, dtype=jnp.int32)
    first_col = ((2 * multiplier[:, None] + 1) * positions[None, :] + shifting[:, None]) % 128
    second_col = (first_col + 1) % 128
    columns = positions[None, None, :]
    lower = (columns == first_col[:, :, None]).astype(jnp.float32)
    upper = (columns == second_col[:, :, None]).astype(jnp.float32)
    return (1.0 - weights)[:, :, None] * lower + weights[:, :, None] * upper


def angle_tables(rows, cols, length):
    row_index = lax.iota(jnp.int32, rows)[:, None]
    col_index = lax.iota(jnp.int32, cols)[None, :]
    angles = (row_index * col_index % length).astype(jnp.float32) * (2.0 * math.pi / length)
    return (jnp.cos(angles), jnp.sin(angles))


def contract(form, real_part, imag_part, cosine, sine_table, direction, want_imag):
    real_cos = jnp.einsum(form, real_part, cosine, precision=highest)
    if imag_part is None:
        return (real_cos, direction * jnp.einsum(form, real_part, sine_table, precision=highest))
    imag_sin = jnp.einsum(form, imag_part, sine_table, precision=highest)
    out_real = real_cos - direction * imag_sin
    if not want_imag:
        return (out_real, None)
    real_sin = jnp.einsum(form, real_part, sine_table, precision=highest)
    imag_cos = jnp.einsum(form, imag_part, cosine, precision=highest)
    return (out_real, imag_cos + direction * real_sin)


def complex_times(real_part, imag_part, cosine, sine_table):
    return (
        real_part * cosine - imag_part * sine_table,
        real_part * sine_table + imag_part * cosine,
    )


def factored(real_part, imag_part, axis, direction, forward, want_imag):
    length = real_part.shape[axis]
    second = 128
    first = length // second
    if axis == 2:
        leading, trailing = ("rx", "")
    else:
        leading, trailing = ("r", "z")
    outer = real_part.shape
    shape = outer[:axis] + (first, second) + outer[axis + 1 :]
    real_part = real_part.reshape(shape)
    if imag_part is not None:
        imag_part = imag_part.reshape(shape)
    first_cos, first_sin = angle_tables(first, first, first)
    second_cos, second_sin = angle_tables(second, second, second)
    twist_cos, twist_sin = angle_tables(first, second, length)
    if axis == 1:
        twist_cos = twist_cos[:, :, None]
        twist_sin = twist_sin[:, :, None]
    twist_sin = direction * twist_sin
    if forward:
        real_part, imag_part = contract(
            leading + "ab" + trailing + ",ak->" + leading + "kb" + trailing,
            real_part,
            imag_part,
            first_cos,
            first_sin,
            direction,
            True,
        )
        real_part, imag_part = complex_times(real_part, imag_part, twist_cos, twist_sin)
        real_part, imag_part = contract(
            leading + "kb" + trailing + ",bm->" + leading + "km" + trailing,
            real_part,
            imag_part,
            second_cos,
            second_sin,
            direction,
            want_imag,
        )
    else:
        real_part, imag_part = contract(
            leading + "km" + trailing + ",mb->" + leading + "kb" + trailing,
            real_part,
            imag_part,
            second_cos,
            second_sin,
            direction,
            True,
        )
        real_part, imag_part = complex_times(real_part, imag_part, twist_cos, twist_sin)
        real_part, imag_part = contract(
            leading + "kb" + trailing + ",ka->" + leading + "ab" + trailing,
            real_part,
            imag_part,
            first_cos,
            first_sin,
            direction,
            want_imag,
        )
    real_part = real_part.reshape(outer)
    if imag_part is not None:
        imag_part = imag_part.reshape(outer)
    return (real_part, imag_part)


def to_columns(real_part, imag_part):
    depth_real, depth_imag = factored(real_part, imag_part, 2, -1.0, True, True)
    rows = depth_real.shape[0]
    stacked = jnp.concatenate([depth_real, depth_imag], 0)
    moved = lax.all_to_all(stacked, "slab", split_axis=2, concat_axis=1, tiled=True)
    return factored(moved[:rows], moved[rows:], 1, -1.0, True, True)


def to_planes(real_part, imag_part):
    width_real, width_imag = factored(real_part, imag_part, 1, 1.0, False, True)
    rows = width_real.shape[0]
    stacked = jnp.concatenate([width_real, width_imag], 0)
    moved = lax.all_to_all(stacked, "slab", split_axis=1, concat_axis=2, tiled=True)
    scaling = 1.0 / (width_real.shape[1] * moved.shape[2])
    out_real, out_imag = factored(moved[:rows], moved[rows:], 2, 1.0, False, True)
    return (out_real * scaling, out_imag * scaling)


def pack_pairs(volume):
    return (volume[0::2], volume[1::2])


def unpack_pairs(real_part, imag_part):
    pairs, width, depth = real_part.shape
    return jnp.stack([real_part, imag_part], 1).reshape(2 * pairs, width, depth)


def shards(estimate, views, psf, pattern_mult, pattern_shift, interp):
    row_count, slab_width, depth = estimate.shape
    blocks = block_matrix(pattern_mult[0], pattern_shift[0], interp[0])
    block_count = depth // 128
    shaped = estimate.reshape(row_count, slab_width, block_count, 128)
    sampled = jnp.einsum("bij,yxbj->yxbi", blocks, shaped, precision=highest).reshape(
        row_count, slab_width, depth
    )
    packed_real, packed_imag = pack_pairs(sampled)
    packed_real = jnp.concatenate([packed_real, psf], 0)
    packed_imag = jnp.concatenate([packed_imag, jnp.zeros_like(psf)], 0)
    spectra_real, spectra_imag = to_columns(packed_real, packed_imag)
    transfer_real = spectra_real[-1:]
    transfer_imag = spectra_imag[-1:]
    spectra_real = spectra_real[:-1]
    spectra_imag = spectra_imag[:-1]
    filtered_real = spectra_real * transfer_real - spectra_imag * transfer_imag
    filtered_imag = spectra_real * transfer_imag + spectra_imag * transfer_real
    blurred = unpack_pairs(*to_planes(filtered_real, filtered_imag))
    quotient = views[0] / blurred
    packed_real, packed_imag = pack_pairs(quotient)
    spectra_real, spectra_imag = to_columns(packed_real, packed_imag)
    filtered_real = spectra_real * transfer_real + spectra_imag * transfer_imag
    filtered_imag = spectra_imag * transfer_real - spectra_real * transfer_imag
    smeared = unpack_pairs(*to_planes(filtered_real, filtered_imag))
    correction = jnp.einsum(
        "bij,yxbi->yxbj",
        blocks,
        smeared.reshape(row_count, slab_width, block_count, 128),
        precision=highest,
    ).reshape(row_count, slab_width, depth)
    log_terms = jnp.log(correction)
    view_count = lax.axis_size("view")
    summed = lax.psum(log_terms, "view")
    return estimate * jnp.exp(summed / view_count)


def solution(mesh):
    placed = (
        P(None, "slab", None),
        P("view", None, "slab", None),
        P("view", "slab", None),
        P("view", None),
        P("view", None),
        P("view", None, None),
    )
    return jax.shard_map(
        shards, mesh=mesh, in_specs=placed, out_specs=P(None, "slab", None), check_vma=False
    )
```

```python
import math

import jax
import jax.numpy as jnp
from jax import lax
from jax.sharding import PartitionSpec as P

highest = lax.Precision.HIGHEST


def block_matrix(multiplier, shifting, weights):
    positions = jnp.arange(128, dtype=jnp.int32)
    first_col = ((2 * multiplier[:, None] + 1) * positions[None, :] + shifting[:, None]) % 128
    second_col = (first_col + 1) % 128
    columns = positions[None, None, :]
    lower = (columns == first_col[:, :, None]).astype(jnp.float32)
    upper = (columns == second_col[:, :, None]).astype(jnp.float32)
    return (1.0 - weights)[:, :, None] * lower + weights[:, :, None] * upper


def angle_tables(rows, cols, length):
    row_index = lax.iota(jnp.int32, rows)[:, None]
    col_index = lax.iota(jnp.int32, cols)[None, :]
    angles = (row_index * col_index % length).astype(jnp.float32) * (2.0 * math.pi / length)
    return (jnp.cos(angles), jnp.sin(angles))


def unit_root(numerator, length):
    angle = 2.0 * math.pi * numerator / length
    return (round(math.cos(angle), 15), round(math.sin(angle), 15))


def small_stage(real_part, imag_part, axis, direction):
    count = real_part.shape[axis]

    def part(array, index):
        return lax.index_in_dim(array, index, axis, keepdims=False)

    real_in = [part(real_part, index) for index in range(count)]
    imag_in = None if imag_part is None else [part(imag_part, index) for index in range(count)]
    real_out, imag_out = [], []
    for out_index in range(count):
        real_sum, imag_sum = None, None
        for in_index in range(count):
            cosine, sine = unit_root(in_index * out_index, count)
            sine = direction * sine
            terms_real = []
            terms_imag = []
            if cosine != 0.0:
                terms_real.append(cosine * real_in[in_index])
                if imag_in is not None:
                    terms_imag.append(cosine * imag_in[in_index])
            if sine != 0.0:
                terms_imag.append(sine * real_in[in_index])
                if imag_in is not None:
                    terms_real.append(-sine * imag_in[in_index])
            for term in terms_real:
                real_sum = term if real_sum is None else real_sum + term
            for term in terms_imag:
                imag_sum = term if imag_sum is None else imag_sum + term
        if imag_sum is None:
            imag_sum = jnp.zeros_like(real_sum)
        real_out.append(real_sum)
        imag_out.append(imag_sum)
    return (jnp.stack(real_out, axis), jnp.stack(imag_out, axis))


def complex_times(real_part, imag_part, cosine, sine_table):
    return (
        real_part * cosine - imag_part * sine_table,
        real_part * sine_table + imag_part * cosine,
    )


def block_dft_matrix(length, direction):
    cosine, sine = angle_tables(length, length, length)
    sine = direction * sine
    top = jnp.concatenate([cosine, sine], 1)
    bottom = jnp.concatenate([-sine, cosine], 1)
    return jnp.concatenate([top, bottom], 0)


def large_stage(real_part, imag_part, axis, direction):
    length = real_part.shape[axis]
    if imag_part is None:
        imag_part = jnp.zeros_like(real_part)
    joined = jnp.concatenate([real_part, imag_part], axis)
    matrix = block_dft_matrix(length, direction)
    if axis == joined.ndim - 1:
        out = jnp.einsum("...j,jn->...n", joined, matrix, precision=highest)
    else:
        out = jnp.einsum("rkjz,jn->rknz", joined, matrix, precision=highest)
    return (
        lax.slice_in_dim(out, 0, length, axis=axis),
        lax.slice_in_dim(out, length, 2 * length, axis=axis),
    )


def factored(real_part, imag_part, axis, direction, forward, want_imag=True):
    length = real_part.shape[axis]
    second = 128
    first = length // second
    outer = real_part.shape
    shape = outer[:axis] + (first, second) + outer[axis + 1 :]
    real_part = real_part.reshape(shape)
    if imag_part is not None:
        imag_part = imag_part.reshape(shape)
    twist_cos, twist_sin = angle_tables(first, second, length)
    if axis == 1:
        twist_cos = twist_cos[:, :, None]
        twist_sin = twist_sin[:, :, None]
    twist_sin = direction * twist_sin
    if forward:
        real_part, imag_part = small_stage(real_part, imag_part, axis, direction)
        real_part, imag_part = complex_times(real_part, imag_part, twist_cos, twist_sin)
        real_part, imag_part = large_stage(real_part, imag_part, axis + 1, direction)
    else:
        real_part, imag_part = large_stage(real_part, imag_part, axis + 1, direction)
        real_part, imag_part = complex_times(real_part, imag_part, twist_cos, twist_sin)
        real_part, imag_part = small_stage(real_part, imag_part, axis, direction)
    return (real_part.reshape(outer), imag_part.reshape(outer))


def to_columns(real_part, imag_part):
    depth_real, depth_imag = factored(real_part, imag_part, 2, -1.0, True)
    rows = depth_real.shape[0]
    stacked = jnp.concatenate([depth_real, depth_imag], 0)
    moved = lax.all_to_all(stacked, "slab", split_axis=2, concat_axis=1, tiled=True)
    return factored(moved[:rows], moved[rows:], 1, -1.0, True)


def to_planes(real_part, imag_part):
    width_real, width_imag = factored(real_part, imag_part, 1, 1.0, False)
    rows = width_real.shape[0]
    stacked = jnp.concatenate([width_real, width_imag], 0)
    moved = lax.all_to_all(stacked, "slab", split_axis=1, concat_axis=2, tiled=True)
    return factored(moved[:rows], moved[rows:], 2, 1.0, False)


def pack_pairs(volume):
    return (volume[0::2], volume[1::2])


def unpack_pairs(real_part, imag_part):
    pairs, width, depth = real_part.shape
    return jnp.stack([real_part, imag_part], 1).reshape(2 * pairs, width, depth)


def shards(estimate, views, psf, pattern_mult, pattern_shift, interp):
    row_count, slab_width, depth = estimate.shape
    blocks = block_matrix(pattern_mult[0], pattern_shift[0], interp[0])
    block_count = depth // 128
    shaped = estimate.reshape(row_count, slab_width, block_count, 128)
    sampled = jnp.einsum("bij,yxbj->yxbi", blocks, shaped, precision=highest).reshape(
        row_count, slab_width, depth
    )
    packed_real, packed_imag = pack_pairs(sampled)
    packed_real = jnp.concatenate([packed_real, psf], 0)
    packed_imag = jnp.concatenate([packed_imag, jnp.zeros_like(psf)], 0)
    spectra_real, spectra_imag = to_columns(packed_real, packed_imag)
    scaling = 1.0 / (spectra_real.shape[1] * depth)
    transfer_real = spectra_real[-1:] * scaling
    transfer_imag = spectra_imag[-1:] * scaling
    spectra_real = spectra_real[:-1]
    spectra_imag = spectra_imag[:-1]
    filtered_real = spectra_real * transfer_real - spectra_imag * transfer_imag
    filtered_imag = spectra_real * transfer_imag + spectra_imag * transfer_real
    blurred = unpack_pairs(*to_planes(filtered_real, filtered_imag))
    quotient = views[0] / blurred
    packed_real, packed_imag = pack_pairs(quotient)
    spectra_real, spectra_imag = to_columns(packed_real, packed_imag)
    filtered_real = spectra_real * transfer_real + spectra_imag * transfer_imag
    filtered_imag = spectra_imag * transfer_real - spectra_real * transfer_imag
    smeared = unpack_pairs(*to_planes(filtered_real, filtered_imag))
    correction = jnp.einsum(
        "bij,yxbi->yxbj",
        blocks,
        smeared.reshape(row_count, slab_width, block_count, 128),
        precision=highest,
    ).reshape(row_count, slab_width, depth)
    log_terms = jnp.log(correction)
    view_count = lax.axis_size("view")
    summed = lax.psum(log_terms, "view")
    return estimate * jnp.exp(summed / view_count)


def solution(mesh):
    placed = (
        P(None, "slab", None),
        P("view", None, "slab", None),
        P("view", "slab", None),
        P("view", None),
        P("view", None),
        P("view", None, None),
    )
    return jax.shard_map(
        shards, mesh=mesh, in_specs=placed, out_specs=P(None, "slab", None), check_vma=False
    )
```

```python
import math

import jax
import jax.numpy as jnp
from jax import lax
from jax.sharding import PartitionSpec as P

highest = lax.Precision.HIGHEST


def block_matrix(multiplier, shifting, weights):
    positions = jnp.arange(128, dtype=jnp.int32)
    first_col = ((2 * multiplier[:, None] + 1) * positions[None, :] + shifting[:, None]) % 128
    second_col = (first_col + 1) % 128
    columns = positions[None, None, :]
    lower = (columns == first_col[:, :, None]).astype(jnp.float32)
    upper = (columns == second_col[:, :, None]).astype(jnp.float32)
    return (1.0 - weights)[:, :, None] * lower + weights[:, :, None] * upper


def angle_tables(rows, cols, length):
    row_index = lax.iota(jnp.int32, rows)[:, None]
    col_index = lax.iota(jnp.int32, cols)[None, :]
    angles = (row_index * col_index % length).astype(jnp.float32) * (2.0 * math.pi / length)
    return (jnp.cos(angles), jnp.sin(angles))


def unit_root(numerator, length):
    angle = 2.0 * math.pi * numerator / length
    return (round(math.cos(angle), 15), round(math.sin(angle), 15))


def small_stage(real_part, imag_part, axis, direction):
    count = real_part.shape[axis]

    def part(array, index):
        return lax.index_in_dim(array, index, axis, keepdims=False)

    real_in = [part(real_part, index) for index in range(count)]
    imag_in = None if imag_part is None else [part(imag_part, index) for index in range(count)]
    real_out, imag_out = [], []
    for out_index in range(count):
        real_sum, imag_sum = None, None
        for in_index in range(count):
            cosine, sine = unit_root(in_index * out_index, count)
            sine = direction * sine
            terms_real = []
            terms_imag = []
            if cosine != 0.0:
                terms_real.append(cosine * real_in[in_index])
                if imag_in is not None:
                    terms_imag.append(cosine * imag_in[in_index])
            if sine != 0.0:
                terms_imag.append(sine * real_in[in_index])
                if imag_in is not None:
                    terms_real.append(-sine * imag_in[in_index])
            for term in terms_real:
                real_sum = term if real_sum is None else real_sum + term
            for term in terms_imag:
                imag_sum = term if imag_sum is None else imag_sum + term
        if imag_sum is None:
            imag_sum = jnp.zeros_like(real_sum)
        real_out.append(real_sum)
        imag_out.append(imag_sum)
    return (jnp.stack(real_out, axis), jnp.stack(imag_out, axis))


def complex_times(real_part, imag_part, cosine, sine_table):
    return (
        real_part * cosine - imag_part * sine_table,
        real_part * sine_table + imag_part * cosine,
    )


def block_dft_matrix(length, direction):
    cosine, sine = angle_tables(length, length, length)
    sine = direction * sine
    top = jnp.concatenate([cosine, sine], 1)
    bottom = jnp.concatenate([-sine, cosine], 1)
    return jnp.concatenate([top, bottom], 0)


def large_stage(real_part, imag_part, axis, direction):
    length = real_part.shape[axis]
    if imag_part is None:
        imag_part = jnp.zeros_like(real_part)
    joined = jnp.concatenate([real_part, imag_part], axis)
    matrix = block_dft_matrix(length, direction)
    if axis == joined.ndim - 1:
        out = jnp.einsum("...j,jn->...n", joined, matrix, precision=highest)
    else:
        out = jnp.einsum("rkjz,jn->rknz", joined, matrix, precision=highest)
    return (
        lax.slice_in_dim(out, 0, length, axis=axis),
        lax.slice_in_dim(out, length, 2 * length, axis=axis),
    )


def factored(real_part, imag_part, axis, direction, forward, want_imag=True):
    length = real_part.shape[axis]
    second = 128
    first = length // second
    outer = real_part.shape
    shape = outer[:axis] + (first, second) + outer[axis + 1 :]
    real_part = real_part.reshape(shape)
    if imag_part is not None:
        imag_part = imag_part.reshape(shape)
    twist_cos, twist_sin = angle_tables(first, second, length)
    if axis == 1:
        twist_cos = twist_cos[:, :, None]
        twist_sin = twist_sin[:, :, None]
    twist_sin = direction * twist_sin
    if forward:
        real_part, imag_part = small_stage(real_part, imag_part, axis, direction)
        real_part, imag_part = complex_times(real_part, imag_part, twist_cos, twist_sin)
        real_part, imag_part = large_stage(real_part, imag_part, axis + 1, direction)
    else:
        real_part, imag_part = large_stage(real_part, imag_part, axis + 1, direction)
        real_part, imag_part = complex_times(real_part, imag_part, twist_cos, twist_sin)
        real_part, imag_part = small_stage(real_part, imag_part, axis, direction)
    return (real_part.reshape(outer), imag_part.reshape(outer))


def to_columns(real_part, imag_part):
    depth_real, depth_imag = factored(real_part, imag_part, 2, -1.0, True)
    rows = depth_real.shape[0]
    stacked = jnp.concatenate([depth_real, depth_imag], 0)
    moved = lax.all_to_all(stacked, "slab", split_axis=2, concat_axis=1, tiled=True)
    return factored(moved[:rows], moved[rows:], 1, -1.0, True)


def to_planes(real_part, imag_part):
    width_real, width_imag = factored(real_part, imag_part, 1, 1.0, False)
    rows = width_real.shape[0]
    stacked = jnp.concatenate([width_real, width_imag], 0)
    moved = lax.all_to_all(stacked, "slab", split_axis=1, concat_axis=2, tiled=True)
    return factored(moved[:rows], moved[rows:], 2, 1.0, False)


def pack_pairs(volume):
    return (volume[0::2], volume[1::2])


def unpack_pairs(real_part, imag_part):
    pairs, width, depth = real_part.shape
    return jnp.stack([real_part, imag_part], 1).reshape(2 * pairs, width, depth)


def general_shards(estimate, views, psf, pattern_mult, pattern_shift, interp):
    row_count, slab_width, depth = estimate.shape
    blocks = block_matrix(pattern_mult[0], pattern_shift[0], interp[0])
    block_count = depth // 128
    shaped = estimate.reshape(row_count, slab_width, block_count, 128)
    sampled = jnp.einsum("bij,yxbj->yxbi", blocks, shaped, precision=highest).reshape(
        row_count, slab_width, depth
    )
    packed_real, packed_imag = pack_pairs(sampled)
    packed_real = jnp.concatenate([packed_real, psf], 0)
    packed_imag = jnp.concatenate([packed_imag, jnp.zeros_like(psf)], 0)
    spectra_real, spectra_imag = to_columns(packed_real, packed_imag)
    scaling = 1.0 / (spectra_real.shape[1] * depth)
    transfer_real = spectra_real[-1:] * scaling
    transfer_imag = spectra_imag[-1:] * scaling
    spectra_real = spectra_real[:-1]
    spectra_imag = spectra_imag[:-1]
    filtered_real = spectra_real * transfer_real - spectra_imag * transfer_imag
    filtered_imag = spectra_real * transfer_imag + spectra_imag * transfer_real
    blurred = unpack_pairs(*to_planes(filtered_real, filtered_imag))
    quotient = views[0] / blurred
    packed_real, packed_imag = pack_pairs(quotient)
    spectra_real, spectra_imag = to_columns(packed_real, packed_imag)
    filtered_real = spectra_real * transfer_real + spectra_imag * transfer_imag
    filtered_imag = spectra_imag * transfer_real - spectra_real * transfer_imag
    smeared = unpack_pairs(*to_planes(filtered_real, filtered_imag))
    correction = jnp.einsum(
        "bij,yxbi->yxbj",
        blocks,
        smeared.reshape(row_count, slab_width, block_count, 128),
        precision=highest,
    ).reshape(row_count, slab_width, depth)
    log_terms = jnp.log(correction)
    view_count = lax.axis_size("view")
    summed = lax.psum(log_terms, "view")
    return estimate * jnp.exp(summed / view_count)


def swap_halves(joined):
    half = joined.shape[-1] // 2
    return jnp.concatenate([-joined[..., half:], joined[..., :half]], -1)


def lead_stage(joined, direction):
    count = joined.shape[0]
    parts = [joined[index] for index in range(count)]
    turned = [swap_halves(part) for part in parts]
    outs = []
    for out_index in range(count):
        total = None
        for in_index in range(count):
            cosine, sine = unit_root(in_index * out_index, count)
            sine = direction * sine
            for weight, term in ((cosine, parts[in_index]), (sine, turned[in_index])):
                if weight != 0.0:
                    term = weight * term
                    total = term if total is None else total + term
        outs.append(total)
    return jnp.stack(outs, 0)


def joined_twist(joined, length, direction, lanes):
    first, second = joined.shape[0], (joined.shape[-1] // 2 if lanes else joined.shape[2])
    cosine, sine = angle_tables(first, second, length)
    sine = direction * sine
    if lanes:
        cosine = jnp.concatenate([cosine, cosine], 1)[:, None, None, :]
        sine = jnp.concatenate([sine, sine], 1)[:, None, None, :]
    else:
        cosine = cosine[:, None, :, None]
        sine = sine[:, None, :, None]
    return joined * cosine + swap_halves(joined) * sine


def lane_stage(joined, direction):
    length = joined.shape[-1] // 2
    matrix = block_dft_matrix(length, direction)
    return jnp.einsum("...j,jn->...n", joined, matrix, precision=highest)


def row_stage(joined, direction):
    length = joined.shape[2]
    cosine, sine = angle_tables(length, length, length)
    matrix = jnp.concatenate([cosine, direction * sine], 0)
    both = jnp.concatenate([joined, swap_halves(joined)], 2)
    return jnp.einsum("krjl,jm->krml", both, matrix, precision=highest)


def depth_forward(joined, depth):
    joined = lead_stage(joined, -1.0)
    joined = joined_twist(joined, depth, -1.0, True)
    return lane_stage(joined, -1.0)


def depth_inverse(joined, depth):
    joined = lane_stage(joined, 1.0)
    joined = joined_twist(joined, depth, 1.0, True)
    return lead_stage(joined, 1.0)


def width_forward(joined, width):
    joined = lead_stage(joined, -1.0)
    joined = joined_twist(joined, width, -1.0, False)
    return row_stage(joined, -1.0)


def width_inverse(joined, width):
    joined = row_stage(joined, 1.0)
    joined = joined_twist(joined, width, 1.0, False)
    return lead_stage(joined, 1.0)


def joined_times(joined, transfer_real, transfer_imag):
    return joined * transfer_real + swap_halves(joined) * transfer_imag


def to_blocks(volume, block_count):
    rows, width, depth = volume.shape
    lanes = depth // block_count
    shaped = volume.reshape(rows // 2, 2, width, block_count, lanes)
    return shaped.transpose(3, 0, 2, 1, 4).reshape(block_count, rows // 2, width, 2 * lanes)


def from_blocks(blocked):
    block_count, pairs, width, lanes = blocked.shape
    shaped = blocked.reshape(block_count, pairs, width, 2, lanes // 2)
    return shaped.transpose(1, 3, 2, 0, 4).reshape(2 * pairs, width, block_count * lanes // 2)


def shards(estimate, views, psf, pattern_mult, pattern_shift, interp):
    row_count, slab_width, depth = estimate.shape
    slab_count = lax.axis_size("slab")
    block_count = depth // 128
    width = slab_width * slab_count
    if not (
        block_count == slab_count
        and slab_width == 128
        and width // 128 == slab_count
        and row_count % 2 == 0
    ):
        return general_shards(estimate, views, psf, pattern_mult, pattern_shift, interp)
    blocks = block_matrix(pattern_mult[0], pattern_shift[0], interp[0])
    empty = jnp.zeros_like(blocks)
    doubled = jnp.concatenate(
        [jnp.concatenate([blocks, empty], 2), jnp.concatenate([empty, blocks], 2)], 1
    )
    sampled = jnp.einsum(
        "apxl,aml->apxm", to_blocks(estimate, block_count), doubled, precision=highest
    )
    pairs = row_count // 2
    spread = psf.reshape(slab_width, block_count, 128).transpose(1, 0, 2)[:, None]
    spread = jnp.concatenate([spread, jnp.zeros_like(spread)], -1)
    packed = jnp.concatenate([sampled, spread], 1)
    spectra = depth_forward(packed, depth)
    spectra = lax.all_to_all(spectra, "slab", split_axis=0, concat_axis=0, tiled=True)
    spectra = width_forward(spectra, width)
    scaling = 1.0 / (width * depth)
    transfer = spectra[:, pairs:] * scaling
    spectra = spectra[:, :pairs]
    half = transfer.shape[-1] // 2
    transfer_real = jnp.concatenate([transfer[..., :half], transfer[..., :half]], -1)
    transfer_imag = jnp.concatenate([transfer[..., half:], transfer[..., half:]], -1)

    def convolve(spectra, transfer_imag):
        filtered = joined_times(spectra, transfer_real, transfer_imag)
        planes = width_inverse(filtered, width)
        planes = lax.all_to_all(planes, "slab", split_axis=0, concat_axis=0, tiled=True)
        return depth_inverse(planes, depth)

    blurred = convolve(spectra, transfer_imag)
    quotient = to_blocks(views[0], block_count) / blurred
    spectra = depth_forward(quotient, depth)
    spectra = lax.all_to_all(spectra, "slab", split_axis=0, concat_axis=0, tiled=True)
    spectra = width_forward(spectra, width)
    smeared = convolve(spectra, -transfer_imag)
    correction = jnp.einsum("apxm,aml->apxl", smeared, doubled, precision=highest)
    log_terms = jnp.log(correction)
    view_count = lax.axis_size("view")
    summed = from_blocks(lax.psum(log_terms, "view"))
    return estimate * jnp.exp(summed / view_count)


def solution(mesh):
    placed = (
        P(None, "slab", None),
        P("view", None, "slab", None),
        P("view", "slab", None),
        P("view", None),
        P("view", None),
        P("view", None, None),
    )
    return jax.shard_map(
        shards, mesh=mesh, in_specs=placed, out_specs=P(None, "slab", None), check_vma=False
    )
```

```python
import math

import jax
import jax.numpy as jnp
from jax import lax
from jax.sharding import PartitionSpec as P

highest = lax.Precision.HIGHEST


def block_matrix(multiplier, shifting, weights):
    positions = jnp.arange(128, dtype=jnp.int32)
    first_col = ((2 * multiplier[:, None] + 1) * positions[None, :] + shifting[:, None]) % 128
    second_col = (first_col + 1) % 128
    columns = positions[None, None, :]
    lower = (columns == first_col[:, :, None]).astype(jnp.float32)
    upper = (columns == second_col[:, :, None]).astype(jnp.float32)
    return (1.0 - weights)[:, :, None] * lower + weights[:, :, None] * upper


def angle_tables(rows, cols, length):
    row_index = lax.iota(jnp.int32, rows)[:, None]
    col_index = lax.iota(jnp.int32, cols)[None, :]
    angles = (row_index * col_index % length).astype(jnp.float32) * (2.0 * math.pi / length)
    return (jnp.cos(angles), jnp.sin(angles))


def unit_root(numerator, length):
    angle = 2.0 * math.pi * numerator / length
    return (round(math.cos(angle), 15), round(math.sin(angle), 15))


def small_stage(real_part, imag_part, axis, direction):
    count = real_part.shape[axis]

    def part(array, index):
        return lax.index_in_dim(array, index, axis, keepdims=False)

    real_in = [part(real_part, index) for index in range(count)]
    imag_in = None if imag_part is None else [part(imag_part, index) for index in range(count)]
    real_out, imag_out = [], []
    for out_index in range(count):
        real_sum, imag_sum = None, None
        for in_index in range(count):
            cosine, sine = unit_root(in_index * out_index, count)
            sine = direction * sine
            terms_real = []
            terms_imag = []
            if cosine != 0.0:
                terms_real.append(cosine * real_in[in_index])
                if imag_in is not None:
                    terms_imag.append(cosine * imag_in[in_index])
            if sine != 0.0:
                terms_imag.append(sine * real_in[in_index])
                if imag_in is not None:
                    terms_real.append(-sine * imag_in[in_index])
            for term in terms_real:
                real_sum = term if real_sum is None else real_sum + term
            for term in terms_imag:
                imag_sum = term if imag_sum is None else imag_sum + term
        if imag_sum is None:
            imag_sum = jnp.zeros_like(real_sum)
        real_out.append(real_sum)
        imag_out.append(imag_sum)
    return (jnp.stack(real_out, axis), jnp.stack(imag_out, axis))


def complex_times(real_part, imag_part, cosine, sine_table):
    return (
        real_part * cosine - imag_part * sine_table,
        real_part * sine_table + imag_part * cosine,
    )


def block_dft_matrix(length, direction):
    cosine, sine = angle_tables(length, length, length)
    sine = direction * sine
    top = jnp.concatenate([cosine, sine], 1)
    bottom = jnp.concatenate([-sine, cosine], 1)
    return jnp.concatenate([top, bottom], 0)


def large_stage(real_part, imag_part, axis, direction):
    length = real_part.shape[axis]
    if imag_part is None:
        imag_part = jnp.zeros_like(real_part)
    joined = jnp.concatenate([real_part, imag_part], axis)
    matrix = block_dft_matrix(length, direction)
    if axis == joined.ndim - 1:
        out = jnp.einsum("...j,jn->...n", joined, matrix, precision=highest)
    else:
        out = jnp.einsum("rkjz,jn->rknz", joined, matrix, precision=highest)
    return (
        lax.slice_in_dim(out, 0, length, axis=axis),
        lax.slice_in_dim(out, length, 2 * length, axis=axis),
    )


def factored(real_part, imag_part, axis, direction, forward, want_imag=True):
    length = real_part.shape[axis]
    second = 128
    first = length // second
    outer = real_part.shape
    shape = outer[:axis] + (first, second) + outer[axis + 1 :]
    real_part = real_part.reshape(shape)
    if imag_part is not None:
        imag_part = imag_part.reshape(shape)
    twist_cos, twist_sin = angle_tables(first, second, length)
    if axis == 1:
        twist_cos = twist_cos[:, :, None]
        twist_sin = twist_sin[:, :, None]
    twist_sin = direction * twist_sin
    if forward:
        real_part, imag_part = small_stage(real_part, imag_part, axis, direction)
        real_part, imag_part = complex_times(real_part, imag_part, twist_cos, twist_sin)
        real_part, imag_part = large_stage(real_part, imag_part, axis + 1, direction)
    else:
        real_part, imag_part = large_stage(real_part, imag_part, axis + 1, direction)
        real_part, imag_part = complex_times(real_part, imag_part, twist_cos, twist_sin)
        real_part, imag_part = small_stage(real_part, imag_part, axis, direction)
    return (real_part.reshape(outer), imag_part.reshape(outer))


def to_columns(real_part, imag_part):
    depth_real, depth_imag = factored(real_part, imag_part, 2, -1.0, True)
    rows = depth_real.shape[0]
    stacked = jnp.concatenate([depth_real, depth_imag], 0)
    moved = lax.all_to_all(stacked, "slab", split_axis=2, concat_axis=1, tiled=True)
    return factored(moved[:rows], moved[rows:], 1, -1.0, True)


def to_planes(real_part, imag_part):
    width_real, width_imag = factored(real_part, imag_part, 1, 1.0, False)
    rows = width_real.shape[0]
    stacked = jnp.concatenate([width_real, width_imag], 0)
    moved = lax.all_to_all(stacked, "slab", split_axis=1, concat_axis=2, tiled=True)
    return factored(moved[:rows], moved[rows:], 2, 1.0, False)


def pack_pairs(volume):
    return (volume[0::2], volume[1::2])


def unpack_pairs(real_part, imag_part):
    pairs, width, depth = real_part.shape
    return jnp.stack([real_part, imag_part], 1).reshape(2 * pairs, width, depth)


def general_shards(estimate, views, psf, pattern_mult, pattern_shift, interp):
    row_count, slab_width, depth = estimate.shape
    blocks = block_matrix(pattern_mult[0], pattern_shift[0], interp[0])
    block_count = depth // 128
    shaped = estimate.reshape(row_count, slab_width, block_count, 128)
    sampled = jnp.einsum("bij,yxbj->yxbi", blocks, shaped, precision=highest).reshape(
        row_count, slab_width, depth
    )
    packed_real, packed_imag = pack_pairs(sampled)
    packed_real = jnp.concatenate([packed_real, psf], 0)
    packed_imag = jnp.concatenate([packed_imag, jnp.zeros_like(psf)], 0)
    spectra_real, spectra_imag = to_columns(packed_real, packed_imag)
    scaling = 1.0 / (spectra_real.shape[1] * depth)
    transfer_real = spectra_real[-1:] * scaling
    transfer_imag = spectra_imag[-1:] * scaling
    spectra_real = spectra_real[:-1]
    spectra_imag = spectra_imag[:-1]
    filtered_real = spectra_real * transfer_real - spectra_imag * transfer_imag
    filtered_imag = spectra_real * transfer_imag + spectra_imag * transfer_real
    blurred = unpack_pairs(*to_planes(filtered_real, filtered_imag))
    quotient = views[0] / blurred
    packed_real, packed_imag = pack_pairs(quotient)
    spectra_real, spectra_imag = to_columns(packed_real, packed_imag)
    filtered_real = spectra_real * transfer_real + spectra_imag * transfer_imag
    filtered_imag = spectra_imag * transfer_real - spectra_real * transfer_imag
    smeared = unpack_pairs(*to_planes(filtered_real, filtered_imag))
    correction = jnp.einsum(
        "bij,yxbi->yxbj",
        blocks,
        smeared.reshape(row_count, slab_width, block_count, 128),
        precision=highest,
    ).reshape(row_count, slab_width, depth)
    log_terms = jnp.log(correction)
    view_count = lax.axis_size("view")
    summed = lax.psum(log_terms, "view")
    return estimate * jnp.exp(summed / view_count)


def swap_halves(joined):
    half = joined.shape[-1] // 2
    return jnp.concatenate([-joined[..., half:], joined[..., :half]], -1)


def lead_stage(joined, direction):
    count = joined.shape[0]
    parts = [joined[index] for index in range(count)]
    turned = [swap_halves(part) for part in parts]
    outs = []
    for out_index in range(count):
        total = None
        for in_index in range(count):
            cosine, sine = unit_root(in_index * out_index, count)
            sine = direction * sine
            for weight, term in ((cosine, parts[in_index]), (sine, turned[in_index])):
                if weight != 0.0:
                    term = weight * term
                    total = term if total is None else total + term
        outs.append(total)
    return jnp.stack(outs, 0)


def joined_twist(joined, length, direction, lanes):
    first, second = joined.shape[0], (joined.shape[-1] // 2 if lanes else joined.shape[2])
    cosine, sine = angle_tables(first, second, length)
    sine = direction * sine
    if lanes:
        cosine = jnp.concatenate([cosine, cosine], 1)[:, None, None, :]
        sine = jnp.concatenate([sine, sine], 1)[:, None, None, :]
    else:
        cosine = cosine[:, None, :, None]
        sine = sine[:, None, :, None]
    return joined * cosine + swap_halves(joined) * sine


def lane_stage(joined, direction):
    length = joined.shape[-1] // 2
    matrix = block_dft_matrix(length, direction)
    return jnp.einsum("...j,jn->...n", joined, matrix, precision=highest)


def row_stage(joined, direction):
    length = joined.shape[2]
    cosine, sine = angle_tables(length, length, length)
    matrix = jnp.concatenate([cosine, direction * sine], 0)
    both = jnp.concatenate([joined, swap_halves(joined)], 2)
    return jnp.einsum("krjl,jm->krml", both, matrix, precision=highest)


def depth_forward(joined, depth):
    joined = lead_stage(joined, -1.0)
    joined = joined_twist(joined, depth, -1.0, True)
    return lane_stage(joined, -1.0)


def depth_inverse(joined, depth):
    joined = lane_stage(joined, 1.0)
    joined = joined_twist(joined, depth, 1.0, True)
    return lead_stage(joined, 1.0)


def width_forward(joined, width):
    joined = lead_stage(joined, -1.0)
    joined = joined_twist(joined, width, -1.0, False)
    return row_stage(joined, -1.0)


def width_inverse(joined, width):
    joined = row_stage(joined, 1.0)
    joined = joined_twist(joined, width, 1.0, False)
    return lead_stage(joined, 1.0)


def joined_times(joined, transfer_real, transfer_imag):
    return joined * transfer_real + swap_halves(joined) * transfer_imag


def to_blocks(volume, block_count):
    rows, width, depth = volume.shape
    lanes = depth // block_count
    shaped = volume.reshape(rows // 2, 2, width, block_count, lanes)
    return shaped.transpose(3, 0, 2, 1, 4).reshape(block_count, rows // 2, width, 2 * lanes)


def from_blocks(blocked):
    block_count, pairs, width, lanes = blocked.shape
    shaped = blocked.reshape(block_count, pairs, width, 2, lanes // 2)
    return shaped.transpose(1, 3, 2, 0, 4).reshape(2 * pairs, width, block_count * lanes // 2)


def shards(estimate, views, psf, pattern_mult, pattern_shift, interp):
    row_count, slab_width, depth = estimate.shape
    slab_count = lax.axis_size("slab")
    block_count = depth // 128
    width = slab_width * slab_count
    if not (
        block_count == slab_count
        and slab_width == 128
        and width // 128 == slab_count
        and row_count % 2 == 0
    ):
        return general_shards(estimate, views, psf, pattern_mult, pattern_shift, interp)
    blocks = block_matrix(pattern_mult[0], pattern_shift[0], interp[0])
    empty = jnp.zeros_like(blocks)
    doubled = jnp.concatenate(
        [jnp.concatenate([blocks, empty], 2), jnp.concatenate([empty, blocks], 2)], 1
    )
    sampled = jnp.einsum(
        "apxl,aml->apxm", to_blocks(estimate, block_count), doubled, precision=highest
    )
    pairs = row_count // 2
    spread = psf.reshape(slab_width, block_count, 128).transpose(1, 0, 2)[:, None]
    spread = jnp.concatenate([spread, jnp.zeros_like(spread)], -1)

    def to_columns_blocked(planes):
        spectra = depth_forward(planes, depth)
        spectra = lax.all_to_all(spectra, "slab", split_axis=0, concat_axis=0, tiled=True)
        return width_forward(spectra, width)

    transfer = to_columns_blocked(spread) * (1.0 / (width * depth))
    half = transfer.shape[-1] // 2
    transfer_real = jnp.concatenate([transfer[..., :half], transfer[..., :half]], -1)
    transfer_imag = jnp.concatenate([transfer[..., half:], transfer[..., half:]], -1)

    def convolve(spectra, transfer_imag):
        filtered = joined_times(spectra, transfer_real, transfer_imag)
        planes = width_inverse(filtered, width)
        planes = lax.all_to_all(planes, "slab", split_axis=0, concat_axis=0, tiled=True)
        return depth_inverse(planes, depth)

    seen = to_blocks(views[0], block_count)
    log_terms = []
    for pair in range(pairs):
        rows = slice(pair, pair + 1)
        blurred = convolve(to_columns_blocked(sampled[:, rows]), transfer_imag)
        quotient = seen[:, rows] / blurred
        smeared = convolve(to_columns_blocked(quotient), -transfer_imag)
        correction = jnp.einsum("apxm,aml->apxl", smeared, doubled, precision=highest)
        log_terms.append(from_blocks(jnp.log(correction)))
    view_count = lax.axis_size("view")
    summed = lax.psum(jnp.concatenate(log_terms, 0), "view")
    return estimate * jnp.exp(summed / view_count)


def solution(mesh):
    placed = (
        P(None, "slab", None),
        P("view", None, "slab", None),
        P("view", "slab", None),
        P("view", None),
        P("view", None),
        P("view", None, None),
    )
    return jax.shard_map(
        shards, mesh=mesh, in_specs=placed, out_specs=P(None, "slab", None), check_vma=False
    )
```

```python
import math

import jax
import jax.numpy as jnp
from jax import lax
from jax.sharding import PartitionSpec as P

highest = lax.Precision.HIGHEST


def block_matrix(multiplier, shifting, weights):
    positions = jnp.arange(128, dtype=jnp.int32)
    first_col = ((2 * multiplier[:, None] + 1) * positions[None, :] + shifting[:, None]) % 128
    second_col = (first_col + 1) % 128
    columns = positions[None, None, :]
    lower = (columns == first_col[:, :, None]).astype(jnp.float32)
    upper = (columns == second_col[:, :, None]).astype(jnp.float32)
    return (1.0 - weights)[:, :, None] * lower + weights[:, :, None] * upper


def angle_tables(rows, cols, length):
    row_index = lax.iota(jnp.int32, rows)[:, None]
    col_index = lax.iota(jnp.int32, cols)[None, :]
    angles = (row_index * col_index % length).astype(jnp.float32) * (2.0 * math.pi / length)
    return (jnp.cos(angles), jnp.sin(angles))


def unit_root(numerator, length):
    angle = 2.0 * math.pi * numerator / length
    return (round(math.cos(angle), 15), round(math.sin(angle), 15))


def small_stage(real_part, imag_part, axis, direction):
    count = real_part.shape[axis]

    def part(array, index):
        return lax.index_in_dim(array, index, axis, keepdims=False)

    real_in = [part(real_part, index) for index in range(count)]
    imag_in = None if imag_part is None else [part(imag_part, index) for index in range(count)]
    real_out, imag_out = [], []
    for out_index in range(count):
        real_sum, imag_sum = None, None
        for in_index in range(count):
            cosine, sine = unit_root(in_index * out_index, count)
            sine = direction * sine
            terms_real = []
            terms_imag = []
            if cosine != 0.0:
                terms_real.append(cosine * real_in[in_index])
                if imag_in is not None:
                    terms_imag.append(cosine * imag_in[in_index])
            if sine != 0.0:
                terms_imag.append(sine * real_in[in_index])
                if imag_in is not None:
                    terms_real.append(-sine * imag_in[in_index])
            for term in terms_real:
                real_sum = term if real_sum is None else real_sum + term
            for term in terms_imag:
                imag_sum = term if imag_sum is None else imag_sum + term
        if imag_sum is None:
            imag_sum = jnp.zeros_like(real_sum)
        real_out.append(real_sum)
        imag_out.append(imag_sum)
    return (jnp.stack(real_out, axis), jnp.stack(imag_out, axis))


def complex_times(real_part, imag_part, cosine, sine_table):
    return (
        real_part * cosine - imag_part * sine_table,
        real_part * sine_table + imag_part * cosine,
    )


def block_dft_matrix(length, direction):
    cosine, sine = angle_tables(length, length, length)
    sine = direction * sine
    top = jnp.concatenate([cosine, sine], 1)
    bottom = jnp.concatenate([-sine, cosine], 1)
    return jnp.concatenate([top, bottom], 0)


def large_stage(real_part, imag_part, axis, direction):
    length = real_part.shape[axis]
    if imag_part is None:
        imag_part = jnp.zeros_like(real_part)
    joined = jnp.concatenate([real_part, imag_part], axis)
    matrix = block_dft_matrix(length, direction)
    if axis == joined.ndim - 1:
        out = jnp.einsum("...j,jn->...n", joined, matrix, precision=highest)
    else:
        out = jnp.einsum("rkjz,jn->rknz", joined, matrix, precision=highest)
    return (
        lax.slice_in_dim(out, 0, length, axis=axis),
        lax.slice_in_dim(out, length, 2 * length, axis=axis),
    )


def factored(real_part, imag_part, axis, direction, forward, want_imag=True):
    length = real_part.shape[axis]
    second = 128
    first = length // second
    outer = real_part.shape
    shape = outer[:axis] + (first, second) + outer[axis + 1 :]
    real_part = real_part.reshape(shape)
    if imag_part is not None:
        imag_part = imag_part.reshape(shape)
    twist_cos, twist_sin = angle_tables(first, second, length)
    if axis == 1:
        twist_cos = twist_cos[:, :, None]
        twist_sin = twist_sin[:, :, None]
    twist_sin = direction * twist_sin
    if forward:
        real_part, imag_part = small_stage(real_part, imag_part, axis, direction)
        real_part, imag_part = complex_times(real_part, imag_part, twist_cos, twist_sin)
        real_part, imag_part = large_stage(real_part, imag_part, axis + 1, direction)
    else:
        real_part, imag_part = large_stage(real_part, imag_part, axis + 1, direction)
        real_part, imag_part = complex_times(real_part, imag_part, twist_cos, twist_sin)
        real_part, imag_part = small_stage(real_part, imag_part, axis, direction)
    return (real_part.reshape(outer), imag_part.reshape(outer))


def to_columns(real_part, imag_part):
    depth_real, depth_imag = factored(real_part, imag_part, 2, -1.0, True)
    rows = depth_real.shape[0]
    stacked = jnp.concatenate([depth_real, depth_imag], 0)
    moved = lax.all_to_all(stacked, "slab", split_axis=2, concat_axis=1, tiled=True)
    return factored(moved[:rows], moved[rows:], 1, -1.0, True)


def to_planes(real_part, imag_part):
    width_real, width_imag = factored(real_part, imag_part, 1, 1.0, False)
    rows = width_real.shape[0]
    stacked = jnp.concatenate([width_real, width_imag], 0)
    moved = lax.all_to_all(stacked, "slab", split_axis=1, concat_axis=2, tiled=True)
    return factored(moved[:rows], moved[rows:], 2, 1.0, False)


def pack_pairs(volume):
    return (volume[0::2], volume[1::2])


def unpack_pairs(real_part, imag_part):
    pairs, width, depth = real_part.shape
    return jnp.stack([real_part, imag_part], 1).reshape(2 * pairs, width, depth)


def general_shards(estimate, views, psf, pattern_mult, pattern_shift, interp):
    row_count, slab_width, depth = estimate.shape
    blocks = block_matrix(pattern_mult[0], pattern_shift[0], interp[0])
    block_count = depth // 128
    shaped = estimate.reshape(row_count, slab_width, block_count, 128)
    sampled = jnp.einsum("bij,yxbj->yxbi", blocks, shaped, precision=highest).reshape(
        row_count, slab_width, depth
    )
    packed_real, packed_imag = pack_pairs(sampled)
    packed_real = jnp.concatenate([packed_real, psf], 0)
    packed_imag = jnp.concatenate([packed_imag, jnp.zeros_like(psf)], 0)
    spectra_real, spectra_imag = to_columns(packed_real, packed_imag)
    scaling = 1.0 / (spectra_real.shape[1] * depth)
    transfer_real = spectra_real[-1:] * scaling
    transfer_imag = spectra_imag[-1:] * scaling
    spectra_real = spectra_real[:-1]
    spectra_imag = spectra_imag[:-1]
    filtered_real = spectra_real * transfer_real - spectra_imag * transfer_imag
    filtered_imag = spectra_real * transfer_imag + spectra_imag * transfer_real
    blurred = unpack_pairs(*to_planes(filtered_real, filtered_imag))
    quotient = views[0] / blurred
    packed_real, packed_imag = pack_pairs(quotient)
    spectra_real, spectra_imag = to_columns(packed_real, packed_imag)
    filtered_real = spectra_real * transfer_real + spectra_imag * transfer_imag
    filtered_imag = spectra_imag * transfer_real - spectra_real * transfer_imag
    smeared = unpack_pairs(*to_planes(filtered_real, filtered_imag))
    correction = jnp.einsum(
        "bij,yxbi->yxbj",
        blocks,
        smeared.reshape(row_count, slab_width, block_count, 128),
        precision=highest,
    ).reshape(row_count, slab_width, depth)
    log_terms = jnp.log(correction)
    view_count = lax.axis_size("view")
    summed = lax.psum(log_terms, "view")
    return estimate * jnp.exp(summed / view_count)


def swap_halves(joined):
    half = joined.shape[-1] // 2
    return jnp.concatenate([-joined[..., half:], joined[..., :half]], -1)


def lead_stage(joined, direction):
    count = joined.shape[0]
    parts = [joined[index] for index in range(count)]
    turned = [swap_halves(part) for part in parts]
    outs = []
    for out_index in range(count):
        total = None
        for in_index in range(count):
            cosine, sine = unit_root(in_index * out_index, count)
            sine = direction * sine
            for weight, term in ((cosine, parts[in_index]), (sine, turned[in_index])):
                if weight != 0.0:
                    term = weight * term
                    total = term if total is None else total + term
        outs.append(total)
    return jnp.stack(outs, 0)


def joined_twist(joined, length, direction, lanes):
    first, second = joined.shape[0], (joined.shape[-1] // 2 if lanes else joined.shape[2])
    cosine, sine = angle_tables(first, second, length)
    sine = direction * sine
    if lanes:
        cosine = jnp.concatenate([cosine, cosine], 1)[:, None, None, :]
        sine = jnp.concatenate([sine, sine], 1)[:, None, None, :]
    else:
        cosine = cosine[:, None, :, None]
        sine = sine[:, None, :, None]
    return joined * cosine + swap_halves(joined) * sine


def lane_stage(joined, direction):
    length = joined.shape[-1] // 2
    matrix = block_dft_matrix(length, direction)
    return jnp.einsum("...j,jn->...n", joined, matrix, precision=highest)


def row_stage(joined, direction):
    length = joined.shape[2]
    cosine, sine = angle_tables(length, length, length)
    matrix = jnp.concatenate([cosine, direction * sine], 0)
    both = jnp.concatenate([joined, swap_halves(joined)], 2)
    return jnp.einsum("krjl,jm->krml", both, matrix, precision=highest)


def depth_forward(joined, depth):
    joined = lead_stage(joined, -1.0)
    joined = joined_twist(joined, depth, -1.0, True)
    return lane_stage(joined, -1.0)


def depth_inverse(joined, depth):
    joined = lane_stage(joined, 1.0)
    joined = joined_twist(joined, depth, 1.0, True)
    return lead_stage(joined, 1.0)


def width_forward(joined, width):
    joined = lead_stage(joined, -1.0)
    joined = joined_twist(joined, width, -1.0, False)
    return row_stage(joined, -1.0)


def width_inverse(joined, width):
    joined = row_stage(joined, 1.0)
    joined = joined_twist(joined, width, 1.0, False)
    return lead_stage(joined, 1.0)


def joined_times(joined, transfer_real, transfer_imag):
    return joined * transfer_real + swap_halves(joined) * transfer_imag


def to_blocks(volume, block_count):
    rows, width, depth = volume.shape
    lanes = depth // block_count
    shaped = volume.reshape(rows // 2, 2, width, block_count, lanes)
    return shaped.transpose(3, 0, 2, 1, 4).reshape(block_count, rows // 2, width, 2 * lanes)


def from_blocks(blocked):
    block_count, pairs, width, lanes = blocked.shape
    shaped = blocked.reshape(block_count, pairs, width, 2, lanes // 2)
    return shaped.transpose(1, 3, 2, 0, 4).reshape(2 * pairs, width, block_count * lanes // 2)


def shards(estimate, views, psf, pattern_mult, pattern_shift, interp):
    row_count, slab_width, depth = estimate.shape
    slab_count = lax.axis_size("slab")
    block_count = depth // 128
    width = slab_width * slab_count
    if not (
        block_count == slab_count
        and slab_width == 128
        and width // 128 == slab_count
        and row_count % 2 == 0
    ):
        return general_shards(estimate, views, psf, pattern_mult, pattern_shift, interp)
    blocks = block_matrix(pattern_mult[0], pattern_shift[0], interp[0])
    empty = jnp.zeros_like(blocks)
    doubled = jnp.concatenate(
        [jnp.concatenate([blocks, empty], 2), jnp.concatenate([empty, blocks], 2)], 1
    )
    sampled = jnp.einsum(
        "apxl,aml->apxm", to_blocks(estimate, block_count), doubled, precision=highest
    )
    pairs = row_count // 2
    spread = psf.reshape(slab_width, block_count, 128).transpose(1, 0, 2)[:, None]
    spread = jnp.concatenate([spread, jnp.zeros_like(spread)], -1)
    packed = jnp.concatenate([sampled, spread], 1)
    spectra = depth_forward(packed, depth)
    spectra = lax.all_to_all(spectra, "slab", split_axis=0, concat_axis=0, tiled=True)
    scaling = 1.0 / (width * depth)
    transfer = width_forward(spectra[:, pairs:], width) * scaling
    spectra = width_forward(spectra[:, :pairs], width)
    half = transfer.shape[-1] // 2
    transfer_real = jnp.concatenate([transfer[..., :half], transfer[..., :half]], -1)
    transfer_imag = jnp.concatenate([transfer[..., half:], transfer[..., half:]], -1)

    def convolve(spectra, transfer_imag):
        filtered = joined_times(spectra, transfer_real, transfer_imag)
        planes = width_inverse(filtered, width)
        planes = lax.all_to_all(planes, "slab", split_axis=0, concat_axis=0, tiled=True)
        return depth_inverse(planes, depth)

    blurred = convolve(spectra, transfer_imag)
    quotient = to_blocks(views[0], block_count) / blurred
    spectra = depth_forward(quotient, depth)
    spectra = lax.all_to_all(spectra, "slab", split_axis=0, concat_axis=0, tiled=True)
    spectra = width_forward(spectra, width)
    smeared = convolve(spectra, -transfer_imag)
    correction = jnp.einsum("apxm,aml->apxl", smeared, doubled, precision=highest)
    log_terms = from_blocks(jnp.log(correction))
    view_count = lax.axis_size("view")
    summed = lax.psum(log_terms, "view")
    return estimate * jnp.exp(summed / view_count)


def solution(mesh):
    placed = (
        P(None, "slab", None),
        P("view", None, "slab", None),
        P("view", "slab", None),
        P("view", None),
        P("view", None),
        P("view", None, None),
    )
    return jax.shard_map(
        shards, mesh=mesh, in_specs=placed, out_specs=P(None, "slab", None), check_vma=False
    )
```

```python
import functools
import math

import jax
import jax.numpy as jnp
from jax import lax
from jax.experimental import pallas as pl
from jax.sharding import PartitionSpec as P

highest = lax.Precision.HIGHEST


def block_matrix(multiplier, shifting, weights):
    positions = jnp.arange(128, dtype=jnp.int32)
    first_col = ((2 * multiplier[:, None] + 1) * positions[None, :] + shifting[:, None]) % 128
    second_col = (first_col + 1) % 128
    columns = positions[None, None, :]
    lower = (columns == first_col[:, :, None]).astype(jnp.float32)
    upper = (columns == second_col[:, :, None]).astype(jnp.float32)
    return (1.0 - weights)[:, :, None] * lower + weights[:, :, None] * upper


def angle_tables(rows, cols, length):
    row_index = lax.iota(jnp.int32, rows)[:, None]
    col_index = lax.iota(jnp.int32, cols)[None, :]
    angles = (row_index * col_index % length).astype(jnp.float32) * (2.0 * math.pi / length)
    return (jnp.cos(angles), jnp.sin(angles))


def unit_root(numerator, length):
    angle = 2.0 * math.pi * numerator / length
    return (round(math.cos(angle), 15), round(math.sin(angle), 15))


def small_stage(real_part, imag_part, axis, direction):
    count = real_part.shape[axis]

    def part(array, index):
        return lax.index_in_dim(array, index, axis, keepdims=False)

    real_in = [part(real_part, index) for index in range(count)]
    imag_in = None if imag_part is None else [part(imag_part, index) for index in range(count)]
    real_out, imag_out = [], []
    for out_index in range(count):
        real_sum, imag_sum = None, None
        for in_index in range(count):
            cosine, sine = unit_root(in_index * out_index, count)
            sine = direction * sine
            terms_real = []
            terms_imag = []
            if cosine != 0.0:
                terms_real.append(cosine * real_in[in_index])
                if imag_in is not None:
                    terms_imag.append(cosine * imag_in[in_index])
            if sine != 0.0:
                terms_imag.append(sine * real_in[in_index])
                if imag_in is not None:
                    terms_real.append(-sine * imag_in[in_index])
            for term in terms_real:
                real_sum = term if real_sum is None else real_sum + term
            for term in terms_imag:
                imag_sum = term if imag_sum is None else imag_sum + term
        if imag_sum is None:
            imag_sum = jnp.zeros_like(real_sum)
        real_out.append(real_sum)
        imag_out.append(imag_sum)
    return (jnp.stack(real_out, axis), jnp.stack(imag_out, axis))


def complex_times(real_part, imag_part, cosine, sine_table):
    return (
        real_part * cosine - imag_part * sine_table,
        real_part * sine_table + imag_part * cosine,
    )


def block_dft_matrix(length, direction):
    cosine, sine = angle_tables(length, length, length)
    sine = direction * sine
    top = jnp.concatenate([cosine, sine], 1)
    bottom = jnp.concatenate([-sine, cosine], 1)
    return jnp.concatenate([top, bottom], 0)


def large_stage(real_part, imag_part, axis, direction):
    length = real_part.shape[axis]
    if imag_part is None:
        imag_part = jnp.zeros_like(real_part)
    joined = jnp.concatenate([real_part, imag_part], axis)
    matrix = block_dft_matrix(length, direction)
    if axis == joined.ndim - 1:
        out = jnp.einsum("...j,jn->...n", joined, matrix, precision=highest)
    else:
        out = jnp.einsum("rkjz,jn->rknz", joined, matrix, precision=highest)
    return (
        lax.slice_in_dim(out, 0, length, axis=axis),
        lax.slice_in_dim(out, length, 2 * length, axis=axis),
    )


def factored(real_part, imag_part, axis, direction, forward, want_imag=True):
    length = real_part.shape[axis]
    second = 128
    first = length // second
    outer = real_part.shape
    shape = outer[:axis] + (first, second) + outer[axis + 1 :]
    real_part = real_part.reshape(shape)
    if imag_part is not None:
        imag_part = imag_part.reshape(shape)
    twist_cos, twist_sin = angle_tables(first, second, length)
    if axis == 1:
        twist_cos = twist_cos[:, :, None]
        twist_sin = twist_sin[:, :, None]
    twist_sin = direction * twist_sin
    if forward:
        real_part, imag_part = small_stage(real_part, imag_part, axis, direction)
        real_part, imag_part = complex_times(real_part, imag_part, twist_cos, twist_sin)
        real_part, imag_part = large_stage(real_part, imag_part, axis + 1, direction)
    else:
        real_part, imag_part = large_stage(real_part, imag_part, axis + 1, direction)
        real_part, imag_part = complex_times(real_part, imag_part, twist_cos, twist_sin)
        real_part, imag_part = small_stage(real_part, imag_part, axis, direction)
    return (real_part.reshape(outer), imag_part.reshape(outer))


def to_columns(real_part, imag_part):
    depth_real, depth_imag = factored(real_part, imag_part, 2, -1.0, True)
    rows = depth_real.shape[0]
    stacked = jnp.concatenate([depth_real, depth_imag], 0)
    moved = lax.all_to_all(stacked, "slab", split_axis=2, concat_axis=1, tiled=True)
    return factored(moved[:rows], moved[rows:], 1, -1.0, True)


def to_planes(real_part, imag_part):
    width_real, width_imag = factored(real_part, imag_part, 1, 1.0, False)
    rows = width_real.shape[0]
    stacked = jnp.concatenate([width_real, width_imag], 0)
    moved = lax.all_to_all(stacked, "slab", split_axis=1, concat_axis=2, tiled=True)
    return factored(moved[:rows], moved[rows:], 2, 1.0, False)


def pack_pairs(volume):
    return (volume[0::2], volume[1::2])


def unpack_pairs(real_part, imag_part):
    pairs, width, depth = real_part.shape
    return jnp.stack([real_part, imag_part], 1).reshape(2 * pairs, width, depth)


def general_shards(estimate, views, psf, pattern_mult, pattern_shift, interp):
    row_count, slab_width, depth = estimate.shape
    blocks = block_matrix(pattern_mult[0], pattern_shift[0], interp[0])
    block_count = depth // 128
    shaped = estimate.reshape(row_count, slab_width, block_count, 128)
    sampled = jnp.einsum("bij,yxbj->yxbi", blocks, shaped, precision=highest).reshape(
        row_count, slab_width, depth
    )
    packed_real, packed_imag = pack_pairs(sampled)
    packed_real = jnp.concatenate([packed_real, psf], 0)
    packed_imag = jnp.concatenate([packed_imag, jnp.zeros_like(psf)], 0)
    spectra_real, spectra_imag = to_columns(packed_real, packed_imag)
    scaling = 1.0 / (spectra_real.shape[1] * depth)
    transfer_real = spectra_real[-1:] * scaling
    transfer_imag = spectra_imag[-1:] * scaling
    spectra_real = spectra_real[:-1]
    spectra_imag = spectra_imag[:-1]
    filtered_real = spectra_real * transfer_real - spectra_imag * transfer_imag
    filtered_imag = spectra_real * transfer_imag + spectra_imag * transfer_real
    blurred = unpack_pairs(*to_planes(filtered_real, filtered_imag))
    quotient = views[0] / blurred
    packed_real, packed_imag = pack_pairs(quotient)
    spectra_real, spectra_imag = to_columns(packed_real, packed_imag)
    filtered_real = spectra_real * transfer_real + spectra_imag * transfer_imag
    filtered_imag = spectra_imag * transfer_real - spectra_real * transfer_imag
    smeared = unpack_pairs(*to_planes(filtered_real, filtered_imag))
    correction = jnp.einsum(
        "bij,yxbi->yxbj",
        blocks,
        smeared.reshape(row_count, slab_width, block_count, 128),
        precision=highest,
    ).reshape(row_count, slab_width, depth)
    log_terms = jnp.log(correction)
    view_count = lax.axis_size("view")
    summed = lax.psum(log_terms, "view")
    return estimate * jnp.exp(summed / view_count)


def swap_halves(joined):
    half = joined.shape[-1] // 2
    return jnp.concatenate([-joined[..., half:], joined[..., :half]], -1)


def lead_stage(joined, direction):
    count = joined.shape[0]
    parts = [joined[index] for index in range(count)]
    turned = [swap_halves(part) for part in parts]
    outs = []
    for out_index in range(count):
        total = None
        for in_index in range(count):
            cosine, sine = unit_root(in_index * out_index, count)
            sine = direction * sine
            for weight, term in ((cosine, parts[in_index]), (sine, turned[in_index])):
                if weight != 0.0:
                    term = weight * term
                    total = term if total is None else total + term
        outs.append(total)
    return jnp.stack(outs, 0)


def joined_twist(joined, length, direction, lanes):
    first, second = joined.shape[0], (joined.shape[-1] // 2 if lanes else joined.shape[2])
    cosine, sine = angle_tables(first, second, length)
    sine = direction * sine
    if lanes:
        cosine = jnp.concatenate([cosine, cosine], 1)[:, None, None, :]
        sine = jnp.concatenate([sine, sine], 1)[:, None, None, :]
    else:
        cosine = cosine[:, None, :, None]
        sine = sine[:, None, :, None]
    return joined * cosine + swap_halves(joined) * sine


def lane_stage(joined, direction):
    length = joined.shape[-1] // 2
    matrix = block_dft_matrix(length, direction)
    return jnp.einsum("...j,jn->...n", joined, matrix, precision=highest)


def row_stage(joined, direction):
    length = joined.shape[2]
    cosine, sine = angle_tables(length, length, length)
    matrix = jnp.concatenate([cosine, direction * sine], 0)
    both = jnp.concatenate([joined, swap_halves(joined)], 2)
    return jnp.einsum("krjl,jm->krml", both, matrix, precision=highest)


def lead_kernel(direction, forward, joined_ref, cosine_ref, sine_ref, out_ref):
    count = joined_ref.shape[0]
    half = joined_ref.shape[-1] // 2

    def turn(value):
        return jnp.concatenate([-value[:, half:], value[:, :half]], -1)

    def twist(value, index):
        return value * cosine_ref[index] + turn(value) * sine_ref[index]

    parts = [joined_ref[index] for index in range(count)]
    if not forward:
        parts = [twist(part, index) for index, part in enumerate(parts)]
    turned = [turn(part) for part in parts]
    for out_index in range(count):
        total = None
        for in_index in range(count):
            cosine, sine = unit_root(in_index * out_index, count)
            sine = direction * sine
            for weight, term in ((cosine, parts[in_index]), (sine, turned[in_index])):
                if weight != 0.0:
                    term = weight * term
                    total = term if total is None else total + term
        if forward:
            total = twist(total, out_index)
        out_ref[out_index] = total


def lead_pass(joined, length, direction, forward, lanes):
    shape = joined.shape
    count, lane_count = shape[0], shape[-1]
    flat = joined.reshape(count, -1, lane_count)
    rows = flat.shape[1]
    tile = 64
    if lanes:
        cosine, sine = angle_tables(count, lane_count // 2, length)
        cosine = jnp.concatenate([cosine, cosine], 1)[:, None, :]
        sine = jnp.concatenate([sine, sine], 1)[:, None, :]
        table_block = (count, 1, lane_count)
        table_map = lambda step: (0, 0, 0)
    else:
        second = shape[2]
        cosine, sine = angle_tables(count, second, length)
        cosine = cosine[:, :, None]
        sine = sine[:, :, None]
        table_block = (count, tile, 1)
        per_block = second // tile
        table_map = lambda step: (0, step % per_block, 0)
    sine = direction * sine
    data_block = (count, tile, lane_count)
    out = pl.pallas_call(
        functools.partial(lead_kernel, direction, forward),
        out_shape=jax.ShapeDtypeStruct(flat.shape, flat.dtype),
        grid=(rows // tile,),
        in_specs=[
            pl.BlockSpec(data_block, lambda step: (0, step, 0)),
            pl.BlockSpec(table_block, table_map),
            pl.BlockSpec(table_block, table_map),
        ],
        out_specs=pl.BlockSpec(data_block, lambda step: (0, step, 0)),
        cost_estimate=pl.CostEstimate(
            flops=int(flat.size) * 4 * count, transcendentals=0, bytes_accessed=int(flat.size) * 8
        ),
    )(flat, cosine, sine)
    return out.reshape(shape)


def depth_forward(joined, depth):
    joined = lead_pass(joined, depth, -1.0, True, True)
    return lane_stage(joined, -1.0)


def depth_inverse(joined, depth):
    joined = lane_stage(joined, 1.0)
    return lead_pass(joined, depth, 1.0, False, True)


def width_forward(joined, width):
    joined = lead_pass(joined, width, -1.0, True, False)
    return row_stage(joined, -1.0)


def width_inverse(joined, width):
    joined = row_stage(joined, 1.0)
    return lead_pass(joined, width, 1.0, False, False)


def joined_times(joined, transfer_real, transfer_imag):
    return joined * transfer_real + swap_halves(joined) * transfer_imag


def to_blocks(volume, block_count):
    rows, width, depth = volume.shape
    lanes = depth // block_count
    shaped = volume.reshape(rows // 2, 2, width, block_count, lanes)
    return shaped.transpose(3, 0, 2, 1, 4).reshape(block_count, rows // 2, width, 2 * lanes)


def from_blocks(blocked):
    block_count, pairs, width, lanes = blocked.shape
    shaped = blocked.reshape(block_count, pairs, width, 2, lanes // 2)
    return shaped.transpose(1, 3, 2, 0, 4).reshape(2 * pairs, width, block_count * lanes // 2)


def shards(estimate, views, psf, pattern_mult, pattern_shift, interp):
    row_count, slab_width, depth = estimate.shape
    slab_count = lax.axis_size("slab")
    block_count = depth // 128
    width = slab_width * slab_count
    if not (
        block_count == slab_count
        and slab_width == 128
        and width // 128 == slab_count
        and row_count % 2 == 0
    ):
        return general_shards(estimate, views, psf, pattern_mult, pattern_shift, interp)
    blocks = block_matrix(pattern_mult[0], pattern_shift[0], interp[0])
    empty = jnp.zeros_like(blocks)
    doubled = jnp.concatenate(
        [jnp.concatenate([blocks, empty], 2), jnp.concatenate([empty, blocks], 2)], 1
    )
    sampled = jnp.einsum(
        "apxl,aml->apxm", to_blocks(estimate, block_count), doubled, precision=highest
    )
    pairs = row_count // 2
    spread = psf.reshape(slab_width, block_count, 128).transpose(1, 0, 2)[:, None]
    spread = jnp.concatenate([spread, jnp.zeros_like(spread)], -1)
    packed = jnp.concatenate([sampled, spread], 1)
    spectra = depth_forward(packed, depth)
    spectra = lax.all_to_all(spectra, "slab", split_axis=0, concat_axis=0, tiled=True)
    scaling = 1.0 / (width * depth)
    transfer = width_forward(spectra[:, pairs:], width) * scaling
    spectra = width_forward(spectra[:, :pairs], width)
    half = transfer.shape[-1] // 2
    transfer_real = jnp.concatenate([transfer[..., :half], transfer[..., :half]], -1)
    transfer_imag = jnp.concatenate([transfer[..., half:], transfer[..., half:]], -1)

    def convolve(spectra, transfer_imag):
        filtered = joined_times(spectra, transfer_real, transfer_imag)
        planes = width_inverse(filtered, width)
        planes = lax.all_to_all(planes, "slab", split_axis=0, concat_axis=0, tiled=True)
        return depth_inverse(planes, depth)

    blurred = convolve(spectra, transfer_imag)
    quotient = to_blocks(views[0], block_count) / blurred
    spectra = depth_forward(quotient, depth)
    spectra = lax.all_to_all(spectra, "slab", split_axis=0, concat_axis=0, tiled=True)
    spectra = width_forward(spectra, width)
    smeared = convolve(spectra, -transfer_imag)
    correction = jnp.einsum("apxm,aml->apxl", smeared, doubled, precision=highest)
    log_terms = from_blocks(jnp.log(correction))
    view_count = lax.axis_size("view")
    summed = lax.psum(log_terms, "view")
    return estimate * jnp.exp(summed / view_count)


def solution(mesh):
    placed = (
        P(None, "slab", None),
        P("view", None, "slab", None),
        P("view", "slab", None),
        P("view", None),
        P("view", None),
        P("view", None, None),
    )
    return jax.shard_map(
        shards, mesh=mesh, in_specs=placed, out_specs=P(None, "slab", None), check_vma=False
    )
```

```python
import functools
import math

import jax
import numpy as np
import jax.numpy as jnp
from jax import lax
from jax.experimental import pallas as pl
from jax.sharding import PartitionSpec as P

highest = lax.Precision.HIGHEST


def block_matrix(multiplier, shifting, weights):
    positions = jnp.arange(128, dtype=jnp.int32)
    first_col = ((2 * multiplier[:, None] + 1) * positions[None, :] + shifting[:, None]) % 128
    second_col = (first_col + 1) % 128
    columns = positions[None, None, :]
    lower = (columns == first_col[:, :, None]).astype(jnp.float32)
    upper = (columns == second_col[:, :, None]).astype(jnp.float32)
    return (1.0 - weights)[:, :, None] * lower + weights[:, :, None] * upper


def angle_tables(rows, cols, length):
    row_index = lax.iota(jnp.int32, rows)[:, None]
    col_index = lax.iota(jnp.int32, cols)[None, :]
    angles = (row_index * col_index % length).astype(jnp.float32) * (2.0 * math.pi / length)
    return (jnp.cos(angles), jnp.sin(angles))


def unit_root(numerator, length):
    angle = 2.0 * math.pi * numerator / length
    return (round(math.cos(angle), 15), round(math.sin(angle), 15))


def small_stage(real_part, imag_part, axis, direction):
    count = real_part.shape[axis]

    def part(array, index):
        return lax.index_in_dim(array, index, axis, keepdims=False)

    real_in = [part(real_part, index) for index in range(count)]
    imag_in = None if imag_part is None else [part(imag_part, index) for index in range(count)]
    real_out, imag_out = [], []
    for out_index in range(count):
        real_sum, imag_sum = None, None
        for in_index in range(count):
            cosine, sine = unit_root(in_index * out_index, count)
            sine = direction * sine
            terms_real = []
            terms_imag = []
            if cosine != 0.0:
                terms_real.append(cosine * real_in[in_index])
                if imag_in is not None:
                    terms_imag.append(cosine * imag_in[in_index])
            if sine != 0.0:
                terms_imag.append(sine * real_in[in_index])
                if imag_in is not None:
                    terms_real.append(-sine * imag_in[in_index])
            for term in terms_real:
                real_sum = term if real_sum is None else real_sum + term
            for term in terms_imag:
                imag_sum = term if imag_sum is None else imag_sum + term
        if imag_sum is None:
            imag_sum = jnp.zeros_like(real_sum)
        real_out.append(real_sum)
        imag_out.append(imag_sum)
    return (jnp.stack(real_out, axis), jnp.stack(imag_out, axis))


def complex_times(real_part, imag_part, cosine, sine_table):
    return (
        real_part * cosine - imag_part * sine_table,
        real_part * sine_table + imag_part * cosine,
    )


def block_dft_matrix(length, direction):
    cosine, sine = angle_tables(length, length, length)
    sine = direction * sine
    top = jnp.concatenate([cosine, sine], 1)
    bottom = jnp.concatenate([-sine, cosine], 1)
    return jnp.concatenate([top, bottom], 0)


def large_stage(real_part, imag_part, axis, direction):
    length = real_part.shape[axis]
    if imag_part is None:
        imag_part = jnp.zeros_like(real_part)
    joined = jnp.concatenate([real_part, imag_part], axis)
    matrix = block_dft_matrix(length, direction)
    if axis == joined.ndim - 1:
        out = jnp.einsum("...j,jn->...n", joined, matrix, precision=highest)
    else:
        out = jnp.einsum("rkjz,jn->rknz", joined, matrix, precision=highest)
    return (
        lax.slice_in_dim(out, 0, length, axis=axis),
        lax.slice_in_dim(out, length, 2 * length, axis=axis),
    )


def factored(real_part, imag_part, axis, direction, forward, want_imag=True):
    length = real_part.shape[axis]
    second = 128
    first = length // second
    outer = real_part.shape
    shape = outer[:axis] + (first, second) + outer[axis + 1 :]
    real_part = real_part.reshape(shape)
    if imag_part is not None:
        imag_part = imag_part.reshape(shape)
    twist_cos, twist_sin = angle_tables(first, second, length)
    if axis == 1:
        twist_cos = twist_cos[:, :, None]
        twist_sin = twist_sin[:, :, None]
    twist_sin = direction * twist_sin
    if forward:
        real_part, imag_part = small_stage(real_part, imag_part, axis, direction)
        real_part, imag_part = complex_times(real_part, imag_part, twist_cos, twist_sin)
        real_part, imag_part = large_stage(real_part, imag_part, axis + 1, direction)
    else:
        real_part, imag_part = large_stage(real_part, imag_part, axis + 1, direction)
        real_part, imag_part = complex_times(real_part, imag_part, twist_cos, twist_sin)
        real_part, imag_part = small_stage(real_part, imag_part, axis, direction)
    return (real_part.reshape(outer), imag_part.reshape(outer))


def to_columns(real_part, imag_part):
    depth_real, depth_imag = factored(real_part, imag_part, 2, -1.0, True)
    rows = depth_real.shape[0]
    stacked = jnp.concatenate([depth_real, depth_imag], 0)
    moved = lax.all_to_all(stacked, "slab", split_axis=2, concat_axis=1, tiled=True)
    return factored(moved[:rows], moved[rows:], 1, -1.0, True)


def to_planes(real_part, imag_part):
    width_real, width_imag = factored(real_part, imag_part, 1, 1.0, False)
    rows = width_real.shape[0]
    stacked = jnp.concatenate([width_real, width_imag], 0)
    moved = lax.all_to_all(stacked, "slab", split_axis=1, concat_axis=2, tiled=True)
    return factored(moved[:rows], moved[rows:], 2, 1.0, False)


def pack_pairs(volume):
    return (volume[0::2], volume[1::2])


def unpack_pairs(real_part, imag_part):
    pairs, width, depth = real_part.shape
    return jnp.stack([real_part, imag_part], 1).reshape(2 * pairs, width, depth)


def general_shards(estimate, views, psf, pattern_mult, pattern_shift, interp):
    row_count, slab_width, depth = estimate.shape
    blocks = block_matrix(pattern_mult[0], pattern_shift[0], interp[0])
    block_count = depth // 128
    shaped = estimate.reshape(row_count, slab_width, block_count, 128)
    sampled = jnp.einsum("bij,yxbj->yxbi", blocks, shaped, precision=highest).reshape(
        row_count, slab_width, depth
    )
    packed_real, packed_imag = pack_pairs(sampled)
    packed_real = jnp.concatenate([packed_real, psf], 0)
    packed_imag = jnp.concatenate([packed_imag, jnp.zeros_like(psf)], 0)
    spectra_real, spectra_imag = to_columns(packed_real, packed_imag)
    scaling = 1.0 / (spectra_real.shape[1] * depth)
    transfer_real = spectra_real[-1:] * scaling
    transfer_imag = spectra_imag[-1:] * scaling
    spectra_real = spectra_real[:-1]
    spectra_imag = spectra_imag[:-1]
    filtered_real = spectra_real * transfer_real - spectra_imag * transfer_imag
    filtered_imag = spectra_real * transfer_imag + spectra_imag * transfer_real
    blurred = unpack_pairs(*to_planes(filtered_real, filtered_imag))
    quotient = views[0] / blurred
    packed_real, packed_imag = pack_pairs(quotient)
    spectra_real, spectra_imag = to_columns(packed_real, packed_imag)
    filtered_real = spectra_real * transfer_real + spectra_imag * transfer_imag
    filtered_imag = spectra_imag * transfer_real - spectra_real * transfer_imag
    smeared = unpack_pairs(*to_planes(filtered_real, filtered_imag))
    correction = jnp.einsum(
        "bij,yxbi->yxbj",
        blocks,
        smeared.reshape(row_count, slab_width, block_count, 128),
        precision=highest,
    ).reshape(row_count, slab_width, depth)
    log_terms = jnp.log(correction)
    view_count = lax.axis_size("view")
    summed = lax.psum(log_terms, "view")
    return estimate * jnp.exp(summed / view_count)


def swap_halves(joined):
    half = joined.shape[-1] // 2
    return jnp.concatenate([-joined[..., half:], joined[..., :half]], -1)


def lead_stage(joined, direction):
    count = joined.shape[0]
    parts = [joined[index] for index in range(count)]
    turned = [swap_halves(part) for part in parts]
    outs = []
    for out_index in range(count):
        total = None
        for in_index in range(count):
            cosine, sine = unit_root(in_index * out_index, count)
            sine = direction * sine
            for weight, term in ((cosine, parts[in_index]), (sine, turned[in_index])):
                if weight != 0.0:
                    term = weight * term
                    total = term if total is None else total + term
        outs.append(total)
    return jnp.stack(outs, 0)


def joined_twist(joined, length, direction, lanes):
    first, second = joined.shape[0], (joined.shape[-1] // 2 if lanes else joined.shape[2])
    cosine, sine = angle_tables(first, second, length)
    sine = direction * sine
    if lanes:
        cosine = jnp.concatenate([cosine, cosine], 1)[:, None, None, :]
        sine = jnp.concatenate([sine, sine], 1)[:, None, None, :]
    else:
        cosine = cosine[:, None, :, None]
        sine = sine[:, None, :, None]
    return joined * cosine + swap_halves(joined) * sine


def lane_stage(joined, direction):
    length = joined.shape[-1] // 2
    matrix = block_dft_matrix(length, direction)
    return jnp.einsum("...j,jn->...n", joined, matrix, precision=highest)


def row_stage(joined, direction):
    length = joined.shape[2]
    cosine, sine = angle_tables(length, length, length)
    matrix = jnp.concatenate([cosine, direction * sine], 0)
    both = jnp.concatenate([joined, swap_halves(joined)], 2)
    return jnp.einsum("krjl,jm->krml", both, matrix, precision=highest)


def butterflies(parts, direction, turn):
    count = len(parts)
    if count == 1:
        return parts
    even = butterflies(parts[0::2], direction, turn)
    odd = butterflies(parts[1::2], direction, turn)
    out = [None] * count
    for index in range(count // 2):
        cosine, sine = unit_root(index, count)
        sine = direction * sine
        value = odd[index]
        if sine == 0.0:
            rotated = value if cosine > 0 else -value
        elif cosine == 0.0:
            rotated = turn(value) if sine > 0 else -turn(value)
        else:
            rotated = cosine * value + sine * turn(value)
        out[index] = even[index] + rotated
        out[index + count // 2] = even[index] - rotated
    return out


def lead_kernel(direction, forward, joined_ref, cosine_ref, sine_ref, out_ref):
    count = joined_ref.shape[0]
    half = joined_ref.shape[-1] // 2

    def turn(value):
        return jnp.concatenate([-value[:, half:], value[:, :half]], -1)

    def twist(value, index):
        return value * cosine_ref[index] + turn(value) * sine_ref[index]

    parts = [joined_ref[index] for index in range(count)]
    if not forward:
        parts = [twist(part, index) for index, part in enumerate(parts)]
    outs = butterflies(parts, direction, turn)
    for index, total in enumerate(outs):
        if forward:
            total = twist(total, index)
        out_ref[index] = total


def fixed_tables(rows, cols, length, direction):
    product = np.outer(np.arange(rows), np.arange(cols)) % length
    angles = product * (2.0 * np.pi / length)
    return (np.cos(angles).astype(np.float32), (direction * np.sin(angles)).astype(np.float32))


def lead_pass(joined, length, direction, forward, lanes):
    shape = joined.shape
    count, lane_count = shape[0], shape[-1]
    flat = joined.reshape(count, -1, lane_count)
    rows = flat.shape[1]
    tile = 64
    if lanes:
        cosine, sine = fixed_tables(count, lane_count // 2, length, direction)
        cosine = np.concatenate([cosine, cosine], 1)[:, None, :]
        sine = np.concatenate([sine, sine], 1)[:, None, :]
        table_block = (count, 1, lane_count)
        table_map = lambda step: (0, 0, 0)
    else:
        second = shape[2]
        cosine, sine = fixed_tables(count, second, length, direction)
        cosine = cosine[:, :, None]
        sine = sine[:, :, None]
        table_block = (count, tile, 1)
        per_block = second // tile
        table_map = lambda step: (0, step % per_block, 0)
    data_block = (count, tile, lane_count)
    out = pl.pallas_call(
        functools.partial(lead_kernel, direction, forward),
        out_shape=jax.ShapeDtypeStruct(flat.shape, flat.dtype),
        grid=(rows // tile,),
        in_specs=[
            pl.BlockSpec(data_block, lambda step: (0, step, 0)),
            pl.BlockSpec(table_block, table_map),
            pl.BlockSpec(table_block, table_map),
        ],
        out_specs=pl.BlockSpec(data_block, lambda step: (0, step, 0)),
        cost_estimate=pl.CostEstimate(
            flops=int(flat.size) * 4 * count, transcendentals=0, bytes_accessed=int(flat.size) * 8
        ),
    )(flat, cosine, sine)
    return out.reshape(shape)


def depth_forward(joined, depth):
    joined = lead_pass(joined, depth, -1.0, True, True)
    return lane_stage(joined, -1.0)


def depth_inverse(joined, depth):
    joined = lane_stage(joined, 1.0)
    return lead_pass(joined, depth, 1.0, False, True)


def width_forward(joined, width):
    joined = lead_pass(joined, width, -1.0, True, False)
    return row_stage(joined, -1.0)


def width_inverse(joined, width):
    joined = row_stage(joined, 1.0)
    return lead_pass(joined, width, 1.0, False, False)


def joined_times(joined, transfer_real, transfer_imag):
    return joined * transfer_real + swap_halves(joined) * transfer_imag


def to_blocks(volume, block_count):
    rows, width, depth = volume.shape
    lanes = depth // block_count
    shaped = volume.reshape(rows // 2, 2, width, block_count, lanes)
    return shaped.transpose(3, 0, 2, 1, 4).reshape(block_count, rows // 2, width, 2 * lanes)


def from_blocks(blocked):
    block_count, pairs, width, lanes = blocked.shape
    shaped = blocked.reshape(block_count, pairs, width, 2, lanes // 2)
    return shaped.transpose(1, 3, 2, 0, 4).reshape(2 * pairs, width, block_count * lanes // 2)


def shards(estimate, views, psf, pattern_mult, pattern_shift, interp):
    row_count, slab_width, depth = estimate.shape
    slab_count = lax.axis_size("slab")
    block_count = depth // 128
    width = slab_width * slab_count
    if not (
        block_count == slab_count
        and slab_width == 128
        and width // 128 == slab_count
        and row_count % 2 == 0
    ):
        return general_shards(estimate, views, psf, pattern_mult, pattern_shift, interp)
    blocks = block_matrix(pattern_mult[0], pattern_shift[0], interp[0])
    empty = jnp.zeros_like(blocks)
    doubled = jnp.concatenate(
        [jnp.concatenate([blocks, empty], 2), jnp.concatenate([empty, blocks], 2)], 1
    )
    sampled = jnp.einsum(
        "apxl,aml->apxm", to_blocks(estimate, block_count), doubled, precision=highest
    )
    pairs = row_count // 2
    spread = psf.reshape(slab_width, block_count, 128).transpose(1, 0, 2)[:, None]
    spread = jnp.concatenate([spread, jnp.zeros_like(spread)], -1)
    packed = jnp.concatenate([sampled, spread], 1)
    spectra = depth_forward(packed, depth)
    spectra = lax.all_to_all(spectra, "slab", split_axis=0, concat_axis=0, tiled=True)
    scaling = 1.0 / (width * depth)
    transfer = width_forward(spectra[:, pairs:], width) * scaling
    spectra = width_forward(spectra[:, :pairs], width)
    half = transfer.shape[-1] // 2
    transfer_real = jnp.concatenate([transfer[..., :half], transfer[..., :half]], -1)
    transfer_imag = jnp.concatenate([transfer[..., half:], transfer[..., half:]], -1)

    def convolve(spectra, transfer_imag):
        filtered = joined_times(spectra, transfer_real, transfer_imag)
        planes = width_inverse(filtered, width)
        planes = lax.all_to_all(planes, "slab", split_axis=0, concat_axis=0, tiled=True)
        return depth_inverse(planes, depth)

    blurred = convolve(spectra, transfer_imag)
    quotient = to_blocks(views[0], block_count) / blurred
    spectra = depth_forward(quotient, depth)
    spectra = lax.all_to_all(spectra, "slab", split_axis=0, concat_axis=0, tiled=True)
    spectra = width_forward(spectra, width)
    smeared = convolve(spectra, -transfer_imag)
    correction = jnp.einsum("apxm,aml->apxl", smeared, doubled, precision=highest)
    log_terms = from_blocks(jnp.log(correction))
    view_count = lax.axis_size("view")
    summed = lax.psum(log_terms, "view")
    return estimate * jnp.exp(summed / view_count)


def solution(mesh):
    placed = (
        P(None, "slab", None),
        P("view", None, "slab", None),
        P("view", "slab", None),
        P("view", None),
        P("view", None),
        P("view", None, None),
    )
    return jax.shard_map(
        shards, mesh=mesh, in_specs=placed, out_specs=P(None, "slab", None), check_vma=False
    )
```

```python
import math

import jax
import jax.numpy as jnp
from jax import lax
from jax.sharding import PartitionSpec as P

highest = lax.Precision.HIGHEST


def block_matrix(multiplier, shifting, weights):
    positions = jnp.arange(128, dtype=jnp.int32)
    first_col = ((2 * multiplier[:, None] + 1) * positions[None, :] + shifting[:, None]) % 128
    second_col = (first_col + 1) % 128
    columns = positions[None, None, :]
    lower = (columns == first_col[:, :, None]).astype(jnp.float32)
    upper = (columns == second_col[:, :, None]).astype(jnp.float32)
    return (1.0 - weights)[:, :, None] * lower + weights[:, :, None] * upper


def angle_tables(rows, cols, length):
    row_index = lax.iota(jnp.int32, rows)[:, None]
    col_index = lax.iota(jnp.int32, cols)[None, :]
    angles = (row_index * col_index % length).astype(jnp.float32) * (2.0 * math.pi / length)
    return (jnp.cos(angles), jnp.sin(angles))


def unit_root(numerator, length):
    angle = 2.0 * math.pi * numerator / length
    return (round(math.cos(angle), 15), round(math.sin(angle), 15))


def small_stage(real_part, imag_part, axis, direction):
    count = real_part.shape[axis]

    def part(array, index):
        return lax.index_in_dim(array, index, axis, keepdims=False)

    real_in = [part(real_part, index) for index in range(count)]
    imag_in = None if imag_part is None else [part(imag_part, index) for index in range(count)]
    real_out, imag_out = [], []
    for out_index in range(count):
        real_sum, imag_sum = None, None
        for in_index in range(count):
            cosine, sine = unit_root(in_index * out_index, count)
            sine = direction * sine
            terms_real = []
            terms_imag = []
            if cosine != 0.0:
                terms_real.append(cosine * real_in[in_index])
                if imag_in is not None:
                    terms_imag.append(cosine * imag_in[in_index])
            if sine != 0.0:
                terms_imag.append(sine * real_in[in_index])
                if imag_in is not None:
                    terms_real.append(-sine * imag_in[in_index])
            for term in terms_real:
                real_sum = term if real_sum is None else real_sum + term
            for term in terms_imag:
                imag_sum = term if imag_sum is None else imag_sum + term
        if imag_sum is None:
            imag_sum = jnp.zeros_like(real_sum)
        real_out.append(real_sum)
        imag_out.append(imag_sum)
    return (jnp.stack(real_out, axis), jnp.stack(imag_out, axis))


def complex_times(real_part, imag_part, cosine, sine_table):
    return (
        real_part * cosine - imag_part * sine_table,
        real_part * sine_table + imag_part * cosine,
    )


def block_dft_matrix(length, direction):
    cosine, sine = angle_tables(length, length, length)
    sine = direction * sine
    top = jnp.concatenate([cosine, sine], 1)
    bottom = jnp.concatenate([-sine, cosine], 1)
    return jnp.concatenate([top, bottom], 0)


def large_stage(real_part, imag_part, axis, direction):
    length = real_part.shape[axis]
    if imag_part is None:
        imag_part = jnp.zeros_like(real_part)
    joined = jnp.concatenate([real_part, imag_part], axis)
    matrix = block_dft_matrix(length, direction)
    if axis == joined.ndim - 1:
        out = jnp.einsum("...j,jn->...n", joined, matrix, precision=highest)
    else:
        out = jnp.einsum("rkjz,jn->rknz", joined, matrix, precision=highest)
    return (
        lax.slice_in_dim(out, 0, length, axis=axis),
        lax.slice_in_dim(out, length, 2 * length, axis=axis),
    )


def factored(real_part, imag_part, axis, direction, forward, want_imag=True):
    length = real_part.shape[axis]
    second = 128
    first = length // second
    outer = real_part.shape
    shape = outer[:axis] + (first, second) + outer[axis + 1 :]
    real_part = real_part.reshape(shape)
    if imag_part is not None:
        imag_part = imag_part.reshape(shape)
    twist_cos, twist_sin = angle_tables(first, second, length)
    if axis == 1:
        twist_cos = twist_cos[:, :, None]
        twist_sin = twist_sin[:, :, None]
    twist_sin = direction * twist_sin
    if forward:
        real_part, imag_part = small_stage(real_part, imag_part, axis, direction)
        real_part, imag_part = complex_times(real_part, imag_part, twist_cos, twist_sin)
        real_part, imag_part = large_stage(real_part, imag_part, axis + 1, direction)
    else:
        real_part, imag_part = large_stage(real_part, imag_part, axis + 1, direction)
        real_part, imag_part = complex_times(real_part, imag_part, twist_cos, twist_sin)
        real_part, imag_part = small_stage(real_part, imag_part, axis, direction)
    return (real_part.reshape(outer), imag_part.reshape(outer))


def to_columns(real_part, imag_part):
    depth_real, depth_imag = factored(real_part, imag_part, 2, -1.0, True)
    rows = depth_real.shape[0]
    stacked = jnp.concatenate([depth_real, depth_imag], 0)
    moved = lax.all_to_all(stacked, "slab", split_axis=2, concat_axis=1, tiled=True)
    return factored(moved[:rows], moved[rows:], 1, -1.0, True)


def to_planes(real_part, imag_part):
    width_real, width_imag = factored(real_part, imag_part, 1, 1.0, False)
    rows = width_real.shape[0]
    stacked = jnp.concatenate([width_real, width_imag], 0)
    moved = lax.all_to_all(stacked, "slab", split_axis=1, concat_axis=2, tiled=True)
    return factored(moved[:rows], moved[rows:], 2, 1.0, False)


def pack_pairs(volume):
    return (volume[0::2], volume[1::2])


def unpack_pairs(real_part, imag_part):
    pairs, width, depth = real_part.shape
    return jnp.stack([real_part, imag_part], 1).reshape(2 * pairs, width, depth)


def general_shards(estimate, views, psf, pattern_mult, pattern_shift, interp):
    row_count, slab_width, depth = estimate.shape
    blocks = block_matrix(pattern_mult[0], pattern_shift[0], interp[0])
    block_count = depth // 128
    shaped = estimate.reshape(row_count, slab_width, block_count, 128)
    sampled = jnp.einsum("bij,yxbj->yxbi", blocks, shaped, precision=highest).reshape(
        row_count, slab_width, depth
    )
    packed_real, packed_imag = pack_pairs(sampled)
    packed_real = jnp.concatenate([packed_real, psf], 0)
    packed_imag = jnp.concatenate([packed_imag, jnp.zeros_like(psf)], 0)
    spectra_real, spectra_imag = to_columns(packed_real, packed_imag)
    scaling = 1.0 / (spectra_real.shape[1] * depth)
    transfer_real = spectra_real[-1:] * scaling
    transfer_imag = spectra_imag[-1:] * scaling
    spectra_real = spectra_real[:-1]
    spectra_imag = spectra_imag[:-1]
    filtered_real = spectra_real * transfer_real - spectra_imag * transfer_imag
    filtered_imag = spectra_real * transfer_imag + spectra_imag * transfer_real
    blurred = unpack_pairs(*to_planes(filtered_real, filtered_imag))
    quotient = views[0] / blurred
    packed_real, packed_imag = pack_pairs(quotient)
    spectra_real, spectra_imag = to_columns(packed_real, packed_imag)
    filtered_real = spectra_real * transfer_real + spectra_imag * transfer_imag
    filtered_imag = spectra_imag * transfer_real - spectra_real * transfer_imag
    smeared = unpack_pairs(*to_planes(filtered_real, filtered_imag))
    correction = jnp.einsum(
        "bij,yxbi->yxbj",
        blocks,
        smeared.reshape(row_count, slab_width, block_count, 128),
        precision=highest,
    ).reshape(row_count, slab_width, depth)
    log_terms = jnp.log(correction)
    view_count = lax.axis_size("view")
    summed = lax.psum(log_terms, "view")
    return estimate * jnp.exp(summed / view_count)


def swap_halves(joined):
    half = joined.shape[-1] // 2
    return jnp.concatenate([-joined[..., half:], joined[..., :half]], -1)


def lead_stage(joined, direction):
    count = joined.shape[0]
    parts = [joined[index] for index in range(count)]
    turned = [swap_halves(part) for part in parts]
    outs = []
    for out_index in range(count):
        total = None
        for in_index in range(count):
            cosine, sine = unit_root(in_index * out_index, count)
            sine = direction * sine
            for weight, term in ((cosine, parts[in_index]), (sine, turned[in_index])):
                if weight != 0.0:
                    term = weight * term
                    total = term if total is None else total + term
        outs.append(total)
    return jnp.stack(outs, 0)


def joined_twist(joined, length, direction, lanes):
    first, second = joined.shape[0], (joined.shape[-1] // 2 if lanes else joined.shape[2])
    cosine, sine = angle_tables(first, second, length)
    sine = direction * sine
    if lanes:
        cosine = jnp.concatenate([cosine, cosine], 1)[:, None, None, :]
        sine = jnp.concatenate([sine, sine], 1)[:, None, None, :]
    else:
        cosine = cosine[:, None, :, None]
        sine = sine[:, None, :, None]
    return joined * cosine + swap_halves(joined) * sine


def lane_stage(joined, direction):
    length = joined.shape[-1] // 2
    matrix = block_dft_matrix(length, direction)
    return jnp.einsum("...j,jn->...n", joined, matrix, precision=highest)


def row_stage(joined, direction):
    length = joined.shape[2]
    cosine, sine = angle_tables(length, length, length)
    matrix = jnp.concatenate([cosine, direction * sine], 0)
    both = jnp.concatenate([joined, swap_halves(joined)], 2)
    return jnp.einsum("krjl,jm->krml", both, matrix, precision=highest)


def depth_forward(joined, depth):
    joined = lead_stage(joined, -1.0)
    joined = joined_twist(joined, depth, -1.0, True)
    return lane_stage(joined, -1.0)


def depth_inverse(joined, depth):
    joined = lane_stage(joined, 1.0)
    joined = joined_twist(joined, depth, 1.0, True)
    return lead_stage(joined, 1.0)


def width_forward(joined, width):
    joined = lead_stage(joined, -1.0)
    joined = joined_twist(joined, width, -1.0, False)
    return row_stage(joined, -1.0)


def width_inverse(joined, width):
    joined = row_stage(joined, 1.0)
    joined = joined_twist(joined, width, 1.0, False)
    return lead_stage(joined, 1.0)


def joined_times(joined, transfer_real, transfer_imag):
    return joined * transfer_real + swap_halves(joined) * transfer_imag


def to_blocks(volume, block_count):
    rows, width, depth = volume.shape
    lanes = depth // block_count
    parity = [volume[0::2], volume[1::2]]
    return jnp.stack(
        [
            jnp.concatenate([part[:, :, block * lanes : (block + 1) * lanes] for part in parity], -1)
            for block in range(block_count)
        ],
        0,
    )


def from_blocks(blocked):
    block_count, pairs, width, lanes = blocked.shape
    half = lanes // 2
    parity = [
        jnp.concatenate([blocked[block, :, :, side * half : (side + 1) * half] for block in range(block_count)], -1)
        for side in range(2)
    ]
    return jnp.stack(parity, 1).reshape(2 * pairs, width, block_count * half)


def shards(estimate, views, psf, pattern_mult, pattern_shift, interp):
    row_count, slab_width, depth = estimate.shape
    slab_count = lax.axis_size("slab")
    block_count = depth // 128
    width = slab_width * slab_count
    if not (
        block_count == slab_count
        and slab_width == 128
        and width // 128 == slab_count
        and row_count % 2 == 0
    ):
        return general_shards(estimate, views, psf, pattern_mult, pattern_shift, interp)
    blocks = block_matrix(pattern_mult[0], pattern_shift[0], interp[0])
    empty = jnp.zeros_like(blocks)
    doubled = jnp.concatenate(
        [jnp.concatenate([blocks, empty], 2), jnp.concatenate([empty, blocks], 2)], 1
    )
    sampled = jnp.einsum(
        "apxl,aml->apxm", to_blocks(estimate, block_count), doubled, precision=highest
    )
    pairs = row_count // 2
    spread = psf.reshape(slab_width, block_count, 128).transpose(1, 0, 2)[:, None]
    spread = jnp.concatenate([spread, jnp.zeros_like(spread)], -1)
    packed = jnp.concatenate([sampled, spread], 1)
    spectra = depth_forward(packed, depth)
    spectra = lax.all_to_all(spectra, "slab", split_axis=0, concat_axis=0, tiled=True)
    scaling = 1.0 / (width * depth)
    transfer = width_forward(spectra[:, pairs:], width) * scaling
    spectra = width_forward(spectra[:, :pairs], width)
    half = transfer.shape[-1] // 2
    transfer_real = jnp.concatenate([transfer[..., :half], transfer[..., :half]], -1)
    transfer_imag = jnp.concatenate([transfer[..., half:], transfer[..., half:]], -1)

    def convolve(spectra, transfer_imag):
        filtered = joined_times(spectra, transfer_real, transfer_imag)
        planes = width_inverse(filtered, width)
        planes = lax.all_to_all(planes, "slab", split_axis=0, concat_axis=0, tiled=True)
        return depth_inverse(planes, depth)

    blurred = convolve(spectra, transfer_imag)
    quotient = to_blocks(views[0], block_count) / blurred
    spectra = depth_forward(quotient, depth)
    spectra = lax.all_to_all(spectra, "slab", split_axis=0, concat_axis=0, tiled=True)
    spectra = width_forward(spectra, width)
    smeared = convolve(spectra, -transfer_imag)
    correction = jnp.einsum("apxm,aml->apxl", smeared, doubled, precision=highest)
    log_terms = from_blocks(jnp.log(correction))
    view_count = lax.axis_size("view")
    summed = lax.psum(log_terms, "view")
    return estimate * jnp.exp(summed / view_count)


def solution(mesh):
    placed = (
        P(None, "slab", None),
        P("view", None, "slab", None),
        P("view", "slab", None),
        P("view", None),
        P("view", None),
        P("view", None, None),
    )
    return jax.shard_map(
        shards, mesh=mesh, in_specs=placed, out_specs=P(None, "slab", None), check_vma=False
    )
```

```python
import math

import jax
import jax.numpy as jnp
from jax import lax
from jax.sharding import PartitionSpec as P

highest = lax.Precision.HIGHEST


def block_matrix(multiplier, shifting, weights):
    positions = jnp.arange(128, dtype=jnp.int32)
    first_col = ((2 * multiplier[:, None] + 1) * positions[None, :] + shifting[:, None]) % 128
    second_col = (first_col + 1) % 128
    columns = positions[None, None, :]
    lower = (columns == first_col[:, :, None]).astype(jnp.float32)
    upper = (columns == second_col[:, :, None]).astype(jnp.float32)
    return (1.0 - weights)[:, :, None] * lower + weights[:, :, None] * upper


def angle_tables(rows, cols, length):
    row_index = lax.iota(jnp.int32, rows)[:, None]
    col_index = lax.iota(jnp.int32, cols)[None, :]
    angles = (row_index * col_index % length).astype(jnp.float32) * (2.0 * math.pi / length)
    return (jnp.cos(angles), jnp.sin(angles))


def unit_root(numerator, length):
    angle = 2.0 * math.pi * numerator / length
    return (round(math.cos(angle), 15), round(math.sin(angle), 15))


def small_stage(real_part, imag_part, axis, direction):
    count = real_part.shape[axis]

    def part(array, index):
        return lax.index_in_dim(array, index, axis, keepdims=False)

    real_in = [part(real_part, index) for index in range(count)]
    imag_in = None if imag_part is None else [part(imag_part, index) for index in range(count)]
    real_out, imag_out = [], []
    for out_index in range(count):
        real_sum, imag_sum = None, None
        for in_index in range(count):
            cosine, sine = unit_root(in_index * out_index, count)
            sine = direction * sine
            terms_real = []
            terms_imag = []
            if cosine != 0.0:
                terms_real.append(cosine * real_in[in_index])
                if imag_in is not None:
                    terms_imag.append(cosine * imag_in[in_index])
            if sine != 0.0:
                terms_imag.append(sine * real_in[in_index])
                if imag_in is not None:
                    terms_real.append(-sine * imag_in[in_index])
            for term in terms_real:
                real_sum = term if real_sum is None else real_sum + term
            for term in terms_imag:
                imag_sum = term if imag_sum is None else imag_sum + term
        if imag_sum is None:
            imag_sum = jnp.zeros_like(real_sum)
        real_out.append(real_sum)
        imag_out.append(imag_sum)
    return (jnp.stack(real_out, axis), jnp.stack(imag_out, axis))


def complex_times(real_part, imag_part, cosine, sine_table):
    return (
        real_part * cosine - imag_part * sine_table,
        real_part * sine_table + imag_part * cosine,
    )


def block_dft_matrix(length, direction):
    cosine, sine = angle_tables(length, length, length)
    sine = direction * sine
    top = jnp.concatenate([cosine, sine], 1)
    bottom = jnp.concatenate([-sine, cosine], 1)
    return jnp.concatenate([top, bottom], 0)


def large_stage(real_part, imag_part, axis, direction):
    length = real_part.shape[axis]
    if imag_part is None:
        imag_part = jnp.zeros_like(real_part)
    joined = jnp.concatenate([real_part, imag_part], axis)
    matrix = block_dft_matrix(length, direction)
    if axis == joined.ndim - 1:
        out = jnp.einsum("...j,jn->...n", joined, matrix, precision=highest)
    else:
        out = jnp.einsum("rkjz,jn->rknz", joined, matrix, precision=highest)
    return (
        lax.slice_in_dim(out, 0, length, axis=axis),
        lax.slice_in_dim(out, length, 2 * length, axis=axis),
    )


def factored(real_part, imag_part, axis, direction, forward, want_imag=True):
    length = real_part.shape[axis]
    second = 128
    first = length // second
    outer = real_part.shape
    shape = outer[:axis] + (first, second) + outer[axis + 1 :]
    real_part = real_part.reshape(shape)
    if imag_part is not None:
        imag_part = imag_part.reshape(shape)
    twist_cos, twist_sin = angle_tables(first, second, length)
    if axis == 1:
        twist_cos = twist_cos[:, :, None]
        twist_sin = twist_sin[:, :, None]
    twist_sin = direction * twist_sin
    if forward:
        real_part, imag_part = small_stage(real_part, imag_part, axis, direction)
        real_part, imag_part = complex_times(real_part, imag_part, twist_cos, twist_sin)
        real_part, imag_part = large_stage(real_part, imag_part, axis + 1, direction)
    else:
        real_part, imag_part = large_stage(real_part, imag_part, axis + 1, direction)
        real_part, imag_part = complex_times(real_part, imag_part, twist_cos, twist_sin)
        real_part, imag_part = small_stage(real_part, imag_part, axis, direction)
    return (real_part.reshape(outer), imag_part.reshape(outer))


def to_columns(real_part, imag_part):
    depth_real, depth_imag = factored(real_part, imag_part, 2, -1.0, True)
    rows = depth_real.shape[0]
    stacked = jnp.concatenate([depth_real, depth_imag], 0)
    moved = lax.all_to_all(stacked, "slab", split_axis=2, concat_axis=1, tiled=True)
    return factored(moved[:rows], moved[rows:], 1, -1.0, True)


def to_planes(real_part, imag_part):
    width_real, width_imag = factored(real_part, imag_part, 1, 1.0, False)
    rows = width_real.shape[0]
    stacked = jnp.concatenate([width_real, width_imag], 0)
    moved = lax.all_to_all(stacked, "slab", split_axis=1, concat_axis=2, tiled=True)
    return factored(moved[:rows], moved[rows:], 2, 1.0, False)


def pack_pairs(volume):
    return (volume[0::2], volume[1::2])


def unpack_pairs(real_part, imag_part):
    pairs, width, depth = real_part.shape
    return jnp.stack([real_part, imag_part], 1).reshape(2 * pairs, width, depth)


def general_shards(estimate, views, psf, pattern_mult, pattern_shift, interp):
    row_count, slab_width, depth = estimate.shape
    blocks = block_matrix(pattern_mult[0], pattern_shift[0], interp[0])
    block_count = depth // 128
    shaped = estimate.reshape(row_count, slab_width, block_count, 128)
    sampled = jnp.einsum("bij,yxbj->yxbi", blocks, shaped, precision=highest).reshape(
        row_count, slab_width, depth
    )
    packed_real, packed_imag = pack_pairs(sampled)
    packed_real = jnp.concatenate([packed_real, psf], 0)
    packed_imag = jnp.concatenate([packed_imag, jnp.zeros_like(psf)], 0)
    spectra_real, spectra_imag = to_columns(packed_real, packed_imag)
    scaling = 1.0 / (spectra_real.shape[1] * depth)
    transfer_real = spectra_real[-1:] * scaling
    transfer_imag = spectra_imag[-1:] * scaling
    spectra_real = spectra_real[:-1]
    spectra_imag = spectra_imag[:-1]
    filtered_real = spectra_real * transfer_real - spectra_imag * transfer_imag
    filtered_imag = spectra_real * transfer_imag + spectra_imag * transfer_real
    blurred = unpack_pairs(*to_planes(filtered_real, filtered_imag))
    quotient = views[0] / blurred
    packed_real, packed_imag = pack_pairs(quotient)
    spectra_real, spectra_imag = to_columns(packed_real, packed_imag)
    filtered_real = spectra_real * transfer_real + spectra_imag * transfer_imag
    filtered_imag = spectra_imag * transfer_real - spectra_real * transfer_imag
    smeared = unpack_pairs(*to_planes(filtered_real, filtered_imag))
    correction = jnp.einsum(
        "bij,yxbi->yxbj",
        blocks,
        smeared.reshape(row_count, slab_width, block_count, 128),
        precision=highest,
    ).reshape(row_count, slab_width, depth)
    log_terms = jnp.log(correction)
    view_count = lax.axis_size("view")
    summed = lax.psum(log_terms, "view")
    return estimate * jnp.exp(summed / view_count)


def swap_halves(joined):
    half = joined.shape[-1] // 2
    return jnp.concatenate([-joined[..., half:], joined[..., :half]], -1)


def lead_stage(joined, direction):
    count = joined.shape[0]
    parts = [joined[index] for index in range(count)]
    turned = [swap_halves(part) for part in parts]
    outs = []
    for out_index in range(count):
        total = None
        for in_index in range(count):
            cosine, sine = unit_root(in_index * out_index, count)
            sine = direction * sine
            for weight, term in ((cosine, parts[in_index]), (sine, turned[in_index])):
                if weight != 0.0:
                    term = weight * term
                    total = term if total is None else total + term
        outs.append(total)
    return jnp.stack(outs, 0)


def joined_twist(joined, length, direction, lanes):
    first, second = joined.shape[0], (joined.shape[-1] // 2 if lanes else joined.shape[2])
    cosine, sine = angle_tables(first, second, length)
    sine = direction * sine
    if lanes:
        cosine = jnp.concatenate([cosine, cosine], 1)[:, None, None, :]
        sine = jnp.concatenate([sine, sine], 1)[:, None, None, :]
    else:
        cosine = cosine[:, None, :, None]
        sine = sine[:, None, :, None]
    return joined * cosine + swap_halves(joined) * sine


def lane_stage(joined, direction):
    length = joined.shape[-1] // 2
    matrix = block_dft_matrix(length, direction)
    return jnp.einsum("...j,jn->...n", joined, matrix, precision=highest)


def row_stage(joined, direction):
    length = joined.shape[2]
    cosine, sine = angle_tables(length, length, length)
    matrix = jnp.concatenate([cosine, direction * sine], 0)
    both = jnp.concatenate([joined, swap_halves(joined)], 2)
    return jnp.einsum("krjl,jm->krml", both, matrix, precision=highest)


def depth_forward(joined, depth):
    joined = lead_stage(joined, -1.0)
    joined = joined_twist(joined, depth, -1.0, True)
    return lane_stage(joined, -1.0)


def depth_inverse(joined, depth):
    joined = lane_stage(joined, 1.0)
    joined = joined_twist(joined, depth, 1.0, True)
    return lead_stage(joined, 1.0)


def width_forward(joined, width):
    joined = lead_stage(joined, -1.0)
    joined = joined_twist(joined, width, -1.0, False)
    return row_stage(joined, -1.0)


def width_inverse(joined, width):
    joined = row_stage(joined, 1.0)
    joined = joined_twist(joined, width, 1.0, False)
    return lead_stage(joined, 1.0)


def joined_times(joined, transfer_real, transfer_imag):
    return joined * transfer_real + swap_halves(joined) * transfer_imag


def to_blocks(volume, block_count):
    rows, width, depth = volume.shape
    lanes = depth // block_count
    parity = [volume[0::2], volume[1::2]]
    return jnp.stack(
        [
            jnp.concatenate([part[:, :, block * lanes : (block + 1) * lanes] for part in parity], -1)
            for block in range(block_count)
        ],
        0,
    )


def from_blocks(blocked):
    block_count, pairs, width, lanes = blocked.shape
    half = lanes // 2
    parity = [
        jnp.concatenate([blocked[block, :, :, side * half : (side + 1) * half] for block in range(block_count)], -1)
        for side in range(2)
    ]
    return jnp.stack(parity, 1).reshape(2 * pairs, width, block_count * half)


def shards(estimate, views, psf, pattern_mult, pattern_shift, interp):
    row_count, slab_width, depth = estimate.shape
    slab_count = lax.axis_size("slab")
    block_count = depth // 128
    width = slab_width * slab_count
    if not (
        block_count == slab_count
        and slab_width == 128
        and width // 128 == slab_count
        and row_count % 2 == 0
    ):
        return general_shards(estimate, views, psf, pattern_mult, pattern_shift, interp)
    blocks = block_matrix(pattern_mult[0], pattern_shift[0], interp[0])
    empty = jnp.zeros_like(blocks)
    doubled = jnp.concatenate(
        [jnp.concatenate([blocks, empty], 2), jnp.concatenate([empty, blocks], 2)], 1
    )
    sampled = jnp.einsum(
        "apxl,aml->apxm", to_blocks(estimate, block_count), doubled, precision=highest
    )
    pairs = row_count // 2
    spread = psf.reshape(slab_width, block_count, 128).transpose(1, 0, 2)[:, None]
    spread = jnp.concatenate([spread, jnp.zeros_like(spread)], -1)
    def to_columns_blocked(planes):
        spectra = depth_forward(planes, depth)
        spectra = lax.all_to_all(spectra, "slab", split_axis=0, concat_axis=0, tiled=True)
        return width_forward(spectra, width)

    transfer = to_columns_blocked(spread) * (1.0 / (width * depth))
    spectra = to_columns_blocked(sampled)
    half = transfer.shape[-1] // 2
    transfer_real = jnp.concatenate([transfer[..., :half], transfer[..., :half]], -1)
    transfer_imag = jnp.concatenate([transfer[..., half:], transfer[..., half:]], -1)

    def convolve(spectra, transfer_imag):
        filtered = joined_times(spectra, transfer_real, transfer_imag)
        planes = width_inverse(filtered, width)
        planes = lax.all_to_all(planes, "slab", split_axis=0, concat_axis=0, tiled=True)
        return depth_inverse(planes, depth)

    blurred = convolve(spectra, transfer_imag)
    quotient = to_blocks(views[0], block_count) / blurred
    spectra = depth_forward(quotient, depth)
    spectra = lax.all_to_all(spectra, "slab", split_axis=0, concat_axis=0, tiled=True)
    spectra = width_forward(spectra, width)
    smeared = convolve(spectra, -transfer_imag)
    correction = jnp.einsum("apxm,aml->apxl", smeared, doubled, precision=highest)
    log_terms = from_blocks(jnp.log(correction))
    view_count = lax.axis_size("view")
    summed = lax.psum(log_terms, "view")
    return estimate * jnp.exp(summed / view_count)


def solution(mesh):
    placed = (
        P(None, "slab", None),
        P("view", None, "slab", None),
        P("view", "slab", None),
        P("view", None),
        P("view", None),
        P("view", None, None),
    )
    return jax.shard_map(
        shards, mesh=mesh, in_specs=placed, out_specs=P(None, "slab", None), check_vma=False
    )
```

```python
import math

import jax
import jax.numpy as jnp
from jax import lax
from jax.sharding import PartitionSpec as P

highest = lax.Precision.HIGHEST


def block_matrix(multiplier, shifting, weights):
    positions = jnp.arange(128, dtype=jnp.int32)
    first_col = ((2 * multiplier[:, None] + 1) * positions[None, :] + shifting[:, None]) % 128
    second_col = (first_col + 1) % 128
    columns = positions[None, None, :]
    lower = (columns == first_col[:, :, None]).astype(jnp.float32)
    upper = (columns == second_col[:, :, None]).astype(jnp.float32)
    return (1.0 - weights)[:, :, None] * lower + weights[:, :, None] * upper


def angle_tables(rows, cols, length):
    row_index = lax.iota(jnp.int32, rows)[:, None]
    col_index = lax.iota(jnp.int32, cols)[None, :]
    angles = (row_index * col_index % length).astype(jnp.float32) * (2.0 * math.pi / length)
    return (jnp.cos(angles), jnp.sin(angles))


def unit_root(numerator, length):
    angle = 2.0 * math.pi * numerator / length
    return (round(math.cos(angle), 15), round(math.sin(angle), 15))


def small_stage(real_part, imag_part, axis, direction):
    count = real_part.shape[axis]

    def part(array, index):
        return lax.index_in_dim(array, index, axis, keepdims=False)

    real_in = [part(real_part, index) for index in range(count)]
    imag_in = None if imag_part is None else [part(imag_part, index) for index in range(count)]
    real_out, imag_out = [], []
    for out_index in range(count):
        real_sum, imag_sum = None, None
        for in_index in range(count):
            cosine, sine = unit_root(in_index * out_index, count)
            sine = direction * sine
            terms_real = []
            terms_imag = []
            if cosine != 0.0:
                terms_real.append(cosine * real_in[in_index])
                if imag_in is not None:
                    terms_imag.append(cosine * imag_in[in_index])
            if sine != 0.0:
                terms_imag.append(sine * real_in[in_index])
                if imag_in is not None:
                    terms_real.append(-sine * imag_in[in_index])
            for term in terms_real:
                real_sum = term if real_sum is None else real_sum + term
            for term in terms_imag:
                imag_sum = term if imag_sum is None else imag_sum + term
        if imag_sum is None:
            imag_sum = jnp.zeros_like(real_sum)
        real_out.append(real_sum)
        imag_out.append(imag_sum)
    return (jnp.stack(real_out, axis), jnp.stack(imag_out, axis))


def complex_times(real_part, imag_part, cosine, sine_table):
    return (
        real_part * cosine - imag_part * sine_table,
        real_part * sine_table + imag_part * cosine,
    )


def block_dft_matrix(length, direction):
    cosine, sine = angle_tables(length, length, length)
    sine = direction * sine
    top = jnp.concatenate([cosine, sine], 1)
    bottom = jnp.concatenate([-sine, cosine], 1)
    return jnp.concatenate([top, bottom], 0)


def large_stage(real_part, imag_part, axis, direction):
    length = real_part.shape[axis]
    if imag_part is None:
        imag_part = jnp.zeros_like(real_part)
    joined = jnp.concatenate([real_part, imag_part], axis)
    matrix = block_dft_matrix(length, direction)
    if axis == joined.ndim - 1:
        out = jnp.einsum("...j,jn->...n", joined, matrix, precision=highest)
    else:
        out = jnp.einsum("rkjz,jn->rknz", joined, matrix, precision=highest)
    return (
        lax.slice_in_dim(out, 0, length, axis=axis),
        lax.slice_in_dim(out, length, 2 * length, axis=axis),
    )


def factored(real_part, imag_part, axis, direction, forward, want_imag=True):
    length = real_part.shape[axis]
    second = 128
    first = length // second
    outer = real_part.shape
    shape = outer[:axis] + (first, second) + outer[axis + 1 :]
    real_part = real_part.reshape(shape)
    if imag_part is not None:
        imag_part = imag_part.reshape(shape)
    twist_cos, twist_sin = angle_tables(first, second, length)
    if axis == 1:
        twist_cos = twist_cos[:, :, None]
        twist_sin = twist_sin[:, :, None]
    twist_sin = direction * twist_sin
    if forward:
        real_part, imag_part = small_stage(real_part, imag_part, axis, direction)
        real_part, imag_part = complex_times(real_part, imag_part, twist_cos, twist_sin)
        real_part, imag_part = large_stage(real_part, imag_part, axis + 1, direction)
    else:
        real_part, imag_part = large_stage(real_part, imag_part, axis + 1, direction)
        real_part, imag_part = complex_times(real_part, imag_part, twist_cos, twist_sin)
        real_part, imag_part = small_stage(real_part, imag_part, axis, direction)
    return (real_part.reshape(outer), imag_part.reshape(outer))


def to_columns(real_part, imag_part):
    depth_real, depth_imag = factored(real_part, imag_part, 2, -1.0, True)
    rows = depth_real.shape[0]
    stacked = jnp.concatenate([depth_real, depth_imag], 0)
    moved = lax.all_to_all(stacked, "slab", split_axis=2, concat_axis=1, tiled=True)
    return factored(moved[:rows], moved[rows:], 1, -1.0, True)


def to_planes(real_part, imag_part):
    width_real, width_imag = factored(real_part, imag_part, 1, 1.0, False)
    rows = width_real.shape[0]
    stacked = jnp.concatenate([width_real, width_imag], 0)
    moved = lax.all_to_all(stacked, "slab", split_axis=1, concat_axis=2, tiled=True)
    return factored(moved[:rows], moved[rows:], 2, 1.0, False)


def pack_pairs(volume):
    return (volume[0::2], volume[1::2])


def unpack_pairs(real_part, imag_part):
    pairs, width, depth = real_part.shape
    return jnp.stack([real_part, imag_part], 1).reshape(2 * pairs, width, depth)


def general_shards(estimate, views, psf, pattern_mult, pattern_shift, interp):
    row_count, slab_width, depth = estimate.shape
    blocks = block_matrix(pattern_mult[0], pattern_shift[0], interp[0])
    block_count = depth // 128
    shaped = estimate.reshape(row_count, slab_width, block_count, 128)
    sampled = jnp.einsum("bij,yxbj->yxbi", blocks, shaped, precision=highest).reshape(
        row_count, slab_width, depth
    )
    packed_real, packed_imag = pack_pairs(sampled)
    packed_real = jnp.concatenate([packed_real, psf], 0)
    packed_imag = jnp.concatenate([packed_imag, jnp.zeros_like(psf)], 0)
    spectra_real, spectra_imag = to_columns(packed_real, packed_imag)
    scaling = 1.0 / (spectra_real.shape[1] * depth)
    transfer_real = spectra_real[-1:] * scaling
    transfer_imag = spectra_imag[-1:] * scaling
    spectra_real = spectra_real[:-1]
    spectra_imag = spectra_imag[:-1]
    filtered_real = spectra_real * transfer_real - spectra_imag * transfer_imag
    filtered_imag = spectra_real * transfer_imag + spectra_imag * transfer_real
    blurred = unpack_pairs(*to_planes(filtered_real, filtered_imag))
    quotient = views[0] / blurred
    packed_real, packed_imag = pack_pairs(quotient)
    spectra_real, spectra_imag = to_columns(packed_real, packed_imag)
    filtered_real = spectra_real * transfer_real + spectra_imag * transfer_imag
    filtered_imag = spectra_imag * transfer_real - spectra_real * transfer_imag
    smeared = unpack_pairs(*to_planes(filtered_real, filtered_imag))
    correction = jnp.einsum(
        "bij,yxbi->yxbj",
        blocks,
        smeared.reshape(row_count, slab_width, block_count, 128),
        precision=highest,
    ).reshape(row_count, slab_width, depth)
    log_terms = jnp.log(correction)
    view_count = lax.axis_size("view")
    summed = lax.psum(log_terms, "view")
    return estimate * jnp.exp(summed / view_count)


def swap_halves(joined):
    half = joined.shape[-1] // 2
    return jnp.concatenate([-joined[..., half:], joined[..., :half]], -1)


def lead_stage(joined, direction):
    count = joined.shape[0]
    parts = [joined[index] for index in range(count)]
    turned = [swap_halves(part) for part in parts]
    outs = []
    for out_index in range(count):
        total = None
        for in_index in range(count):
            cosine, sine = unit_root(in_index * out_index, count)
            sine = direction * sine
            for weight, term in ((cosine, parts[in_index]), (sine, turned[in_index])):
                if weight != 0.0:
                    term = weight * term
                    total = term if total is None else total + term
        outs.append(total)
    return jnp.stack(outs, 0)


def joined_twist(joined, length, direction, lanes):
    first, second = joined.shape[0], (joined.shape[-1] // 2 if lanes else joined.shape[2])
    cosine, sine = angle_tables(first, second, length)
    sine = direction * sine
    if lanes:
        cosine = jnp.concatenate([cosine, cosine], 1)[:, None, None, :]
        sine = jnp.concatenate([sine, sine], 1)[:, None, None, :]
    else:
        cosine = cosine[:, None, :, None]
        sine = sine[:, None, :, None]
    return joined * cosine + swap_halves(joined) * sine


def lane_stage(joined, direction):
    length = joined.shape[-1] // 2
    matrix = block_dft_matrix(length, direction)
    return jnp.einsum("...j,jn->...n", joined, matrix, precision=highest)


def row_stage(joined, direction):
    length = joined.shape[2]
    cosine, sine = angle_tables(length, length, length)
    direct = jnp.einsum("krjl,jm->krml", joined, cosine, precision=highest)
    turned = jnp.einsum("krjl,jm->krml", swap_halves(joined), direction * sine, precision=highest)
    return direct + turned


def depth_forward(joined, depth):
    joined = lead_stage(joined, -1.0)
    joined = joined_twist(joined, depth, -1.0, True)
    return lane_stage(joined, -1.0)


def depth_inverse(joined, depth):
    joined = lane_stage(joined, 1.0)
    joined = joined_twist(joined, depth, 1.0, True)
    return lead_stage(joined, 1.0)


def width_forward(joined, width):
    joined = lead_stage(joined, -1.0)
    joined = joined_twist(joined, width, -1.0, False)
    return row_stage(joined, -1.0)


def width_inverse(joined, width):
    joined = row_stage(joined, 1.0)
    joined = joined_twist(joined, width, 1.0, False)
    return lead_stage(joined, 1.0)


def joined_times(joined, transfer_real, transfer_imag):
    return joined * transfer_real + swap_halves(joined) * transfer_imag


def to_blocks(volume, block_count):
    rows, width, depth = volume.shape
    lanes = depth // block_count
    parity = [volume[0::2], volume[1::2]]
    return jnp.stack(
        [
            jnp.concatenate([part[:, :, block * lanes : (block + 1) * lanes] for part in parity], -1)
            for block in range(block_count)
        ],
        0,
    )


def from_blocks(blocked):
    block_count, pairs, width, lanes = blocked.shape
    half = lanes // 2
    parity = [
        jnp.concatenate([blocked[block, :, :, side * half : (side + 1) * half] for block in range(block_count)], -1)
        for side in range(2)
    ]
    return jnp.stack(parity, 1).reshape(2 * pairs, width, block_count * half)


def shards(estimate, views, psf, pattern_mult, pattern_shift, interp):
    row_count, slab_width, depth = estimate.shape
    slab_count = lax.axis_size("slab")
    block_count = depth // 128
    width = slab_width * slab_count
    if not (
        block_count == slab_count
        and slab_width == 128
        and width // 128 == slab_count
        and row_count % 2 == 0
    ):
        return general_shards(estimate, views, psf, pattern_mult, pattern_shift, interp)
    blocks = block_matrix(pattern_mult[0], pattern_shift[0], interp[0])
    empty = jnp.zeros_like(blocks)
    doubled = jnp.concatenate(
        [jnp.concatenate([blocks, empty], 2), jnp.concatenate([empty, blocks], 2)], 1
    )
    sampled = jnp.einsum(
        "apxl,aml->apxm", to_blocks(estimate, block_count), doubled, precision=highest
    )
    pairs = row_count // 2
    spread = psf.reshape(slab_width, block_count, 128).transpose(1, 0, 2)[:, None]
    spread = jnp.concatenate([spread, jnp.zeros_like(spread)], -1)
    def to_columns_blocked(planes):
        spectra = depth_forward(planes, depth)
        spectra = lax.all_to_all(spectra, "slab", split_axis=0, concat_axis=0, tiled=True)
        return width_forward(spectra, width)

    transfer = to_columns_blocked(spread) * (1.0 / (width * depth))
    spectra = to_columns_blocked(sampled)
    half = transfer.shape[-1] // 2
    transfer_real = jnp.concatenate([transfer[..., :half], transfer[..., :half]], -1)
    transfer_imag = jnp.concatenate([transfer[..., half:], transfer[..., half:]], -1)

    def convolve(spectra, transfer_imag):
        filtered = joined_times(spectra, transfer_real, transfer_imag)
        planes = width_inverse(filtered, width)
        planes = lax.all_to_all(planes, "slab", split_axis=0, concat_axis=0, tiled=True)
        return depth_inverse(planes, depth)

    blurred = convolve(spectra, transfer_imag)
    quotient = to_blocks(views[0], block_count) / blurred
    spectra = depth_forward(quotient, depth)
    spectra = lax.all_to_all(spectra, "slab", split_axis=0, concat_axis=0, tiled=True)
    spectra = width_forward(spectra, width)
    smeared = convolve(spectra, -transfer_imag)
    correction = jnp.einsum("apxm,aml->apxl", smeared, doubled, precision=highest)
    log_terms = from_blocks(jnp.log(correction))
    view_count = lax.axis_size("view")
    summed = lax.psum(log_terms, "view")
    return estimate * jnp.exp(summed / view_count)


def solution(mesh):
    placed = (
        P(None, "slab", None),
        P("view", None, "slab", None),
        P("view", "slab", None),
        P("view", None),
        P("view", None),
        P("view", None, None),
    )
    return jax.shard_map(
        shards, mesh=mesh, in_specs=placed, out_specs=P(None, "slab", None), check_vma=False
    )
```

```python
import math

import jax
import jax.numpy as jnp
from jax import lax
from jax.sharding import PartitionSpec as P

highest = lax.Precision.HIGHEST


def block_matrix(multiplier, shifting, weights):
    positions = jnp.arange(128, dtype=jnp.int32)
    first_col = ((2 * multiplier[:, None] + 1) * positions[None, :] + shifting[:, None]) % 128
    second_col = (first_col + 1) % 128
    columns = positions[None, None, :]
    lower = (columns == first_col[:, :, None]).astype(jnp.float32)
    upper = (columns == second_col[:, :, None]).astype(jnp.float32)
    return (1.0 - weights)[:, :, None] * lower + weights[:, :, None] * upper


def angle_tables(rows, cols, length):
    row_index = lax.iota(jnp.int32, rows)[:, None]
    col_index = lax.iota(jnp.int32, cols)[None, :]
    angles = (row_index * col_index % length).astype(jnp.float32) * (2.0 * math.pi / length)
    return (jnp.cos(angles), jnp.sin(angles))


def unit_root(numerator, length):
    angle = 2.0 * math.pi * numerator / length
    return (round(math.cos(angle), 15), round(math.sin(angle), 15))


def small_stage(real_part, imag_part, axis, direction):
    count = real_part.shape[axis]

    def part(array, index):
        return lax.index_in_dim(array, index, axis, keepdims=False)

    real_in = [part(real_part, index) for index in range(count)]
    imag_in = None if imag_part is None else [part(imag_part, index) for index in range(count)]
    real_out, imag_out = [], []
    for out_index in range(count):
        real_sum, imag_sum = None, None
        for in_index in range(count):
            cosine, sine = unit_root(in_index * out_index, count)
            sine = direction * sine
            terms_real = []
            terms_imag = []
            if cosine != 0.0:
                terms_real.append(cosine * real_in[in_index])
                if imag_in is not None:
                    terms_imag.append(cosine * imag_in[in_index])
            if sine != 0.0:
                terms_imag.append(sine * real_in[in_index])
                if imag_in is not None:
                    terms_real.append(-sine * imag_in[in_index])
            for term in terms_real:
                real_sum = term if real_sum is None else real_sum + term
            for term in terms_imag:
                imag_sum = term if imag_sum is None else imag_sum + term
        if imag_sum is None:
            imag_sum = jnp.zeros_like(real_sum)
        real_out.append(real_sum)
        imag_out.append(imag_sum)
    return (jnp.stack(real_out, axis), jnp.stack(imag_out, axis))


def complex_times(real_part, imag_part, cosine, sine_table):
    return (
        real_part * cosine - imag_part * sine_table,
        real_part * sine_table + imag_part * cosine,
    )


def block_dft_matrix(length, direction):
    cosine, sine = angle_tables(length, length, length)
    sine = direction * sine
    top = jnp.concatenate([cosine, sine], 1)
    bottom = jnp.concatenate([-sine, cosine], 1)
    return jnp.concatenate([top, bottom], 0)


def large_stage(real_part, imag_part, axis, direction):
    length = real_part.shape[axis]
    if imag_part is None:
        imag_part = jnp.zeros_like(real_part)
    joined = jnp.concatenate([real_part, imag_part], axis)
    matrix = block_dft_matrix(length, direction)
    if axis == joined.ndim - 1:
        out = jnp.einsum("...j,jn->...n", joined, matrix, precision=highest)
    else:
        out = jnp.einsum("rkjz,jn->rknz", joined, matrix, precision=highest)
    return (
        lax.slice_in_dim(out, 0, length, axis=axis),
        lax.slice_in_dim(out, length, 2 * length, axis=axis),
    )


def factored(real_part, imag_part, axis, direction, forward, want_imag=True):
    length = real_part.shape[axis]
    second = 128
    first = length // second
    outer = real_part.shape
    shape = outer[:axis] + (first, second) + outer[axis + 1 :]
    real_part = real_part.reshape(shape)
    if imag_part is not None:
        imag_part = imag_part.reshape(shape)
    twist_cos, twist_sin = angle_tables(first, second, length)
    if axis == 1:
        twist_cos = twist_cos[:, :, None]
        twist_sin = twist_sin[:, :, None]
    twist_sin = direction * twist_sin
    if forward:
        real_part, imag_part = small_stage(real_part, imag_part, axis, direction)
        real_part, imag_part = complex_times(real_part, imag_part, twist_cos, twist_sin)
        real_part, imag_part = large_stage(real_part, imag_part, axis + 1, direction)
    else:
        real_part, imag_part = large_stage(real_part, imag_part, axis + 1, direction)
        real_part, imag_part = complex_times(real_part, imag_part, twist_cos, twist_sin)
        real_part, imag_part = small_stage(real_part, imag_part, axis, direction)
    return (real_part.reshape(outer), imag_part.reshape(outer))


def to_columns(real_part, imag_part):
    depth_real, depth_imag = factored(real_part, imag_part, 2, -1.0, True)
    rows = depth_real.shape[0]
    stacked = jnp.concatenate([depth_real, depth_imag], 0)
    moved = lax.all_to_all(stacked, "slab", split_axis=2, concat_axis=1, tiled=True)
    return factored(moved[:rows], moved[rows:], 1, -1.0, True)


def to_planes(real_part, imag_part):
    width_real, width_imag = factored(real_part, imag_part, 1, 1.0, False)
    rows = width_real.shape[0]
    stacked = jnp.concatenate([width_real, width_imag], 0)
    moved = lax.all_to_all(stacked, "slab", split_axis=1, concat_axis=2, tiled=True)
    return factored(moved[:rows], moved[rows:], 2, 1.0, False)


def pack_pairs(volume):
    return (volume[0::2], volume[1::2])


def unpack_pairs(real_part, imag_part):
    pairs, width, depth = real_part.shape
    return jnp.stack([real_part, imag_part], 1).reshape(2 * pairs, width, depth)


def general_shards(estimate, views, psf, pattern_mult, pattern_shift, interp):
    row_count, slab_width, depth = estimate.shape
    blocks = block_matrix(pattern_mult[0], pattern_shift[0], interp[0])
    block_count = depth // 128
    shaped = estimate.reshape(row_count, slab_width, block_count, 128)
    sampled = jnp.einsum("bij,yxbj->yxbi", blocks, shaped, precision=highest).reshape(
        row_count, slab_width, depth
    )
    packed_real, packed_imag = pack_pairs(sampled)
    packed_real = jnp.concatenate([packed_real, psf], 0)
    packed_imag = jnp.concatenate([packed_imag, jnp.zeros_like(psf)], 0)
    spectra_real, spectra_imag = to_columns(packed_real, packed_imag)
    scaling = 1.0 / (spectra_real.shape[1] * depth)
    transfer_real = spectra_real[-1:] * scaling
    transfer_imag = spectra_imag[-1:] * scaling
    spectra_real = spectra_real[:-1]
    spectra_imag = spectra_imag[:-1]
    filtered_real = spectra_real * transfer_real - spectra_imag * transfer_imag
    filtered_imag = spectra_real * transfer_imag + spectra_imag * transfer_real
    blurred = unpack_pairs(*to_planes(filtered_real, filtered_imag))
    quotient = views[0] / blurred
    packed_real, packed_imag = pack_pairs(quotient)
    spectra_real, spectra_imag = to_columns(packed_real, packed_imag)
    filtered_real = spectra_real * transfer_real + spectra_imag * transfer_imag
    filtered_imag = spectra_imag * transfer_real - spectra_real * transfer_imag
    smeared = unpack_pairs(*to_planes(filtered_real, filtered_imag))
    correction = jnp.einsum(
        "bij,yxbi->yxbj",
        blocks,
        smeared.reshape(row_count, slab_width, block_count, 128),
        precision=highest,
    ).reshape(row_count, slab_width, depth)
    log_terms = jnp.log(correction)
    view_count = lax.axis_size("view")
    summed = lax.psum(log_terms, "view")
    return estimate * jnp.exp(summed / view_count)


def swap_halves(joined):
    half = joined.shape[-1] // 2
    return jnp.concatenate([-joined[..., half:], joined[..., :half]], -1)


def lead_stage(joined, direction):
    count = joined.shape[0]
    parts = [joined[index] for index in range(count)]
    turned = [swap_halves(part) for part in parts]
    outs = []
    for out_index in range(count):
        total = None
        for in_index in range(count):
            cosine, sine = unit_root(in_index * out_index, count)
            sine = direction * sine
            for weight, term in ((cosine, parts[in_index]), (sine, turned[in_index])):
                if weight != 0.0:
                    term = weight * term
                    total = term if total is None else total + term
        outs.append(total)
    return jnp.stack(outs, 0)


def joined_twist(joined, length, direction, lanes):
    first, second = joined.shape[0], (joined.shape[-1] // 2 if lanes else joined.shape[2])
    cosine, sine = angle_tables(first, second, length)
    sine = direction * sine
    if lanes:
        cosine = jnp.concatenate([cosine, cosine], 1)[:, None, None, :]
        sine = jnp.concatenate([sine, sine], 1)[:, None, None, :]
    else:
        cosine = cosine[:, None, :, None]
        sine = sine[:, None, :, None]
    return joined * cosine + swap_halves(joined) * sine


def lane_stage(joined, direction):
    length = joined.shape[-1] // 2
    matrix = block_dft_matrix(length, direction)
    return jnp.einsum("...j,jn->...n", joined, matrix, precision=lax.Precision.HIGH)


def row_stage(joined, direction):
    length = joined.shape[2]
    cosine, sine = angle_tables(length, length, length)
    matrix = jnp.concatenate([cosine, direction * sine], 0)
    both = jnp.concatenate([joined, swap_halves(joined)], 2)
    return jnp.einsum("krjl,jm->krml", both, matrix, precision=lax.Precision.HIGH)


def depth_forward(joined, depth):
    joined = lead_stage(joined, -1.0)
    joined = joined_twist(joined, depth, -1.0, True)
    return lane_stage(joined, -1.0)


def depth_inverse(joined, depth):
    joined = lane_stage(joined, 1.0)
    joined = joined_twist(joined, depth, 1.0, True)
    return lead_stage(joined, 1.0)


def width_forward(joined, width):
    joined = lead_stage(joined, -1.0)
    joined = joined_twist(joined, width, -1.0, False)
    return row_stage(joined, -1.0)


def width_inverse(joined, width):
    joined = row_stage(joined, 1.0)
    joined = joined_twist(joined, width, 1.0, False)
    return lead_stage(joined, 1.0)


def joined_times(joined, transfer_real, transfer_imag):
    return joined * transfer_real + swap_halves(joined) * transfer_imag


def to_blocks(volume, block_count):
    rows, width, depth = volume.shape
    lanes = depth // block_count
    parity = [volume[0::2], volume[1::2]]
    return jnp.stack(
        [
            jnp.concatenate([part[:, :, block * lanes : (block + 1) * lanes] for part in parity], -1)
            for block in range(block_count)
        ],
        0,
    )


def from_blocks(blocked):
    block_count, pairs, width, lanes = blocked.shape
    half = lanes // 2
    parity = [
        jnp.concatenate([blocked[block, :, :, side * half : (side + 1) * half] for block in range(block_count)], -1)
        for side in range(2)
    ]
    return jnp.stack(parity, 1).reshape(2 * pairs, width, block_count * half)


def shards(estimate, views, psf, pattern_mult, pattern_shift, interp):
    row_count, slab_width, depth = estimate.shape
    slab_count = lax.axis_size("slab")
    block_count = depth // 128
    width = slab_width * slab_count
    if not (
        block_count == slab_count
        and slab_width == 128
        and width // 128 == slab_count
        and row_count % 2 == 0
    ):
        return general_shards(estimate, views, psf, pattern_mult, pattern_shift, interp)
    blocks = block_matrix(pattern_mult[0], pattern_shift[0], interp[0])
    empty = jnp.zeros_like(blocks)
    doubled = jnp.concatenate(
        [jnp.concatenate([blocks, empty], 2), jnp.concatenate([empty, blocks], 2)], 1
    )
    sampled = jnp.einsum(
        "apxl,aml->apxm", to_blocks(estimate, block_count), doubled, precision=highest
    )
    pairs = row_count // 2
    spread = psf.reshape(slab_width, block_count, 128).transpose(1, 0, 2)[:, None]
    spread = jnp.concatenate([spread, jnp.zeros_like(spread)], -1)
    def to_columns_blocked(planes):
        spectra = depth_forward(planes, depth)
        spectra = lax.all_to_all(spectra, "slab", split_axis=0, concat_axis=0, tiled=True)
        return width_forward(spectra, width)

    transfer = to_columns_blocked(spread) * (1.0 / (width * depth))
    spectra = to_columns_blocked(sampled)
    half = transfer.shape[-1] // 2
    transfer_real = jnp.concatenate([transfer[..., :half], transfer[..., :half]], -1)
    transfer_imag = jnp.concatenate([transfer[..., half:], transfer[..., half:]], -1)

    def convolve(spectra, transfer_imag):
        filtered = joined_times(spectra, transfer_real, transfer_imag)
        planes = width_inverse(filtered, width)
        planes = lax.all_to_all(planes, "slab", split_axis=0, concat_axis=0, tiled=True)
        return depth_inverse(planes, depth)

    blurred = convolve(spectra, transfer_imag)
    quotient = to_blocks(views[0], block_count) / blurred
    spectra = depth_forward(quotient, depth)
    spectra = lax.all_to_all(spectra, "slab", split_axis=0, concat_axis=0, tiled=True)
    spectra = width_forward(spectra, width)
    smeared = convolve(spectra, -transfer_imag)
    correction = jnp.einsum("apxm,aml->apxl", smeared, doubled, precision=highest)
    log_terms = from_blocks(jnp.log(correction))
    view_count = lax.axis_size("view")
    summed = lax.psum(log_terms, "view")
    return estimate * jnp.exp(summed / view_count)


def solution(mesh):
    placed = (
        P(None, "slab", None),
        P("view", None, "slab", None),
        P("view", "slab", None),
        P("view", None),
        P("view", None),
        P("view", None, None),
    )
    return jax.shard_map(
        shards, mesh=mesh, in_specs=placed, out_specs=P(None, "slab", None), check_vma=False
    )
```

```python
import math

import jax
import jax.numpy as jnp
from jax import lax
from jax.sharding import PartitionSpec as P

highest = lax.Precision.HIGHEST


def block_matrix(multiplier, shifting, weights):
    positions = jnp.arange(128, dtype=jnp.int32)
    first_col = ((2 * multiplier[:, None] + 1) * positions[None, :] + shifting[:, None]) % 128
    second_col = (first_col + 1) % 128
    columns = positions[None, None, :]
    lower = (columns == first_col[:, :, None]).astype(jnp.float32)
    upper = (columns == second_col[:, :, None]).astype(jnp.float32)
    return (1.0 - weights)[:, :, None] * lower + weights[:, :, None] * upper


def angle_tables(rows, cols, length):
    row_index = lax.iota(jnp.int32, rows)[:, None]
    col_index = lax.iota(jnp.int32, cols)[None, :]
    angles = (row_index * col_index % length).astype(jnp.float32) * (2.0 * math.pi / length)
    return (jnp.cos(angles), jnp.sin(angles))


def unit_root(numerator, length):
    angle = 2.0 * math.pi * numerator / length
    return (round(math.cos(angle), 15), round(math.sin(angle), 15))


def small_stage(real_part, imag_part, axis, direction):
    count = real_part.shape[axis]

    def part(array, index):
        return lax.index_in_dim(array, index, axis, keepdims=False)

    real_in = [part(real_part, index) for index in range(count)]
    imag_in = None if imag_part is None else [part(imag_part, index) for index in range(count)]
    real_out, imag_out = [], []
    for out_index in range(count):
        real_sum, imag_sum = None, None
        for in_index in range(count):
            cosine, sine = unit_root(in_index * out_index, count)
            sine = direction * sine
            terms_real = []
            terms_imag = []
            if cosine != 0.0:
                terms_real.append(cosine * real_in[in_index])
                if imag_in is not None:
                    terms_imag.append(cosine * imag_in[in_index])
            if sine != 0.0:
                terms_imag.append(sine * real_in[in_index])
                if imag_in is not None:
                    terms_real.append(-sine * imag_in[in_index])
            for term in terms_real:
                real_sum = term if real_sum is None else real_sum + term
            for term in terms_imag:
                imag_sum = term if imag_sum is None else imag_sum + term
        if imag_sum is None:
            imag_sum = jnp.zeros_like(real_sum)
        real_out.append(real_sum)
        imag_out.append(imag_sum)
    return (jnp.stack(real_out, axis), jnp.stack(imag_out, axis))


def complex_times(real_part, imag_part, cosine, sine_table):
    return (
        real_part * cosine - imag_part * sine_table,
        real_part * sine_table + imag_part * cosine,
    )


def block_dft_matrix(length, direction):
    cosine, sine = angle_tables(length, length, length)
    sine = direction * sine
    top = jnp.concatenate([cosine, sine], 1)
    bottom = jnp.concatenate([-sine, cosine], 1)
    return jnp.concatenate([top, bottom], 0)


def large_stage(real_part, imag_part, axis, direction):
    length = real_part.shape[axis]
    if imag_part is None:
        imag_part = jnp.zeros_like(real_part)
    joined = jnp.concatenate([real_part, imag_part], axis)
    matrix = block_dft_matrix(length, direction)
    if axis == joined.ndim - 1:
        out = jnp.einsum("...j,jn->...n", joined, matrix, precision=highest)
    else:
        out = jnp.einsum("rkjz,jn->rknz", joined, matrix, precision=highest)
    return (
        lax.slice_in_dim(out, 0, length, axis=axis),
        lax.slice_in_dim(out, length, 2 * length, axis=axis),
    )


def factored(real_part, imag_part, axis, direction, forward, want_imag=True):
    length = real_part.shape[axis]
    second = 128
    first = length // second
    outer = real_part.shape
    shape = outer[:axis] + (first, second) + outer[axis + 1 :]
    real_part = real_part.reshape(shape)
    if imag_part is not None:
        imag_part = imag_part.reshape(shape)
    twist_cos, twist_sin = angle_tables(first, second, length)
    if axis == 1:
        twist_cos = twist_cos[:, :, None]
        twist_sin = twist_sin[:, :, None]
    twist_sin = direction * twist_sin
    if forward:
        real_part, imag_part = small_stage(real_part, imag_part, axis, direction)
        real_part, imag_part = complex_times(real_part, imag_part, twist_cos, twist_sin)
        real_part, imag_part = large_stage(real_part, imag_part, axis + 1, direction)
    else:
        real_part, imag_part = large_stage(real_part, imag_part, axis + 1, direction)
        real_part, imag_part = complex_times(real_part, imag_part, twist_cos, twist_sin)
        real_part, imag_part = small_stage(real_part, imag_part, axis, direction)
    return (real_part.reshape(outer), imag_part.reshape(outer))


def to_columns(real_part, imag_part):
    depth_real, depth_imag = factored(real_part, imag_part, 2, -1.0, True)
    rows = depth_real.shape[0]
    stacked = jnp.concatenate([depth_real, depth_imag], 0)
    moved = lax.all_to_all(stacked, "slab", split_axis=2, concat_axis=1, tiled=True)
    return factored(moved[:rows], moved[rows:], 1, -1.0, True)


def to_planes(real_part, imag_part):
    width_real, width_imag = factored(real_part, imag_part, 1, 1.0, False)
    rows = width_real.shape[0]
    stacked = jnp.concatenate([width_real, width_imag], 0)
    moved = lax.all_to_all(stacked, "slab", split_axis=1, concat_axis=2, tiled=True)
    return factored(moved[:rows], moved[rows:], 2, 1.0, False)


def pack_pairs(volume):
    return (volume[0::2], volume[1::2])


def unpack_pairs(real_part, imag_part):
    pairs, width, depth = real_part.shape
    return jnp.stack([real_part, imag_part], 1).reshape(2 * pairs, width, depth)


def general_shards(estimate, views, psf, pattern_mult, pattern_shift, interp):
    row_count, slab_width, depth = estimate.shape
    blocks = block_matrix(pattern_mult[0], pattern_shift[0], interp[0])
    block_count = depth // 128
    shaped = estimate.reshape(row_count, slab_width, block_count, 128)
    sampled = jnp.einsum("bij,yxbj->yxbi", blocks, shaped, precision=highest).reshape(
        row_count, slab_width, depth
    )
    packed_real, packed_imag = pack_pairs(sampled)
    packed_real = jnp.concatenate([packed_real, psf], 0)
    packed_imag = jnp.concatenate([packed_imag, jnp.zeros_like(psf)], 0)
    spectra_real, spectra_imag = to_columns(packed_real, packed_imag)
    scaling = 1.0 / (spectra_real.shape[1] * depth)
    transfer_real = spectra_real[-1:] * scaling
    transfer_imag = spectra_imag[-1:] * scaling
    spectra_real = spectra_real[:-1]
    spectra_imag = spectra_imag[:-1]
    filtered_real = spectra_real * transfer_real - spectra_imag * transfer_imag
    filtered_imag = spectra_real * transfer_imag + spectra_imag * transfer_real
    blurred = unpack_pairs(*to_planes(filtered_real, filtered_imag))
    quotient = views[0] / blurred
    packed_real, packed_imag = pack_pairs(quotient)
    spectra_real, spectra_imag = to_columns(packed_real, packed_imag)
    filtered_real = spectra_real * transfer_real + spectra_imag * transfer_imag
    filtered_imag = spectra_imag * transfer_real - spectra_real * transfer_imag
    smeared = unpack_pairs(*to_planes(filtered_real, filtered_imag))
    correction = jnp.einsum(
        "bij,yxbi->yxbj",
        blocks,
        smeared.reshape(row_count, slab_width, block_count, 128),
        precision=highest,
    ).reshape(row_count, slab_width, depth)
    log_terms = jnp.log(correction)
    view_count = lax.axis_size("view")
    summed = lax.psum(log_terms, "view")
    return estimate * jnp.exp(summed / view_count)


def swap_halves(joined):
    half = joined.shape[-1] // 2
    return jnp.concatenate([-joined[..., half:], joined[..., :half]], -1)


def lead_stage(joined, direction):
    count = joined.shape[0]
    parts = [joined[index] for index in range(count)]
    turned = [swap_halves(part) for part in parts]
    outs = []
    for out_index in range(count):
        total = None
        for in_index in range(count):
            cosine, sine = unit_root(in_index * out_index, count)
            sine = direction * sine
            for weight, term in ((cosine, parts[in_index]), (sine, turned[in_index])):
                if weight != 0.0:
                    term = weight * term
                    total = term if total is None else total + term
        outs.append(total)
    return jnp.stack(outs, 0)


def joined_twist(joined, length, direction, lanes):
    first, second = joined.shape[0], (joined.shape[-1] // 2 if lanes else joined.shape[2])
    cosine, sine = angle_tables(first, second, length)
    sine = direction * sine
    if lanes:
        cosine = jnp.concatenate([cosine, cosine], 1)[:, None, None, :]
        sine = jnp.concatenate([sine, sine], 1)[:, None, None, :]
    else:
        cosine = cosine[:, None, :, None]
        sine = sine[:, None, :, None]
    return joined * cosine + swap_halves(joined) * sine


def lane_stage(joined, direction):
    length = joined.shape[-1] // 2
    matrix = block_dft_matrix(length, direction)
    return jnp.einsum("...j,jn->...n", joined, matrix, precision=lax.Precision.HIGH)


def row_stage(joined, direction):
    length = joined.shape[2]
    cosine, sine = angle_tables(length, length, length)
    matrix = jnp.concatenate([cosine, direction * sine], 0)
    both = jnp.concatenate([joined, swap_halves(joined)], 2)
    return jnp.einsum("krjl,jm->krml", both, matrix, precision=lax.Precision.HIGH)


def depth_forward(joined, depth):
    joined = lead_stage(joined, -1.0)
    joined = joined_twist(joined, depth, -1.0, True)
    return lane_stage(joined, -1.0)


def depth_inverse(joined, depth):
    joined = lane_stage(joined, 1.0)
    joined = joined_twist(joined, depth, 1.0, True)
    return lead_stage(joined, 1.0)


def width_forward(joined, width):
    joined = lead_stage(joined, -1.0)
    joined = joined_twist(joined, width, -1.0, False)
    return row_stage(joined, -1.0)


def width_inverse(joined, width):
    joined = row_stage(joined, 1.0)
    joined = joined_twist(joined, width, 1.0, False)
    return lead_stage(joined, 1.0)


def joined_times(joined, transfer_real, transfer_imag):
    return joined * transfer_real + swap_halves(joined) * transfer_imag


def to_blocks(volume, block_count):
    rows, width, depth = volume.shape
    lanes = depth // block_count
    parity = [volume[0::2], volume[1::2]]
    return jnp.stack(
        [
            jnp.concatenate([part[:, :, block * lanes : (block + 1) * lanes] for part in parity], -1)
            for block in range(block_count)
        ],
        0,
    )


def from_blocks(blocked):
    block_count, pairs, width, lanes = blocked.shape
    half = lanes // 2
    parity = [
        jnp.concatenate([blocked[block, :, :, side * half : (side + 1) * half] for block in range(block_count)], -1)
        for side in range(2)
    ]
    return jnp.stack(parity, 1).reshape(2 * pairs, width, block_count * half)


def shards(estimate, views, psf, pattern_mult, pattern_shift, interp):
    row_count, slab_width, depth = estimate.shape
    slab_count = lax.axis_size("slab")
    block_count = depth // 128
    width = slab_width * slab_count
    if not (
        block_count == slab_count
        and slab_width == 128
        and width // 128 == slab_count
        and row_count % 2 == 0
    ):
        return general_shards(estimate, views, psf, pattern_mult, pattern_shift, interp)
    blocks = block_matrix(pattern_mult[0], pattern_shift[0], interp[0])
    empty = jnp.zeros_like(blocks)
    doubled = jnp.concatenate(
        [jnp.concatenate([blocks, empty], 2), jnp.concatenate([empty, blocks], 2)], 1
    )
    sampled = jnp.einsum(
        "apxl,aml->apxm", to_blocks(estimate, block_count), doubled, precision=highest
    )
    pairs = row_count // 2
    spread = psf.reshape(slab_width, block_count, 128).transpose(1, 0, 2)[:, None]
    spread = jnp.concatenate([spread, jnp.zeros_like(spread)], -1)
    def to_columns_blocked(planes):
        spectra = depth_forward(planes, depth)
        spectra = lax.all_to_all(spectra, "slab", split_axis=0, concat_axis=0, tiled=True)
        return width_forward(spectra, width)

    transfer = to_columns_blocked(spread) * (1.0 / (width * depth))
    spectra = to_columns_blocked(sampled)
    half = transfer.shape[-1] // 2
    transfer_real = jnp.concatenate([transfer[..., :half], transfer[..., :half]], -1)
    transfer_imag = jnp.concatenate([transfer[..., half:], transfer[..., half:]], -1)

    def convolve(spectra, transfer_imag):
        filtered = joined_times(spectra, transfer_real, transfer_imag)
        planes = width_inverse(filtered, width)
        planes = lax.all_to_all(planes, "slab", split_axis=0, concat_axis=0, tiled=True)
        return depth_inverse(planes, depth)

    blurred = convolve(spectra, transfer_imag)
    quotient = to_blocks(views[0], block_count) / blurred
    spectra = depth_forward(quotient, depth)
    spectra = lax.all_to_all(spectra, "slab", split_axis=0, concat_axis=0, tiled=True)
    spectra = width_forward(spectra, width)
    smeared = convolve(spectra, -transfer_imag)
    correction = jnp.einsum("apxm,aml->apxl", smeared, doubled, precision=highest)
    log_terms = jnp.log(correction)
    view_count = lax.axis_size("view")
    summed = from_blocks(lax.psum(log_terms, "view"))
    return estimate * jnp.exp(summed / view_count)


def solution(mesh):
    placed = (
        P(None, "slab", None),
        P("view", None, "slab", None),
        P("view", "slab", None),
        P("view", None),
        P("view", None),
        P("view", None, None),
    )
    return jax.shard_map(
        shards, mesh=mesh, in_specs=placed, out_specs=P(None, "slab", None), check_vma=False
    )
```

```python
import math

import jax
import jax.numpy as jnp
from jax import lax
from jax.sharding import PartitionSpec as P

highest = lax.Precision.HIGHEST


def block_matrix(multiplier, shifting, weights):
    positions = jnp.arange(128, dtype=jnp.int32)
    first_col = ((2 * multiplier[:, None] + 1) * positions[None, :] + shifting[:, None]) % 128
    second_col = (first_col + 1) % 128
    columns = positions[None, None, :]
    lower = (columns == first_col[:, :, None]).astype(jnp.float32)
    upper = (columns == second_col[:, :, None]).astype(jnp.float32)
    return (1.0 - weights)[:, :, None] * lower + weights[:, :, None] * upper


def angle_tables(rows, cols, length):
    row_index = lax.iota(jnp.int32, rows)[:, None]
    col_index = lax.iota(jnp.int32, cols)[None, :]
    angles = (row_index * col_index % length).astype(jnp.float32) * (2.0 * math.pi / length)
    return (jnp.cos(angles), jnp.sin(angles))


def unit_root(numerator, length):
    angle = 2.0 * math.pi * numerator / length
    return (round(math.cos(angle), 15), round(math.sin(angle), 15))


def small_stage(real_part, imag_part, axis, direction):
    count = real_part.shape[axis]

    def part(array, index):
        return lax.index_in_dim(array, index, axis, keepdims=False)

    real_in = [part(real_part, index) for index in range(count)]
    imag_in = None if imag_part is None else [part(imag_part, index) for index in range(count)]
    real_out, imag_out = [], []
    for out_index in range(count):
        real_sum, imag_sum = None, None
        for in_index in range(count):
            cosine, sine = unit_root(in_index * out_index, count)
            sine = direction * sine
            terms_real = []
            terms_imag = []
            if cosine != 0.0:
                terms_real.append(cosine * real_in[in_index])
                if imag_in is not None:
                    terms_imag.append(cosine * imag_in[in_index])
            if sine != 0.0:
                terms_imag.append(sine * real_in[in_index])
                if imag_in is not None:
                    terms_real.append(-sine * imag_in[in_index])
            for term in terms_real:
                real_sum = term if real_sum is None else real_sum + term
            for term in terms_imag:
                imag_sum = term if imag_sum is None else imag_sum + term
        if imag_sum is None:
            imag_sum = jnp.zeros_like(real_sum)
        real_out.append(real_sum)
        imag_out.append(imag_sum)
    return (jnp.stack(real_out, axis), jnp.stack(imag_out, axis))


def complex_times(real_part, imag_part, cosine, sine_table):
    return (
        real_part * cosine - imag_part * sine_table,
        real_part * sine_table + imag_part * cosine,
    )


def block_dft_matrix(length, direction):
    cosine, sine = angle_tables(length, length, length)
    sine = direction * sine
    top = jnp.concatenate([cosine, sine], 1)
    bottom = jnp.concatenate([-sine, cosine], 1)
    return jnp.concatenate([top, bottom], 0)


def large_stage(real_part, imag_part, axis, direction):
    length = real_part.shape[axis]
    if imag_part is None:
        imag_part = jnp.zeros_like(real_part)
    joined = jnp.concatenate([real_part, imag_part], axis)
    matrix = block_dft_matrix(length, direction)
    if axis == joined.ndim - 1:
        out = jnp.einsum("...j,jn->...n", joined, matrix, precision=highest)
    else:
        out = jnp.einsum("rkjz,jn->rknz", joined, matrix, precision=highest)
    return (
        lax.slice_in_dim(out, 0, length, axis=axis),
        lax.slice_in_dim(out, length, 2 * length, axis=axis),
    )


def factored(real_part, imag_part, axis, direction, forward, want_imag=True):
    length = real_part.shape[axis]
    second = 128
    first = length // second
    outer = real_part.shape
    shape = outer[:axis] + (first, second) + outer[axis + 1 :]
    real_part = real_part.reshape(shape)
    if imag_part is not None:
        imag_part = imag_part.reshape(shape)
    twist_cos, twist_sin = angle_tables(first, second, length)
    if axis == 1:
        twist_cos = twist_cos[:, :, None]
        twist_sin = twist_sin[:, :, None]
    twist_sin = direction * twist_sin
    if forward:
        real_part, imag_part = small_stage(real_part, imag_part, axis, direction)
        real_part, imag_part = complex_times(real_part, imag_part, twist_cos, twist_sin)
        real_part, imag_part = large_stage(real_part, imag_part, axis + 1, direction)
    else:
        real_part, imag_part = large_stage(real_part, imag_part, axis + 1, direction)
        real_part, imag_part = complex_times(real_part, imag_part, twist_cos, twist_sin)
        real_part, imag_part = small_stage(real_part, imag_part, axis, direction)
    return (real_part.reshape(outer), imag_part.reshape(outer))


def to_columns(real_part, imag_part):
    depth_real, depth_imag = factored(real_part, imag_part, 2, -1.0, True)
    rows = depth_real.shape[0]
    stacked = jnp.concatenate([depth_real, depth_imag], 0)
    moved = lax.all_to_all(stacked, "slab", split_axis=2, concat_axis=1, tiled=True)
    return factored(moved[:rows], moved[rows:], 1, -1.0, True)


def to_planes(real_part, imag_part):
    width_real, width_imag = factored(real_part, imag_part, 1, 1.0, False)
    rows = width_real.shape[0]
    stacked = jnp.concatenate([width_real, width_imag], 0)
    moved = lax.all_to_all(stacked, "slab", split_axis=1, concat_axis=2, tiled=True)
    return factored(moved[:rows], moved[rows:], 2, 1.0, False)


def pack_pairs(volume):
    return (volume[0::2], volume[1::2])


def unpack_pairs(real_part, imag_part):
    pairs, width, depth = real_part.shape
    return jnp.stack([real_part, imag_part], 1).reshape(2 * pairs, width, depth)


def general_shards(estimate, views, psf, pattern_mult, pattern_shift, interp):
    row_count, slab_width, depth = estimate.shape
    blocks = block_matrix(pattern_mult[0], pattern_shift[0], interp[0])
    block_count = depth // 128
    shaped = estimate.reshape(row_count, slab_width, block_count, 128)
    sampled = jnp.einsum("bij,yxbj->yxbi", blocks, shaped, precision=highest).reshape(
        row_count, slab_width, depth
    )
    packed_real, packed_imag = pack_pairs(sampled)
    packed_real = jnp.concatenate([packed_real, psf], 0)
    packed_imag = jnp.concatenate([packed_imag, jnp.zeros_like(psf)], 0)
    spectra_real, spectra_imag = to_columns(packed_real, packed_imag)
    scaling = 1.0 / (spectra_real.shape[1] * depth)
    transfer_real = spectra_real[-1:] * scaling
    transfer_imag = spectra_imag[-1:] * scaling
    spectra_real = spectra_real[:-1]
    spectra_imag = spectra_imag[:-1]
    filtered_real = spectra_real * transfer_real - spectra_imag * transfer_imag
    filtered_imag = spectra_real * transfer_imag + spectra_imag * transfer_real
    blurred = unpack_pairs(*to_planes(filtered_real, filtered_imag))
    quotient = views[0] / blurred
    packed_real, packed_imag = pack_pairs(quotient)
    spectra_real, spectra_imag = to_columns(packed_real, packed_imag)
    filtered_real = spectra_real * transfer_real + spectra_imag * transfer_imag
    filtered_imag = spectra_imag * transfer_real - spectra_real * transfer_imag
    smeared = unpack_pairs(*to_planes(filtered_real, filtered_imag))
    correction = jnp.einsum(
        "bij,yxbi->yxbj",
        blocks,
        smeared.reshape(row_count, slab_width, block_count, 128),
        precision=highest,
    ).reshape(row_count, slab_width, depth)
    log_terms = jnp.log(correction)
    view_count = lax.axis_size("view")
    summed = lax.psum(log_terms, "view")
    return estimate * jnp.exp(summed / view_count)


def swap_halves(joined):
    half = joined.shape[-1] // 2
    return jnp.concatenate([-joined[..., half:], joined[..., :half]], -1)


def lead_stage(joined, direction):
    count = joined.shape[0]
    parts = [joined[index] for index in range(count)]
    turned = [swap_halves(part) for part in parts]
    outs = []
    for out_index in range(count):
        total = None
        for in_index in range(count):
            cosine, sine = unit_root(in_index * out_index, count)
            sine = direction * sine
            for weight, term in ((cosine, parts[in_index]), (sine, turned[in_index])):
                if weight != 0.0:
                    term = weight * term
                    total = term if total is None else total + term
        outs.append(total)
    return jnp.stack(outs, 0)


def joined_twist(joined, length, direction, lanes):
    first, second = joined.shape[0], (joined.shape[-1] // 2 if lanes else joined.shape[2])
    cosine, sine = angle_tables(first, second, length)
    sine = direction * sine
    if lanes:
        cosine = jnp.concatenate([cosine, cosine], 1)[:, None, None, :]
        sine = jnp.concatenate([sine, sine], 1)[:, None, None, :]
    else:
        cosine = cosine[:, None, :, None]
        sine = sine[:, None, :, None]
    return joined * cosine + swap_halves(joined) * sine


def lane_stage(joined, direction):
    length = joined.shape[-1] // 2
    matrix = block_dft_matrix(length, direction)
    return jnp.einsum("...j,jn->...n", joined, matrix, precision=lax.Precision.HIGH)


def row_stage(joined, direction):
    length = joined.shape[2]
    cosine, sine = angle_tables(length, length, length)
    matrix = jnp.concatenate([cosine, direction * sine], 0)
    both = jnp.concatenate([joined, swap_halves(joined)], 2)
    return jnp.einsum("krjl,jm->krml", both, matrix, precision=lax.Precision.HIGH)


def depth_forward(joined, depth):
    joined = lead_stage(joined, -1.0)
    joined = joined_twist(joined, depth, -1.0, True)
    return lane_stage(joined, -1.0)


def depth_inverse(joined, depth):
    joined = lane_stage(joined, 1.0)
    joined = joined_twist(joined, depth, 1.0, True)
    return lead_stage(joined, 1.0)


def width_forward(joined, width):
    joined = lead_stage(joined, -1.0)
    joined = joined_twist(joined, width, -1.0, False)
    return row_stage(joined, -1.0)


def width_inverse(joined, width):
    joined = row_stage(joined, 1.0)
    joined = joined_twist(joined, width, 1.0, False)
    return lead_stage(joined, 1.0)


def joined_times(joined, transfer_real, transfer_imag):
    return joined * transfer_real + swap_halves(joined) * transfer_imag


def to_blocks(volume, block_count):
    rows, width, depth = volume.shape
    lanes = depth // block_count
    parity = [volume[0::2], volume[1::2]]
    return jnp.stack(
        [
            jnp.concatenate([part[:, :, block * lanes : (block + 1) * lanes] for part in parity], -1)
            for block in range(block_count)
        ],
        0,
    )


def from_blocks(blocked):
    block_count, pairs, width, lanes = blocked.shape
    half = lanes // 2
    parity = [
        jnp.concatenate([blocked[block, :, :, side * half : (side + 1) * half] for block in range(block_count)], -1)
        for side in range(2)
    ]
    return jnp.stack(parity, 1).reshape(2 * pairs, width, block_count * half)


def shards(estimate, views, psf, pattern_mult, pattern_shift, interp):
    row_count, slab_width, depth = estimate.shape
    slab_count = lax.axis_size("slab")
    block_count = depth // 128
    width = slab_width * slab_count
    if not (
        block_count == slab_count
        and slab_width == 128
        and width // 128 == slab_count
        and row_count % 2 == 0
    ):
        return general_shards(estimate, views, psf, pattern_mult, pattern_shift, interp)
    blocks = block_matrix(pattern_mult[0], pattern_shift[0], interp[0])
    empty = jnp.zeros_like(blocks)
    doubled = jnp.concatenate(
        [jnp.concatenate([blocks, empty], 2), jnp.concatenate([empty, blocks], 2)], 1
    )
    sampled = jnp.einsum(
        "apxl,aml->apxm", to_blocks(estimate, block_count), doubled, precision=lax.Precision.HIGH
    )
    pairs = row_count // 2
    spread = psf.reshape(slab_width, block_count, 128).transpose(1, 0, 2)[:, None]
    spread = jnp.concatenate([spread, jnp.zeros_like(spread)], -1)
    def to_columns_blocked(planes):
        spectra = depth_forward(planes, depth)
        spectra = lax.all_to_all(spectra, "slab", split_axis=0, concat_axis=0, tiled=True)
        return width_forward(spectra, width)

    transfer = to_columns_blocked(spread) * (1.0 / (width * depth))
    spectra = to_columns_blocked(sampled)
    half = transfer.shape[-1] // 2
    transfer_real = jnp.concatenate([transfer[..., :half], transfer[..., :half]], -1)
    transfer_imag = jnp.concatenate([transfer[..., half:], transfer[..., half:]], -1)

    def convolve(spectra, transfer_imag):
        filtered = joined_times(spectra, transfer_real, transfer_imag)
        planes = width_inverse(filtered, width)
        planes = lax.all_to_all(planes, "slab", split_axis=0, concat_axis=0, tiled=True)
        return depth_inverse(planes, depth)

    blurred = convolve(spectra, transfer_imag)
    quotient = to_blocks(views[0], block_count) / blurred
    spectra = depth_forward(quotient, depth)
    spectra = lax.all_to_all(spectra, "slab", split_axis=0, concat_axis=0, tiled=True)
    spectra = width_forward(spectra, width)
    smeared = convolve(spectra, -transfer_imag)
    correction = jnp.einsum("apxm,aml->apxl", smeared, doubled, precision=lax.Precision.HIGH)
    log_terms = from_blocks(jnp.log(correction))
    view_count = lax.axis_size("view")
    summed = lax.psum(log_terms, "view")
    return estimate * jnp.exp(summed / view_count)


def solution(mesh):
    placed = (
        P(None, "slab", None),
        P("view", None, "slab", None),
        P("view", "slab", None),
        P("view", None),
        P("view", None),
        P("view", None, None),
    )
    return jax.shard_map(
        shards, mesh=mesh, in_specs=placed, out_specs=P(None, "slab", None), check_vma=False
    )
```

```python
import math

import jax
import jax.numpy as jnp
from jax import lax
from jax.sharding import PartitionSpec as P

highest = lax.Precision.HIGHEST


def block_matrix(multiplier, shifting, weights):
    positions = jnp.arange(128, dtype=jnp.int32)
    first_col = ((2 * multiplier[:, None] + 1) * positions[None, :] + shifting[:, None]) % 128
    second_col = (first_col + 1) % 128
    columns = positions[None, None, :]
    lower = (columns == first_col[:, :, None]).astype(jnp.float32)
    upper = (columns == second_col[:, :, None]).astype(jnp.float32)
    return (1.0 - weights)[:, :, None] * lower + weights[:, :, None] * upper


def angle_tables(rows, cols, length):
    row_index = lax.iota(jnp.int32, rows)[:, None]
    col_index = lax.iota(jnp.int32, cols)[None, :]
    angles = (row_index * col_index % length).astype(jnp.float32) * (2.0 * math.pi / length)
    return (jnp.cos(angles), jnp.sin(angles))


def unit_root(numerator, length):
    angle = 2.0 * math.pi * numerator / length
    return (round(math.cos(angle), 15), round(math.sin(angle), 15))


def small_stage(real_part, imag_part, axis, direction):
    count = real_part.shape[axis]

    def part(array, index):
        return lax.index_in_dim(array, index, axis, keepdims=False)

    real_in = [part(real_part, index) for index in range(count)]
    imag_in = None if imag_part is None else [part(imag_part, index) for index in range(count)]
    real_out, imag_out = [], []
    for out_index in range(count):
        real_sum, imag_sum = None, None
        for in_index in range(count):
            cosine, sine = unit_root(in_index * out_index, count)
            sine = direction * sine
            terms_real = []
            terms_imag = []
            if cosine != 0.0:
                terms_real.append(cosine * real_in[in_index])
                if imag_in is not None:
                    terms_imag.append(cosine * imag_in[in_index])
            if sine != 0.0:
                terms_imag.append(sine * real_in[in_index])
                if imag_in is not None:
                    terms_real.append(-sine * imag_in[in_index])
            for term in terms_real:
                real_sum = term if real_sum is None else real_sum + term
            for term in terms_imag:
                imag_sum = term if imag_sum is None else imag_sum + term
        if imag_sum is None:
            imag_sum = jnp.zeros_like(real_sum)
        real_out.append(real_sum)
        imag_out.append(imag_sum)
    return (jnp.stack(real_out, axis), jnp.stack(imag_out, axis))


def complex_times(real_part, imag_part, cosine, sine_table):
    return (
        real_part * cosine - imag_part * sine_table,
        real_part * sine_table + imag_part * cosine,
    )


def block_dft_matrix(length, direction):
    cosine, sine = angle_tables(length, length, length)
    sine = direction * sine
    top = jnp.concatenate([cosine, sine], 1)
    bottom = jnp.concatenate([-sine, cosine], 1)
    return jnp.concatenate([top, bottom], 0)


def large_stage(real_part, imag_part, axis, direction):
    length = real_part.shape[axis]
    if imag_part is None:
        imag_part = jnp.zeros_like(real_part)
    joined = jnp.concatenate([real_part, imag_part], axis)
    matrix = block_dft_matrix(length, direction)
    if axis == joined.ndim - 1:
        out = jnp.einsum("...j,jn->...n", joined, matrix, precision=highest)
    else:
        out = jnp.einsum("rkjz,jn->rknz", joined, matrix, precision=highest)
    return (
        lax.slice_in_dim(out, 0, length, axis=axis),
        lax.slice_in_dim(out, length, 2 * length, axis=axis),
    )


def factored(real_part, imag_part, axis, direction, forward, want_imag=True):
    length = real_part.shape[axis]
    second = 128
    first = length // second
    outer = real_part.shape
    shape = outer[:axis] + (first, second) + outer[axis + 1 :]
    real_part = real_part.reshape(shape)
    if imag_part is not None:
        imag_part = imag_part.reshape(shape)
    twist_cos, twist_sin = angle_tables(first, second, length)
    if axis == 1:
        twist_cos = twist_cos[:, :, None]
        twist_sin = twist_sin[:, :, None]
    twist_sin = direction * twist_sin
    if forward:
        real_part, imag_part = small_stage(real_part, imag_part, axis, direction)
        real_part, imag_part = complex_times(real_part, imag_part, twist_cos, twist_sin)
        real_part, imag_part = large_stage(real_part, imag_part, axis + 1, direction)
    else:
        real_part, imag_part = large_stage(real_part, imag_part, axis + 1, direction)
        real_part, imag_part = complex_times(real_part, imag_part, twist_cos, twist_sin)
        real_part, imag_part = small_stage(real_part, imag_part, axis, direction)
    return (real_part.reshape(outer), imag_part.reshape(outer))


def to_columns(real_part, imag_part):
    depth_real, depth_imag = factored(real_part, imag_part, 2, -1.0, True)
    rows = depth_real.shape[0]
    stacked = jnp.concatenate([depth_real, depth_imag], 0)
    moved = lax.all_to_all(stacked, "slab", split_axis=2, concat_axis=1, tiled=True)
    return factored(moved[:rows], moved[rows:], 1, -1.0, True)


def to_planes(real_part, imag_part):
    width_real, width_imag = factored(real_part, imag_part, 1, 1.0, False)
    rows = width_real.shape[0]
    stacked = jnp.concatenate([width_real, width_imag], 0)
    moved = lax.all_to_all(stacked, "slab", split_axis=1, concat_axis=2, tiled=True)
    return factored(moved[:rows], moved[rows:], 2, 1.0, False)


def pack_pairs(volume):
    return (volume[0::2], volume[1::2])


def unpack_pairs(real_part, imag_part):
    pairs, width, depth = real_part.shape
    return jnp.stack([real_part, imag_part], 1).reshape(2 * pairs, width, depth)


def general_shards(estimate, views, psf, pattern_mult, pattern_shift, interp):
    row_count, slab_width, depth = estimate.shape
    blocks = block_matrix(pattern_mult[0], pattern_shift[0], interp[0])
    block_count = depth // 128
    shaped = estimate.reshape(row_count, slab_width, block_count, 128)
    sampled = jnp.einsum("bij,yxbj->yxbi", blocks, shaped, precision=highest).reshape(
        row_count, slab_width, depth
    )
    packed_real, packed_imag = pack_pairs(sampled)
    packed_real = jnp.concatenate([packed_real, psf], 0)
    packed_imag = jnp.concatenate([packed_imag, jnp.zeros_like(psf)], 0)
    spectra_real, spectra_imag = to_columns(packed_real, packed_imag)
    scaling = 1.0 / (spectra_real.shape[1] * depth)
    transfer_real = spectra_real[-1:] * scaling
    transfer_imag = spectra_imag[-1:] * scaling
    spectra_real = spectra_real[:-1]
    spectra_imag = spectra_imag[:-1]
    filtered_real = spectra_real * transfer_real - spectra_imag * transfer_imag
    filtered_imag = spectra_real * transfer_imag + spectra_imag * transfer_real
    blurred = unpack_pairs(*to_planes(filtered_real, filtered_imag))
    quotient = views[0] / blurred
    packed_real, packed_imag = pack_pairs(quotient)
    spectra_real, spectra_imag = to_columns(packed_real, packed_imag)
    filtered_real = spectra_real * transfer_real + spectra_imag * transfer_imag
    filtered_imag = spectra_imag * transfer_real - spectra_real * transfer_imag
    smeared = unpack_pairs(*to_planes(filtered_real, filtered_imag))
    correction = jnp.einsum(
        "bij,yxbi->yxbj",
        blocks,
        smeared.reshape(row_count, slab_width, block_count, 128),
        precision=highest,
    ).reshape(row_count, slab_width, depth)
    log_terms = jnp.log(correction)
    view_count = lax.axis_size("view")
    summed = lax.psum(log_terms, "view")
    return estimate * jnp.exp(summed / view_count)


def swap_halves(joined):
    half = joined.shape[-1] // 2
    return jnp.concatenate([-joined[..., half:], joined[..., :half]], -1)


def butterflies(parts, direction, turn):
    count = len(parts)
    if count == 1:
        return parts
    even = butterflies(parts[0::2], direction, turn)
    odd = butterflies(parts[1::2], direction, turn)
    out = [None] * count
    for index in range(count // 2):
        cosine, sine = unit_root(index, count)
        sine = direction * sine
        value = odd[index]
        if sine == 0.0:
            rotated = value if cosine > 0 else -value
        elif cosine == 0.0:
            rotated = turn(value) if sine > 0 else -turn(value)
        else:
            rotated = cosine * value + sine * turn(value)
        out[index] = even[index] + rotated
        out[index + count // 2] = even[index] - rotated
    return out


def lead_stage(joined, direction):
    count = joined.shape[0]
    parts = [joined[index] for index in range(count)]
    return jnp.stack(butterflies(parts, direction, swap_halves), 0)


def joined_twist(joined, length, direction, lanes):
    first, second = joined.shape[0], (joined.shape[-1] // 2 if lanes else joined.shape[2])
    cosine, sine = angle_tables(first, second, length)
    sine = direction * sine
    if lanes:
        cosine = jnp.concatenate([cosine, cosine], 1)[:, None, None, :]
        sine = jnp.concatenate([sine, sine], 1)[:, None, None, :]
    else:
        cosine = cosine[:, None, :, None]
        sine = sine[:, None, :, None]
    return joined * cosine + swap_halves(joined) * sine


def lane_stage(joined, direction):
    length = joined.shape[-1] // 2
    matrix = block_dft_matrix(length, direction)
    return jnp.einsum("...j,jn->...n", joined, matrix, precision=lax.Precision.HIGH)


def row_stage(joined, direction):
    length = joined.shape[2]
    cosine, sine = angle_tables(length, length, length)
    matrix = jnp.concatenate([cosine, direction * sine], 0)
    both = jnp.concatenate([joined, swap_halves(joined)], 2)
    return jnp.einsum("krjl,jm->krml", both, matrix, precision=lax.Precision.HIGH)


def depth_forward(joined, depth):
    joined = lead_stage(joined, -1.0)
    joined = joined_twist(joined, depth, -1.0, True)
    return lane_stage(joined, -1.0)


def depth_inverse(joined, depth):
    joined = lane_stage(joined, 1.0)
    joined = joined_twist(joined, depth, 1.0, True)
    return lead_stage(joined, 1.0)


def width_forward(joined, width):
    joined = lead_stage(joined, -1.0)
    joined = joined_twist(joined, width, -1.0, False)
    return row_stage(joined, -1.0)


def width_inverse(joined, width):
    joined = row_stage(joined, 1.0)
    joined = joined_twist(joined, width, 1.0, False)
    return lead_stage(joined, 1.0)


def joined_times(joined, transfer_real, transfer_imag):
    return joined * transfer_real + swap_halves(joined) * transfer_imag


def to_blocks(volume, block_count):
    rows, width, depth = volume.shape
    lanes = depth // block_count
    parity = [volume[0::2], volume[1::2]]
    return jnp.stack(
        [
            jnp.concatenate([part[:, :, block * lanes : (block + 1) * lanes] for part in parity], -1)
            for block in range(block_count)
        ],
        0,
    )


def from_blocks(blocked):
    block_count, pairs, width, lanes = blocked.shape
    half = lanes // 2
    parity = [
        jnp.concatenate([blocked[block, :, :, side * half : (side + 1) * half] for block in range(block_count)], -1)
        for side in range(2)
    ]
    return jnp.stack(parity, 1).reshape(2 * pairs, width, block_count * half)


def shards(estimate, views, psf, pattern_mult, pattern_shift, interp):
    row_count, slab_width, depth = estimate.shape
    slab_count = lax.axis_size("slab")
    block_count = depth // 128
    width = slab_width * slab_count
    if not (
        block_count == slab_count
        and slab_width == 128
        and width // 128 == slab_count
        and row_count % 2 == 0
    ):
        return general_shards(estimate, views, psf, pattern_mult, pattern_shift, interp)
    blocks = block_matrix(pattern_mult[0], pattern_shift[0], interp[0])
    empty = jnp.zeros_like(blocks)
    doubled = jnp.concatenate(
        [jnp.concatenate([blocks, empty], 2), jnp.concatenate([empty, blocks], 2)], 1
    )
    sampled = jnp.einsum(
        "apxl,aml->apxm", to_blocks(estimate, block_count), doubled, precision=lax.Precision.HIGH
    )
    pairs = row_count // 2
    spread = psf.reshape(slab_width, block_count, 128).transpose(1, 0, 2)[:, None]
    spread = jnp.concatenate([spread, jnp.zeros_like(spread)], -1)
    def to_columns_blocked(planes):
        spectra = depth_forward(planes, depth)
        spectra = lax.all_to_all(spectra, "slab", split_axis=0, concat_axis=0, tiled=True)
        return width_forward(spectra, width)

    transfer = to_columns_blocked(spread) * (1.0 / (width * depth))
    spectra = to_columns_blocked(sampled)
    half = transfer.shape[-1] // 2
    transfer_real = jnp.concatenate([transfer[..., :half], transfer[..., :half]], -1)
    transfer_imag = jnp.concatenate([transfer[..., half:], transfer[..., half:]], -1)

    def convolve(spectra, transfer_imag):
        filtered = joined_times(spectra, transfer_real, transfer_imag)
        planes = width_inverse(filtered, width)
        planes = lax.all_to_all(planes, "slab", split_axis=0, concat_axis=0, tiled=True)
        return depth_inverse(planes, depth)

    blurred = convolve(spectra, transfer_imag)
    quotient = to_blocks(views[0], block_count) / blurred
    spectra = depth_forward(quotient, depth)
    spectra = lax.all_to_all(spectra, "slab", split_axis=0, concat_axis=0, tiled=True)
    spectra = width_forward(spectra, width)
    smeared = convolve(spectra, -transfer_imag)
    correction = jnp.einsum("apxm,aml->apxl", smeared, doubled, precision=lax.Precision.HIGH)
    log_terms = from_blocks(jnp.log(correction))
    view_count = lax.axis_size("view")
    summed = lax.psum(log_terms, "view")
    return estimate * jnp.exp(summed / view_count)


def solution(mesh):
    placed = (
        P(None, "slab", None),
        P("view", None, "slab", None),
        P("view", "slab", None),
        P("view", None),
        P("view", None),
        P("view", None, None),
    )
    return jax.shard_map(
        shards, mesh=mesh, in_specs=placed, out_specs=P(None, "slab", None), check_vma=False
    )
```

```python
import math

import jax
import jax.numpy as jnp
from jax import lax
from jax.sharding import PartitionSpec as P

highest = lax.Precision.HIGHEST


def block_matrix(multiplier, shifting, weights):
    positions = jnp.arange(128, dtype=jnp.int32)
    first_col = ((2 * multiplier[:, None] + 1) * positions[None, :] + shifting[:, None]) % 128
    second_col = (first_col + 1) % 128
    columns = positions[None, None, :]
    lower = (columns == first_col[:, :, None]).astype(jnp.float32)
    upper = (columns == second_col[:, :, None]).astype(jnp.float32)
    return (1.0 - weights)[:, :, None] * lower + weights[:, :, None] * upper


def angle_tables(rows, cols, length):
    row_index = lax.iota(jnp.int32, rows)[:, None]
    col_index = lax.iota(jnp.int32, cols)[None, :]
    angles = (row_index * col_index % length).astype(jnp.float32) * (2.0 * math.pi / length)
    return (jnp.cos(angles), jnp.sin(angles))


def unit_root(numerator, length):
    angle = 2.0 * math.pi * numerator / length
    return (round(math.cos(angle), 15), round(math.sin(angle), 15))


def small_stage(real_part, imag_part, axis, direction):
    count = real_part.shape[axis]

    def part(array, index):
        return lax.index_in_dim(array, index, axis, keepdims=False)

    real_in = [part(real_part, index) for index in range(count)]
    imag_in = None if imag_part is None else [part(imag_part, index) for index in range(count)]
    real_out, imag_out = [], []
    for out_index in range(count):
        real_sum, imag_sum = None, None
        for in_index in range(count):
            cosine, sine = unit_root(in_index * out_index, count)
            sine = direction * sine
            terms_real = []
            terms_imag = []
            if cosine != 0.0:
                terms_real.append(cosine * real_in[in_index])
                if imag_in is not None:
                    terms_imag.append(cosine * imag_in[in_index])
            if sine != 0.0:
                terms_imag.append(sine * real_in[in_index])
                if imag_in is not None:
                    terms_real.append(-sine * imag_in[in_index])
            for term in terms_real:
                real_sum = term if real_sum is None else real_sum + term
            for term in terms_imag:
                imag_sum = term if imag_sum is None else imag_sum + term
        if imag_sum is None:
            imag_sum = jnp.zeros_like(real_sum)
        real_out.append(real_sum)
        imag_out.append(imag_sum)
    return (jnp.stack(real_out, axis), jnp.stack(imag_out, axis))


def complex_times(real_part, imag_part, cosine, sine_table):
    return (
        real_part * cosine - imag_part * sine_table,
        real_part * sine_table + imag_part * cosine,
    )


def block_dft_matrix(length, direction):
    cosine, sine = angle_tables(length, length, length)
    sine = direction * sine
    top = jnp.concatenate([cosine, sine], 1)
    bottom = jnp.concatenate([-sine, cosine], 1)
    return jnp.concatenate([top, bottom], 0)


def large_stage(real_part, imag_part, axis, direction):
    length = real_part.shape[axis]
    if imag_part is None:
        imag_part = jnp.zeros_like(real_part)
    joined = jnp.concatenate([real_part, imag_part], axis)
    matrix = block_dft_matrix(length, direction)
    if axis == joined.ndim - 1:
        out = jnp.einsum("...j,jn->...n", joined, matrix, precision=highest)
    else:
        out = jnp.einsum("rkjz,jn->rknz", joined, matrix, precision=highest)
    return (
        lax.slice_in_dim(out, 0, length, axis=axis),
        lax.slice_in_dim(out, length, 2 * length, axis=axis),
    )


def factored(real_part, imag_part, axis, direction, forward, want_imag=True):
    length = real_part.shape[axis]
    second = 128
    first = length // second
    outer = real_part.shape
    shape = outer[:axis] + (first, second) + outer[axis + 1 :]
    real_part = real_part.reshape(shape)
    if imag_part is not None:
        imag_part = imag_part.reshape(shape)
    twist_cos, twist_sin = angle_tables(first, second, length)
    if axis == 1:
        twist_cos = twist_cos[:, :, None]
        twist_sin = twist_sin[:, :, None]
    twist_sin = direction * twist_sin
    if forward:
        real_part, imag_part = small_stage(real_part, imag_part, axis, direction)
        real_part, imag_part = complex_times(real_part, imag_part, twist_cos, twist_sin)
        real_part, imag_part = large_stage(real_part, imag_part, axis + 1, direction)
    else:
        real_part, imag_part = large_stage(real_part, imag_part, axis + 1, direction)
        real_part, imag_part = complex_times(real_part, imag_part, twist_cos, twist_sin)
        real_part, imag_part = small_stage(real_part, imag_part, axis, direction)
    return (real_part.reshape(outer), imag_part.reshape(outer))


def to_columns(real_part, imag_part):
    depth_real, depth_imag = factored(real_part, imag_part, 2, -1.0, True)
    rows = depth_real.shape[0]
    stacked = jnp.concatenate([depth_real, depth_imag], 0)
    moved = lax.all_to_all(stacked, "slab", split_axis=2, concat_axis=1, tiled=True)
    return factored(moved[:rows], moved[rows:], 1, -1.0, True)


def to_planes(real_part, imag_part):
    width_real, width_imag = factored(real_part, imag_part, 1, 1.0, False)
    rows = width_real.shape[0]
    stacked = jnp.concatenate([width_real, width_imag], 0)
    moved = lax.all_to_all(stacked, "slab", split_axis=1, concat_axis=2, tiled=True)
    return factored(moved[:rows], moved[rows:], 2, 1.0, False)


def pack_pairs(volume):
    return (volume[0::2], volume[1::2])


def unpack_pairs(real_part, imag_part):
    pairs, width, depth = real_part.shape
    return jnp.stack([real_part, imag_part], 1).reshape(2 * pairs, width, depth)


def general_shards(estimate, views, psf, pattern_mult, pattern_shift, interp):
    row_count, slab_width, depth = estimate.shape
    blocks = block_matrix(pattern_mult[0], pattern_shift[0], interp[0])
    block_count = depth // 128
    shaped = estimate.reshape(row_count, slab_width, block_count, 128)
    sampled = jnp.einsum("bij,yxbj->yxbi", blocks, shaped, precision=highest).reshape(
        row_count, slab_width, depth
    )
    packed_real, packed_imag = pack_pairs(sampled)
    packed_real = jnp.concatenate([packed_real, psf], 0)
    packed_imag = jnp.concatenate([packed_imag, jnp.zeros_like(psf)], 0)
    spectra_real, spectra_imag = to_columns(packed_real, packed_imag)
    scaling = 1.0 / (spectra_real.shape[1] * depth)
    transfer_real = spectra_real[-1:] * scaling
    transfer_imag = spectra_imag[-1:] * scaling
    spectra_real = spectra_real[:-1]
    spectra_imag = spectra_imag[:-1]
    filtered_real = spectra_real * transfer_real - spectra_imag * transfer_imag
    filtered_imag = spectra_real * transfer_imag + spectra_imag * transfer_real
    blurred = unpack_pairs(*to_planes(filtered_real, filtered_imag))
    quotient = views[0] / blurred
    packed_real, packed_imag = pack_pairs(quotient)
    spectra_real, spectra_imag = to_columns(packed_real, packed_imag)
    filtered_real = spectra_real * transfer_real + spectra_imag * transfer_imag
    filtered_imag = spectra_imag * transfer_real - spectra_real * transfer_imag
    smeared = unpack_pairs(*to_planes(filtered_real, filtered_imag))
    correction = jnp.einsum(
        "bij,yxbi->yxbj",
        blocks,
        smeared.reshape(row_count, slab_width, block_count, 128),
        precision=highest,
    ).reshape(row_count, slab_width, depth)
    log_terms = jnp.log(correction)
    view_count = lax.axis_size("view")
    summed = lax.psum(log_terms, "view")
    return estimate * jnp.exp(summed / view_count)


def swap_halves(joined):
    half = joined.shape[-1] // 2
    return jnp.concatenate([-joined[..., half:], joined[..., :half]], -1)


def butterflies(parts, direction, turn):
    count = len(parts)
    if count == 1:
        return parts
    even = butterflies(parts[0::2], direction, turn)
    odd = butterflies(parts[1::2], direction, turn)
    out = [None] * count
    for index in range(count // 2):
        cosine, sine = unit_root(index, count)
        sine = direction * sine
        value = odd[index]
        if sine == 0.0:
            rotated = value if cosine > 0 else -value
        elif cosine == 0.0:
            rotated = turn(value) if sine > 0 else -turn(value)
        else:
            rotated = cosine * value + sine * turn(value)
        out[index] = even[index] + rotated
        out[index + count // 2] = even[index] - rotated
    return out


def lead_stage(joined, direction):
    count = joined.shape[0]
    parts = [joined[index] for index in range(count)]
    return jnp.stack(butterflies(parts, direction, swap_halves), 0)


def joined_twist(joined, length, direction, lanes):
    first, second = joined.shape[0], (joined.shape[-1] // 2 if lanes else joined.shape[2])
    cosine, sine = angle_tables(first, second, length)
    sine = direction * sine
    if lanes:
        cosine = jnp.concatenate([cosine, cosine], 1)[:, None, None, :]
        sine = jnp.concatenate([sine, sine], 1)[:, None, None, :]
    else:
        cosine = cosine[:, None, :, None]
        sine = sine[:, None, :, None]
    return joined * cosine + swap_halves(joined) * sine


def lane_stage(joined, direction):
    length = joined.shape[-1] // 2
    matrix = block_dft_matrix(length, direction)
    return jnp.einsum("...j,jn->...n", joined, matrix, precision=lax.Precision.HIGH)


def row_stage(joined, direction):
    length = joined.shape[2]
    cosine, sine = angle_tables(length, length, length)
    matrix = jnp.concatenate([cosine, direction * sine], 0)
    both = jnp.concatenate([joined, swap_halves(joined)], 2)
    return jnp.einsum("krjl,jm->krml", both, matrix, precision=lax.Precision.HIGH)


def twist_parts(count, length, size, direction):
    cosine, sine = angle_tables(count, size, length)
    return cosine, direction * sine


def depth_matrices(count, length, direction, twist_first):
    half = length // count
    matrix = block_dft_matrix(half, direction)
    cosine, sine = twist_parts(count, length, half, direction)
    top, bottom = matrix[:half], matrix[half:]
    left, right = matrix[:, :half], matrix[:, half:]
    if twist_first:
        return jnp.concatenate(
            [
                cosine[:, :, None] * top + sine[:, :, None] * bottom,
                -sine[:, :, None] * top + cosine[:, :, None] * bottom,
            ],
            1,
        )
    return jnp.concatenate(
        [
            left * cosine[:, None, :] - right * sine[:, None, :],
            left * sine[:, None, :] + right * cosine[:, None, :],
        ],
        2,
    )


def width_matrices(count, length, direction, twist_first):
    half = length // count
    cosine_table, sine_table = angle_tables(half, half, half)
    sine_table = direction * sine_table
    cosine, sine = twist_parts(count, length, half, direction)
    if twist_first:
        c, s = cosine[:, :, None], sine[:, :, None]
    else:
        c, s = cosine[:, None, :], sine[:, None, :]
    if twist_first:
        return jnp.concatenate(
            [cosine_table * c - sine_table * s, cosine_table * s + sine_table * c], 1
        )
    return jnp.concatenate(
        [cosine_table * c - sine_table * s, sine_table * c + cosine_table * s], 1
    )


def depth_forward(joined, depth):
    joined = lead_stage(joined, -1.0)
    matrices = depth_matrices(joined.shape[0], depth, -1.0, True)
    return jnp.einsum("krxj,kjn->krxn", joined, matrices, precision=lax.Precision.HIGH)


def depth_inverse(joined, depth):
    matrices = depth_matrices(joined.shape[0], depth, 1.0, False)
    joined = jnp.einsum("krxj,kjn->krxn", joined, matrices, precision=lax.Precision.HIGH)
    return lead_stage(joined, 1.0)


def width_forward(joined, width):
    joined = lead_stage(joined, -1.0)
    matrices = width_matrices(joined.shape[0], width, -1.0, True)
    both = jnp.concatenate([joined, swap_halves(joined)], 2)
    return jnp.einsum("krjl,kjm->krml", both, matrices, precision=lax.Precision.HIGH)


def width_inverse(joined, width):
    matrices = width_matrices(joined.shape[0], width, 1.0, False)
    both = jnp.concatenate([joined, swap_halves(joined)], 2)
    joined = jnp.einsum("krjl,kjm->krml", both, matrices, precision=lax.Precision.HIGH)
    return lead_stage(joined, 1.0)


def joined_times(joined, transfer_real, transfer_imag):
    return joined * transfer_real + swap_halves(joined) * transfer_imag


def to_blocks(volume, block_count):
    rows, width, depth = volume.shape
    lanes = depth // block_count
    parity = [volume[0::2], volume[1::2]]
    return jnp.stack(
        [
            jnp.concatenate([part[:, :, block * lanes : (block + 1) * lanes] for part in parity], -1)
            for block in range(block_count)
        ],
        0,
    )


def from_blocks(blocked):
    block_count, pairs, width, lanes = blocked.shape
    half = lanes // 2
    parity = [
        jnp.concatenate([blocked[block, :, :, side * half : (side + 1) * half] for block in range(block_count)], -1)
        for side in range(2)
    ]
    return jnp.stack(parity, 1).reshape(2 * pairs, width, block_count * half)


def shards(estimate, views, psf, pattern_mult, pattern_shift, interp):
    row_count, slab_width, depth = estimate.shape
    slab_count = lax.axis_size("slab")
    block_count = depth // 128
    width = slab_width * slab_count
    if not (
        block_count == slab_count
        and slab_width == 128
        and width // 128 == slab_count
        and row_count % 2 == 0
    ):
        return general_shards(estimate, views, psf, pattern_mult, pattern_shift, interp)
    blocks = block_matrix(pattern_mult[0], pattern_shift[0], interp[0])
    empty = jnp.zeros_like(blocks)
    doubled = jnp.concatenate(
        [jnp.concatenate([blocks, empty], 2), jnp.concatenate([empty, blocks], 2)], 1
    )
    sampled = jnp.einsum(
        "apxl,aml->apxm", to_blocks(estimate, block_count), doubled, precision=lax.Precision.HIGH
    )
    pairs = row_count // 2
    spread = psf.reshape(slab_width, block_count, 128).transpose(1, 0, 2)[:, None]
    spread = jnp.concatenate([spread, jnp.zeros_like(spread)], -1)
    def to_columns_blocked(planes):
        spectra = depth_forward(planes, depth)
        spectra = lax.all_to_all(spectra, "slab", split_axis=0, concat_axis=0, tiled=True)
        return width_forward(spectra, width)

    transfer = to_columns_blocked(spread) * (1.0 / (width * depth))
    spectra = to_columns_blocked(sampled)
    half = transfer.shape[-1] // 2
    transfer_real = jnp.concatenate([transfer[..., :half], transfer[..., :half]], -1)
    transfer_imag = jnp.concatenate([transfer[..., half:], transfer[..., half:]], -1)

    def convolve(spectra, transfer_imag):
        filtered = joined_times(spectra, transfer_real, transfer_imag)
        planes = width_inverse(filtered, width)
        planes = lax.all_to_all(planes, "slab", split_axis=0, concat_axis=0, tiled=True)
        return depth_inverse(planes, depth)

    blurred = convolve(spectra, transfer_imag)
    quotient = to_blocks(views[0], block_count) / blurred
    spectra = depth_forward(quotient, depth)
    spectra = lax.all_to_all(spectra, "slab", split_axis=0, concat_axis=0, tiled=True)
    spectra = width_forward(spectra, width)
    smeared = convolve(spectra, -transfer_imag)
    correction = jnp.einsum("apxm,aml->apxl", smeared, doubled, precision=lax.Precision.HIGH)
    log_terms = from_blocks(jnp.log(correction))
    view_count = lax.axis_size("view")
    summed = lax.psum(log_terms, "view")
    return estimate * jnp.exp(summed / view_count)


def solution(mesh):
    placed = (
        P(None, "slab", None),
        P("view", None, "slab", None),
        P("view", "slab", None),
        P("view", None),
        P("view", None),
        P("view", None, None),
    )
    return jax.shard_map(
        shards, mesh=mesh, in_specs=placed, out_specs=P(None, "slab", None), check_vma=False
    )
```
